128 devices in a mesh: kvh: 4 (over z), blk: 32 (over y, x, core).
Axes of the slice: x: 4, y: 4, z: 4, core: 2. Of those that a mesh axis runs over, the one named last changes fastest.
Arguments:
- queries: bfloat16 [4096, 4096], P('blk', 'kvh')
- suffix_key_rows: bfloat16 [4096, 1024], P('blk', 'kvh')
- suffix_value_rows: bfloat16 [4096, 1024], P('blk', 'kvh'), may hold values from -6 to 6
- prefix_block_keys: bfloat16 [512, 128, 1024], P('blk', None, 'kvh')
- prefix_block_values: bfloat16 [512, 128, 1024], P('blk', None, 'kvh'), may hold values from -6 to 6
- block_group: int32 [512], P('blk'), may hold values from 0 to 15, as said below
- suffix_len: int32 [64], replicated, may hold values from 32 to 96, as said below
- request_group: int32 [64], replicated, may hold values from 0 to 15, as said below
- w_out: bfloat16 [4096, 4096], P('kvh'), may hold values from -1.5 to 1.5
Outputs:
- output: bfloat16 [4096, 4096], P('blk', 'kvh')
The draws below stay inside these ranges and needn't reach their ends.
Inputs may be any that keep to these rules, and one draw needn't show every extreme that they name: `block_group`: every group owns exactly 32 blocks; no index of blk holds more than 1 block of one group, and some holds exactly 1. `request_group`: every group has exactly 4 requests. `suffix_len`: the lengths sum to 4096; both ends of the range are reached; no request begins at a multiple of 128 other than 0.
All inputs are finite; a program needn't handle non-finite values.
Results may differ from the reference program's by a relative error of at most 0.005.
Values may be sent and summed in bfloat16 or wider, within the bound.
No kernel may reach another device: no remote copies, remote signals or barrier semaphores. Data moves between devices by JAX's collectives and lax.ppermute only.
A program may use at most 256 MiB of HBM per device.

```python
import math
import jax
import jax.numpy as jnp
from jax import lax

D = 4096
QUERY_HEADS = 32
KEY_VALUE_HEADS = 8
HEAD_SIZE = 128
ROWS_PER_SHARD = 128
PREFIX_TOKENS = 4096
BLOCK_TOKENS = 128
SUFFIX_ROWS = 4096
REQ = 64
GROUPS = 16
PREFIX_BLOCKS = 512


def build_query_rows(key):
    random_seed_key = jax.random.fold_in(key, 21)
    unscaled_values = jnp.clip(jax.random.normal(random_seed_key, (SUFFIX_ROWS, QUERY_HEADS * HEAD_SIZE), jnp.float32), -6.0, 6.0)
    return unscaled_values


def draw_queries(key, part):
    return build_query_rows(key).astype(jnp.bfloat16)


def draw_suffix_key_rows(key, part):
    query_head_split = build_query_rows(key).reshape(SUFFIX_ROWS, KEY_VALUE_HEADS, QUERY_HEADS // KEY_VALUE_HEADS, HEAD_SIZE)
    random_noise_term = jnp.clip(jax.random.normal(jax.random.fold_in(key, 31), (SUFFIX_ROWS, KEY_VALUE_HEADS, HEAD_SIZE), jnp.float32), -6.0, 6.0)
    correlated_term = 0.5 * jnp.sum(query_head_split, axis=2) + 0.4 * random_noise_term
    return jnp.clip(correlated_term, -8.0, 8.0).reshape(SUFFIX_ROWS, KEY_VALUE_HEADS * HEAD_SIZE).astype(jnp.bfloat16)


def draw_prefix_block_keys(key, part):
    random_seed_key = jax.random.fold_in(key, 41)
    unscaled_values = jnp.clip(jax.random.normal(random_seed_key, (PREFIX_BLOCKS, BLOCK_TOKENS, KEY_VALUE_HEADS * HEAD_SIZE), jnp.float32), -6.0, 6.0)
    return unscaled_values.astype(jnp.bfloat16)


def draw_block_group(key, part):
    per_group = PREFIX_TOKENS // BLOCK_TOKENS
    holders = 2 * GROUPS
    per_holder = PREFIX_BLOCKS // holders
    places = jnp.arange(PREFIX_BLOCKS, dtype=jnp.int32)
    relabel = jax.random.permutation(jax.random.fold_in(key, 51), GROUPS).astype(jnp.int32)
    rotate = jax.random.randint(jax.random.fold_in(key, 52), (), 0, holders).astype(jnp.int32)
    group_of = relabel[places // per_group]
    holder = (places + rotate) % holders
    local_at = places // holders
    holder_keys = jax.random.split(jax.random.fold_in(key, 53), holders)
    shuffles = jax.vmap(lambda one_key: jax.random.permutation(one_key, per_holder))(holder_keys).astype(jnp.int32)
    target = holder * per_holder + shuffles[holder, local_at]
    return jnp.zeros((PREFIX_BLOCKS,), jnp.int32).at[target].set(group_of).astype(jnp.int32)


def draw_suffix_len(key, part):
    shard_rows = ROWS_PER_SHARD
    pair_count = REQ // 2
    lowest = max(1, shard_rows // 8)
    highest = max(lowest, shard_rows // 4)
    after = jax.random.randint(jax.random.fold_in(key, 71), (pair_count,), lowest, highest + 1).astype(jnp.int32)
    after = after.at[0].set(shard_rows // 4).at[pair_count - 1].set(shard_rows // 4).at[1].set(lowest)
    before = jax.random.randint(jax.random.fold_in(key, 72), (pair_count,), lowest, highest + 1).astype(jnp.int32)
    before = before.at[0].set(0).at[2].set(lowest)
    before_next = jnp.concatenate([before[1:], jnp.zeros((1,), jnp.int32)])
    even_len = before + after
    odd_len = shard_rows - before_next - after
    return jnp.stack([even_len, odd_len], axis=1).reshape(REQ).astype(jnp.int32)


def draw_request_group(key, part):
    return (jax.random.permutation(jax.random.fold_in(key, 61), REQ) // 4).astype(jnp.int32)


def shard_levels(stream_key, dims, shards, low, largest):
    def one(position, parts):
        draws = jax.random.uniform(jax.random.fold_in(jax.random.fold_in(stream_key, 6), position), (parts,), jnp.float32, low / len(shards), largest / len(shards))
        return jnp.repeat(jnp.exp(draws), dims[position] // parts).reshape((-1,) + (1,) * (len(dims) - position - 1))

    level = one(*shards[0])
    for cut in shards[1:]:
        level = level * one(*cut)
    return level


def normal_values(stream_key, dims, width, reach, shards=(), held_as=jnp.bfloat16):
    entries = width * jax.random.normal(stream_key, dims, jnp.float32)
    if shards:
        entries = entries * shard_levels(stream_key, dims, shards, -0.22, 0.18)
    return jnp.clip(entries, -reach, reach).astype(held_as)


def setup_inputs(seed: int = 0) -> dict:
    key_of = jax.random.split(jax.random.key(seed), 10)
    return {
        "queries": draw_queries(jax.random.fold_in(key_of[9], 71), 0),
        "suffix_key_rows": draw_suffix_key_rows(jax.random.fold_in(key_of[9], 71), 0),
        "suffix_value_rows": normal_values(key_of[2], (SUFFIX_ROWS, KEY_VALUE_HEADS * HEAD_SIZE), 1.0, 6.0, ((0, 32), (1, 4))),
        "prefix_block_keys": draw_prefix_block_keys(jax.random.fold_in(key_of[9], 71), 0),
        "prefix_block_values": normal_values(key_of[4], (PREFIX_BLOCKS, BLOCK_TOKENS, KEY_VALUE_HEADS * HEAD_SIZE), 1.0, 6.0, ((0, 32), (2, 4))),
        "block_group": draw_block_group(jax.random.fold_in(key_of[9], 71), 0),
        "suffix_len": draw_suffix_len(jax.random.fold_in(key_of[9], 71), 0),
        "request_group": draw_request_group(jax.random.fold_in(key_of[9], 71), 0),
        "w_out": normal_values(key_of[8], (QUERY_HEADS * HEAD_SIZE, D), (QUERY_HEADS * HEAD_SIZE // 256) ** -0.5, 1.5, ((0, 4),)),
    }


def slot_table(suffix_len, request_group, tok_dev, row_count):
    req_count = suffix_len.shape[0]
    group_count = req_count // 4
    row_ends = jnp.cumsum(suffix_len).astype(jnp.int32)
    starts = (row_ends - suffix_len).astype(jnp.int32)
    member = (request_group[None, :] == jnp.arange(group_count, dtype=jnp.int32)[:, None]).astype(jnp.int32)
    rank_of = (jnp.cumsum(member, axis=1) - 1).astype(jnp.int32)
    slot_ids = jnp.arange(4 * tok_dev, dtype=jnp.int32)
    which_req = slot_ids // tok_dev
    offset = slot_ids % tok_dev
    picked = member[:, None, :] * (rank_of[:, None, :] == which_req[None, :, None]).astype(jnp.int32)
    length = lax.optimization_barrier(jnp.sum(picked * suffix_len[None, None, :], axis=2)).astype(jnp.int32)
    row_begin = lax.optimization_barrier(jnp.sum(picked * starts[None, None, :], axis=2)).astype(jnp.int32)
    slot_valid = offset[None, :] < length
    return (jnp.where(slot_valid, row_begin + offset[None, :], row_count).astype(jnp.int32), slot_valid)

def reference(queries, suffix_key_rows, suffix_value_rows, prefix_block_keys, prefix_block_values, block_group, suffix_len, request_group, w_out):
    row_count = queries.shape[0]
    group_count = suffix_len.shape[0] // 4
    per_group = PREFIX_TOKENS // BLOCK_TOKENS
    query_group_width = QUERY_HEADS // KEY_VALUE_HEADS
    score_scale = 1.0 / math.sqrt(HEAD_SIZE)
    slot_rows, slot_valid = slot_table(suffix_len, request_group, ROWS_PER_SHARD, row_count)
    block_order = jnp.argsort(block_group, stable=True).astype(jnp.int32).reshape(group_count, per_group)
    padded_query_rows = jnp.concatenate([queries, jnp.zeros((1, QUERY_HEADS * HEAD_SIZE), jnp.bfloat16)], axis=0)
    padded_key_rows = jnp.concatenate([suffix_key_rows, jnp.zeros((1, KEY_VALUE_HEADS * HEAD_SIZE), jnp.bfloat16)], axis=0)
    padded_value_rows = jnp.concatenate([suffix_value_rows, jnp.zeros((1, KEY_VALUE_HEADS * HEAD_SIZE), jnp.bfloat16)], axis=0)
    item_rows = slot_rows.reshape(group_count * 4, ROWS_PER_SHARD)
    item_valid = slot_valid.reshape(group_count * 4, ROWS_PER_SHARD)
    item_group = (jnp.arange(group_count * 4, dtype=jnp.int32) // 4).astype(jnp.int32)
    offsets = jnp.arange(ROWS_PER_SHARD, dtype=jnp.int32)
    causal = offsets[None, :] <= offsets[:, None]

    def one_item(packed):
        local_row_count, valid_here, group_here = packed
        local_block_count = block_order[group_here]
        query_float_rows = padded_query_rows[local_row_count].astype(jnp.float32).reshape(ROWS_PER_SHARD, KEY_VALUE_HEADS, query_group_width, HEAD_SIZE)
        prefix_key_rows = prefix_block_keys[local_block_count].astype(jnp.float32).reshape(PREFIX_TOKENS, KEY_VALUE_HEADS, HEAD_SIZE)
        prefix_value_rows = prefix_block_values[local_block_count].astype(jnp.float32).reshape(PREFIX_TOKENS, KEY_VALUE_HEADS, HEAD_SIZE)
        request_key_rows = padded_key_rows[local_row_count].astype(jnp.float32).reshape(ROWS_PER_SHARD, KEY_VALUE_HEADS, HEAD_SIZE)
        request_value_rows = padded_value_rows[local_row_count].astype(jnp.float32).reshape(ROWS_PER_SHARD, KEY_VALUE_HEADS, HEAD_SIZE)
        far_s = jnp.einsum('sgjd,tgd->sgjt', query_float_rows, prefix_key_rows) * score_scale
        near_s = jnp.einsum('sgjd,tgd->sgjt', query_float_rows, request_key_rows) * score_scale
        allowed = causal & valid_here[None, :]
        near_s = jnp.where(allowed[:, None, None, :], near_s, -jnp.inf)
        row_top = jnp.maximum(lax.optimization_barrier(jnp.max(far_s, axis=3)), lax.optimization_barrier(jnp.max(near_s, axis=3)))[..., None]
        far_p = jnp.exp(far_s - row_top)
        near_p = jnp.exp(near_s - row_top)
        denominator = lax.optimization_barrier(jnp.sum(far_p, axis=3)) + lax.optimization_barrier(jnp.sum(near_p, axis=3))
        far_w = lax.optimization_barrier(far_p.astype(jnp.bfloat16)).astype(jnp.float32)
        near_w = lax.optimization_barrier(near_p.astype(jnp.bfloat16)).astype(jnp.float32)
        context = jnp.einsum('sgjt,tgd->sgjd', far_w, prefix_value_rows) + jnp.einsum('sgjt,tgd->sgjd', near_w, request_value_rows)
        return (context / denominator[..., None]).astype(jnp.bfloat16).reshape(ROWS_PER_SHARD, QUERY_HEADS * HEAD_SIZE)
    results = lax.map(one_item, (item_rows, item_valid, item_group))
    attention = jnp.zeros((row_count + 1, QUERY_HEADS * HEAD_SIZE), jnp.bfloat16).at[slot_rows.reshape(-1)].set(results.reshape(-1, QUERY_HEADS * HEAD_SIZE))[:row_count]
    return jnp.dot(attention, w_out, preferred_element_type=jnp.float32).astype(jnp.bfloat16)
```

```python
import functools
import math

import jax
import jax.numpy as jnp
from jax import lax
from jax.experimental import pallas as pl
from jax.experimental.pallas import tpu as pltpu
from jax.sharding import PartitionSpec as P

HEAD_SIZE = 128
SLOTS = 5
STAT_LANES = 128


def from_behind(block, axis, distance):
    devices = range(lax.axis_size(axis))
    route = [(i - distance, i) for i in devices if i - distance in devices]
    return lax.ppermute(block, axis, route)


def request_of(row_ids, starts, row_ends):
    inside = (row_ids[:, None] >= starts[None, :]) & (row_ids[:, None] < row_ends[None, :])
    req_ids = jnp.arange(starts.shape[0], dtype=jnp.int32)
    return jnp.sum(jnp.where(inside, req_ids[None, :], 0), axis=1)


def tile_tables(suffix_len, request_group, block_group, n_tiles, tile):
    row_ends = jnp.cumsum(suffix_len).astype(jnp.int32)
    starts = row_ends - suffix_len
    tile_lo = jnp.arange(n_tiles, dtype=jnp.int32) * tile
    first = jnp.sum((row_ends[None, :] <= tile_lo[:, None]).astype(jnp.int32), axis=1)
    last = jnp.sum((row_ends[None, :] <= (tile_lo + tile - 1)[:, None]).astype(jnp.int32), axis=1)
    req = first[:, None] + jnp.arange(SLOTS, dtype=jnp.int32)[None, :]
    valid = req <= last[:, None]
    req_v = jnp.minimum(req, last[:, None])
    lo = jnp.where(valid, starts[req_v], 0).astype(jnp.int32)
    hi = jnp.where(valid, row_ends[req_v], 0).astype(jnp.int32)
    group_count = suffix_len.shape[0] // 4
    blocks = block_group.shape[0]
    owns = block_group[None, :] == jnp.arange(group_count, dtype=jnp.int32)[:, None]
    block_of_group = jnp.sum(
        jnp.where(owns, jnp.arange(blocks, dtype=jnp.int32)[None, :], 0), axis=1
    ).astype(jnp.int32)
    blk = block_of_group[request_group[req_v]].astype(jnp.int32)
    return lo.reshape(-1), hi.reshape(-1), blk.reshape(-1)


def _scores(q_ref, k_ref, j, h, query_group_width, scale):
    kv = h // query_group_width
    q = q_ref[:, h * HEAD_SIZE : (h + 1) * HEAD_SIZE]
    k = k_ref[j, :, kv * HEAD_SIZE : (kv + 1) * HEAD_SIZE]
    s = lax.dot_general(q, k, (((1,), (1,)), ((), ())), preferred_element_type=jnp.float32)
    return s * scale


def max_kernel(lo_ref, hi_ref, blk_ref, q_ref, k_ref, m_ref, *, heads, qgw, scale):
    i = pl.program_id(0)
    tile = q_ref.shape[0]
    rows = i * tile + lax.broadcasted_iota(jnp.int32, (tile, 1), 0)
    m_ref[...] = jnp.full(m_ref.shape, -jnp.inf, jnp.float32)
    for s in range(SLOTS):
        a = lo_ref[i * SLOTS + s]
        b = hi_ref[i * SLOTS + s]
        j = blk_ref[i * SLOTS + s]

        @pl.when(a < b)
        def _():
            mask = (rows >= a) & (rows < b)
            for h in range(heads):
                sc = _scores(q_ref, k_ref, j, h, qgw, scale)
                mx = jnp.max(sc, axis=1, keepdims=True)
                m_ref[:, h : h + 1] = jnp.where(mask, mx, m_ref[:, h : h + 1])


def ctx_kernel(lo_ref, hi_ref, blk_ref, q_ref, k_ref, v_ref, m_ref, o_ref, *, heads, qgw, scale):
    i = pl.program_id(0)
    tile = q_ref.shape[0]
    rows = i * tile + lax.broadcasted_iota(jnp.int32, (tile, 1), 0)
    o_ref[...] = jnp.zeros(o_ref.shape, jnp.float32)
    for s in range(SLOTS):
        a = lo_ref[i * SLOTS + s]
        b = hi_ref[i * SLOTS + s]
        j = blk_ref[i * SLOTS + s]

        @pl.when(a < b)
        def _():
            mask = (rows >= a) & (rows < b)
            for h in range(heads):
                kv = h // qgw
                sc = _scores(q_ref, k_ref, j, h, qgw, scale)
                p = jnp.where(mask, jnp.exp(sc - m_ref[:, h : h + 1]), 0.0)
                v = v_ref[j, :, kv * HEAD_SIZE : (kv + 1) * HEAD_SIZE]
                ctx = jnp.dot(p.astype(jnp.bfloat16), v, preferred_element_type=jnp.float32)
                cols = slice(h * HEAD_SIZE, (h + 1) * HEAD_SIZE)
                o_ref[:, cols] = o_ref[:, cols] + ctx
                tcol = slice(heads * HEAD_SIZE + h, heads * HEAD_SIZE + h + 1)
                o_ref[:, tcol] = o_ref[:, tcol] + jnp.sum(p, axis=1, keepdims=True)


def per_device(
    queries,
    suffix_key_rows,
    suffix_value_rows,
    prefix_block_keys,
    prefix_block_values,
    block_group,
    suffix_len,
    request_group,
    w_out,
):
    tok_dev = queries.shape[0]
    q_cols = queries.shape[1]
    kv_cols = suffix_key_rows.shape[1]
    local_kv = kv_cols // HEAD_SIZE
    local_heads = q_cols // HEAD_SIZE
    qgw = local_heads // local_kv
    blocks, block_len, _ = prefix_block_keys.shape
    blk_count = lax.axis_size("blk")
    row_count = blk_count * tok_dev
    blk_index = lax.axis_index("blk")
    scale = 1.0 / math.sqrt(HEAD_SIZE)
    tile = tok_dev
    n_tiles = row_count // tile

    gathered = lax.all_gather(queries, "blk", axis=0, tiled=True)
    lo, hi, blk = tile_tables(suffix_len, request_group, block_group, n_tiles, tile)

    q_spec = pl.BlockSpec((tile, q_cols), lambda i, *_: (i, 0))
    kv_spec = pl.BlockSpec((blocks, block_len, kv_cols), lambda i, *_: (0, 0, 0))
    m_spec = pl.BlockSpec((tile, local_heads), lambda i, *_: (i, 0))
    kw = dict(heads=local_heads, qgw=qgw, scale=scale)

    local_max = pl.pallas_call(
        functools.partial(max_kernel, **kw),
        out_shape=jax.ShapeDtypeStruct((row_count, local_heads), jnp.float32),
        grid_spec=pltpu.PrefetchScalarGridSpec(
            num_scalar_prefetch=3,
            grid=(n_tiles,),
            in_specs=[q_spec, kv_spec],
            out_specs=m_spec,
        ),
    )(lo, hi, blk, gathered, prefix_block_keys)
    far_max = lax.pmax(local_max, "blk")

    width = q_cols + STAT_LANES
    partial = pl.pallas_call(
        functools.partial(ctx_kernel, **kw),
        out_shape=jax.ShapeDtypeStruct((row_count, width), jnp.float32),
        grid_spec=pltpu.PrefetchScalarGridSpec(
            num_scalar_prefetch=3,
            grid=(n_tiles,),
            in_specs=[q_spec, kv_spec, kv_spec, m_spec],
            out_specs=pl.BlockSpec((tile, width), lambda i, *_: (i, 0)),
        ),
    )(lo, hi, blk, gathered, prefix_block_keys, prefix_block_values, far_max)
    got = lax.psum_scatter(partial, "blk", scatter_dimension=0, tiled=True)
    far_context = got[:, :q_cols].reshape(tok_dev, local_kv, qgw, HEAD_SIZE)
    far_total = got[:, q_cols : q_cols + local_heads].reshape(tok_dev, local_kv, qgw)
    own_far_max = lax.dynamic_slice_in_dim(far_max, blk_index * tok_dev, tok_dev, 0).reshape(
        tok_dev, local_kv, qgw
    )

    row_ends = jnp.cumsum(suffix_len)
    starts = row_ends - suffix_len
    own_rows = blk_index * tok_dev + jnp.arange(tok_dev, dtype=jnp.int32)
    earlier_keys, earlier_values = from_behind((suffix_key_rows, suffix_value_rows), "blk", 1)
    near_keys = jnp.concatenate([earlier_keys, suffix_key_rows], axis=0).reshape(
        2 * tok_dev, local_kv, HEAD_SIZE
    )
    near_values = jnp.concatenate([earlier_values, suffix_value_rows], axis=0).reshape(
        2 * tok_dev, local_kv, HEAD_SIZE
    )
    near_rows = (blk_index - 1) * tok_dev + jnp.arange(2 * tok_dev, dtype=jnp.int32)
    own_req = request_of(own_rows, starts, row_ends)
    near_req = request_of(near_rows, starts, row_ends)
    allowed = (
        (own_req[:, None] == near_req[None, :])
        & (near_rows[None, :] <= own_rows[:, None])
        & (near_rows[None, :] >= 0)
    )
    own_queries = queries.reshape(tok_dev, local_kv, qgw, HEAD_SIZE)
    near_scores = (
        jnp.einsum("sgjd,tgd->sgjt", own_queries, near_keys, preferred_element_type=jnp.float32)
        * scale
    )
    near_scores = jnp.where(allowed[:, None, None, :], near_scores, -jnp.inf)
    near_max = jnp.max(near_scores, axis=3)
    top = jnp.maximum(own_far_max, near_max)
    near_prob = jnp.exp(near_scores - top[..., None])
    near_total = jnp.sum(near_prob, axis=3)
    near_context = jnp.einsum(
        "sgjt,tgd->sgjd",
        near_prob.astype(jnp.bfloat16),
        near_values,
        preferred_element_type=jnp.float32,
    )
    far_scale = jnp.exp(own_far_max - top)
    context = far_context * far_scale[..., None] + near_context
    denominator = far_total * far_scale + near_total
    attention = (context / denominator[..., None]).reshape(tok_dev, q_cols).astype(jnp.bfloat16)
    projected = jnp.dot(attention, w_out, preferred_element_type=jnp.float32)
    return lax.psum_scatter(projected, "kvh", scatter_dimension=1, tiled=True).astype(jnp.bfloat16)


def solution(mesh):
    placed = (
        P("blk", "kvh"),
        P("blk", "kvh"),
        P("blk", "kvh"),
        P("blk", None, "kvh"),
        P("blk", None, "kvh"),
        P("blk"),
        P(),
        P(),
        P("kvh", None),
    )
    return jax.shard_map(
        per_device, mesh=mesh, in_specs=placed, out_specs=P("blk", "kvh"), check_vma=False
    )
```

```python
import functools
import math

import jax
import jax.numpy as jnp
from jax import lax
from jax.experimental import pallas as pl
from jax.experimental.pallas import tpu as pltpu
from jax.sharding import PartitionSpec as P

HEAD_SIZE = 128
SLOTS = 5
STAT_LANES = 128


def from_behind(block, axis, distance):
    devices = range(lax.axis_size(axis))
    route = [(i - distance, i) for i in devices if i - distance in devices]
    return lax.ppermute(block, axis, route)


def request_of(row_ids, starts, row_ends):
    inside = (row_ids[:, None] >= starts[None, :]) & (row_ids[:, None] < row_ends[None, :])
    req_ids = jnp.arange(starts.shape[0], dtype=jnp.int32)
    return jnp.sum(jnp.where(inside, req_ids[None, :], 0), axis=1)


def tile_tables(suffix_len, request_group, block_group, n_tiles, tile):
    row_ends = jnp.cumsum(suffix_len).astype(jnp.int32)
    starts = row_ends - suffix_len
    tile_lo = jnp.arange(n_tiles, dtype=jnp.int32) * tile
    first = jnp.sum((row_ends[None, :] <= tile_lo[:, None]).astype(jnp.int32), axis=1)
    last = jnp.sum((row_ends[None, :] <= (tile_lo + tile - 1)[:, None]).astype(jnp.int32), axis=1)
    req = first[:, None] + jnp.arange(SLOTS, dtype=jnp.int32)[None, :]
    valid = req <= last[:, None]
    req_v = jnp.minimum(req, last[:, None])
    lo = jnp.where(valid, starts[req_v], 0).astype(jnp.int32)
    hi = jnp.where(valid, row_ends[req_v], 0).astype(jnp.int32)
    group_count = suffix_len.shape[0] // 4
    blocks = block_group.shape[0]
    owns = block_group[None, :] == jnp.arange(group_count, dtype=jnp.int32)[:, None]
    block_of_group = jnp.sum(
        jnp.where(owns, jnp.arange(blocks, dtype=jnp.int32)[None, :], 0), axis=1
    ).astype(jnp.int32)
    blk = block_of_group[request_group[req_v]].astype(jnp.int32)
    return lo.reshape(-1), hi.reshape(-1), blk.reshape(-1)


def _slot_mask(lo_ref, hi_ref, base, rows):
    seg = lax.broadcasted_iota(jnp.int32, (1, SLOTS * HEAD_SIZE), 1) // HEAD_SIZE
    lo = jnp.zeros(seg.shape, jnp.int32)
    hi = jnp.zeros(seg.shape, jnp.int32)
    for s in range(SLOTS):
        lo = jnp.where(seg == s, lo_ref[base + s], lo)
        hi = jnp.where(seg == s, hi_ref[base + s], hi)
    return (rows >= lo) & (rows < hi)


def _slot_keys(kt_ref, blk_ref, base, kv):
    cols = slice(kv * HEAD_SIZE, (kv + 1) * HEAD_SIZE)
    return jnp.concatenate([kt_ref[blk_ref[base + s], cols, :] for s in range(SLOTS)], axis=1)


def _slot_values(v_ref, blk_ref, base, kv):
    cols = slice(kv * HEAD_SIZE, (kv + 1) * HEAD_SIZE)
    return jnp.concatenate([v_ref[blk_ref[base + s], :, cols] for s in range(SLOTS)], axis=0)


def max_kernel(lo_ref, hi_ref, blk_ref, q_ref, kt_ref, m_ref, *, heads, qgw, scale):
    i = pl.program_id(0)
    tile = q_ref.shape[0]
    base = i * SLOTS
    rows = i * tile + lax.broadcasted_iota(jnp.int32, (tile, 1), 0)
    mask = _slot_mask(lo_ref, hi_ref, base, rows)
    lane = lax.broadcasted_iota(jnp.int32, (1, STAT_LANES), 1)
    stats = jnp.full((tile, STAT_LANES), -jnp.inf, jnp.float32)
    for kv in range(heads // qgw):
        keys = _slot_keys(kt_ref, blk_ref, base, kv)
        for j in range(qgw):
            h = kv * qgw + j
            q = q_ref[:, h * HEAD_SIZE : (h + 1) * HEAD_SIZE]
            sc = jnp.dot(q, keys, preferred_element_type=jnp.float32) * scale
            mx = jnp.max(jnp.where(mask, sc, -jnp.inf), axis=1, keepdims=True)
            stats = jnp.where(lane == h, mx, stats)
    m_ref[...] = stats[:, :heads]


def ctx_kernel(lo_ref, hi_ref, blk_ref, q_ref, kt_ref, v_ref, m_ref, o_ref, *, heads, qgw, scale):
    i = pl.program_id(0)
    tile = q_ref.shape[0]
    base = i * SLOTS
    rows = i * tile + lax.broadcasted_iota(jnp.int32, (tile, 1), 0)
    mask = _slot_mask(lo_ref, hi_ref, base, rows)
    lane = lax.broadcasted_iota(jnp.int32, (1, STAT_LANES), 1)
    totals = jnp.zeros((tile, STAT_LANES), jnp.float32)
    top = m_ref[...]
    for kv in range(heads // qgw):
        keys = _slot_keys(kt_ref, blk_ref, base, kv)
        values = _slot_values(v_ref, blk_ref, base, kv)
        for j in range(qgw):
            h = kv * qgw + j
            q = q_ref[:, h * HEAD_SIZE : (h + 1) * HEAD_SIZE]
            sc = jnp.dot(q, keys, preferred_element_type=jnp.float32) * scale
            p = jnp.exp(jnp.where(mask, sc - top[:, h : h + 1], -jnp.inf))
            ctx = jnp.dot(p.astype(jnp.bfloat16), values, preferred_element_type=jnp.float32)
            o_ref[:, h * HEAD_SIZE : (h + 1) * HEAD_SIZE] = ctx
            totals = jnp.where(lane == h, jnp.sum(p, axis=1, keepdims=True), totals)
    o_ref[:, heads * HEAD_SIZE :] = totals


def butterfly_max(x, axis):
    n = lax.axis_size(axis)
    d = 1
    while d < n:
        x = jnp.maximum(x, lax.ppermute(x, axis, [(i, i ^ d) for i in range(n)]))
        d *= 2
    return x


def per_device(
    queries,
    suffix_key_rows,
    suffix_value_rows,
    prefix_block_keys,
    prefix_block_values,
    block_group,
    suffix_len,
    request_group,
    w_out,
):
    tok_dev = queries.shape[0]
    q_cols = queries.shape[1]
    kv_cols = suffix_key_rows.shape[1]
    local_kv = kv_cols // HEAD_SIZE
    local_heads = q_cols // HEAD_SIZE
    qgw = local_heads // local_kv
    blocks, block_len, _ = prefix_block_keys.shape
    blk_count = lax.axis_size("blk")
    row_count = blk_count * tok_dev
    blk_index = lax.axis_index("blk")
    scale = 1.0 / math.sqrt(HEAD_SIZE)
    tile = tok_dev
    n_tiles = row_count // tile

    gathered = lax.all_gather(queries, "blk", axis=0, tiled=True)
    lo, hi, blk = tile_tables(suffix_len, request_group, block_group, n_tiles, tile)

    q_spec = pl.BlockSpec((tile, q_cols), lambda i, *_: (i, 0))
    kv_spec = pl.BlockSpec((blocks, block_len, kv_cols), lambda i, *_: (0, 0, 0))
    kt_spec = pl.BlockSpec((blocks, kv_cols, block_len), lambda i, *_: (0, 0, 0))
    keys_t = jnp.swapaxes(prefix_block_keys, 1, 2)
    m_spec = pl.BlockSpec((tile, local_heads), lambda i, *_: (i, 0))
    kw = dict(heads=local_heads, qgw=qgw, scale=scale)

    local_max = pl.pallas_call(
        functools.partial(max_kernel, **kw),
        out_shape=jax.ShapeDtypeStruct((row_count, local_heads), jnp.float32),
        grid_spec=pltpu.PrefetchScalarGridSpec(
            num_scalar_prefetch=3,
            grid=(n_tiles,),
            in_specs=[q_spec, kt_spec],
            out_specs=m_spec,
        ),
    )(lo, hi, blk, gathered, keys_t)
    far_max = butterfly_max(local_max, "blk")

    width = q_cols + STAT_LANES
    partial = pl.pallas_call(
        functools.partial(ctx_kernel, **kw),
        out_shape=jax.ShapeDtypeStruct((row_count, width), jnp.float32),
        grid_spec=pltpu.PrefetchScalarGridSpec(
            num_scalar_prefetch=3,
            grid=(n_tiles,),
            in_specs=[q_spec, kt_spec, kv_spec, m_spec],
            out_specs=pl.BlockSpec((tile, width), lambda i, *_: (i, 0)),
        ),
    )(lo, hi, blk, gathered, keys_t, prefix_block_values, far_max)
    got = lax.psum_scatter(partial, "blk", scatter_dimension=0, tiled=True)
    far_context = got[:, :q_cols].reshape(tok_dev, local_kv, qgw, HEAD_SIZE)
    far_total = got[:, q_cols : q_cols + local_heads].reshape(tok_dev, local_kv, qgw)
    own_far_max = lax.dynamic_slice_in_dim(far_max, blk_index * tok_dev, tok_dev, 0).reshape(
        tok_dev, local_kv, qgw
    )

    row_ends = jnp.cumsum(suffix_len)
    starts = row_ends - suffix_len
    own_rows = blk_index * tok_dev + jnp.arange(tok_dev, dtype=jnp.int32)
    earlier_keys, earlier_values = from_behind((suffix_key_rows, suffix_value_rows), "blk", 1)
    near_keys = jnp.concatenate([earlier_keys, suffix_key_rows], axis=0).reshape(
        2 * tok_dev, local_kv, HEAD_SIZE
    )
    near_values = jnp.concatenate([earlier_values, suffix_value_rows], axis=0).reshape(
        2 * tok_dev, local_kv, HEAD_SIZE
    )
    near_rows = (blk_index - 1) * tok_dev + jnp.arange(2 * tok_dev, dtype=jnp.int32)
    own_req = request_of(own_rows, starts, row_ends)
    near_req = request_of(near_rows, starts, row_ends)
    allowed = (
        (own_req[:, None] == near_req[None, :])
        & (near_rows[None, :] <= own_rows[:, None])
        & (near_rows[None, :] >= 0)
    )
    own_queries = queries.reshape(tok_dev, local_kv, qgw, HEAD_SIZE)
    near_scores = (
        jnp.einsum("sgjd,tgd->sgjt", own_queries, near_keys, preferred_element_type=jnp.float32)
        * scale
    )
    near_scores = jnp.where(allowed[:, None, None, :], near_scores, -jnp.inf)
    near_max = jnp.max(near_scores, axis=3)
    top = jnp.maximum(own_far_max, near_max)
    near_prob = jnp.exp(near_scores - top[..., None])
    near_total = jnp.sum(near_prob, axis=3)
    near_context = jnp.einsum(
        "sgjt,tgd->sgjd",
        near_prob.astype(jnp.bfloat16),
        near_values,
        preferred_element_type=jnp.float32,
    )
    far_scale = jnp.exp(own_far_max - top)
    context = far_context * far_scale[..., None] + near_context
    denominator = far_total * far_scale + near_total
    attention = (context / denominator[..., None]).reshape(tok_dev, q_cols).astype(jnp.bfloat16)
    projected = jnp.dot(attention, w_out, preferred_element_type=jnp.float32)
    return lax.psum_scatter(projected, "kvh", scatter_dimension=1, tiled=True).astype(jnp.bfloat16)


def solution(mesh):
    placed = (
        P("blk", "kvh"),
        P("blk", "kvh"),
        P("blk", "kvh"),
        P("blk", None, "kvh"),
        P("blk", None, "kvh"),
        P("blk"),
        P(),
        P(),
        P("kvh", None),
    )
    return jax.shard_map(
        per_device, mesh=mesh, in_specs=placed, out_specs=P("blk", "kvh"), check_vma=False
    )
```

```python
import functools
import math

import jax
import jax.numpy as jnp
from jax import lax
from jax.experimental import pallas as pl
from jax.experimental.pallas import tpu as pltpu
from jax.sharding import PartitionSpec as P

HEAD_SIZE = 128
SLOTS = 5
STAT_LANES = 128


def from_behind(block, axis, distance):
    devices = range(lax.axis_size(axis))
    route = [(i - distance, i) for i in devices if i - distance in devices]
    return lax.ppermute(block, axis, route)


def request_of(row_ids, starts, row_ends):
    inside = (row_ids[:, None] >= starts[None, :]) & (row_ids[:, None] < row_ends[None, :])
    req_ids = jnp.arange(starts.shape[0], dtype=jnp.int32)
    return jnp.sum(jnp.where(inside, req_ids[None, :], 0), axis=1)


def tile_tables(suffix_len, request_group, block_group, n_tiles, tile):
    row_ends = jnp.cumsum(suffix_len).astype(jnp.int32)
    starts = row_ends - suffix_len
    tile_lo = jnp.arange(n_tiles, dtype=jnp.int32) * tile
    first = jnp.sum((row_ends[None, :] <= tile_lo[:, None]).astype(jnp.int32), axis=1)
    last = jnp.sum((row_ends[None, :] <= (tile_lo + tile - 1)[:, None]).astype(jnp.int32), axis=1)
    req = first[:, None] + jnp.arange(SLOTS, dtype=jnp.int32)[None, :]
    valid = req <= last[:, None]
    req_v = jnp.minimum(req, last[:, None])
    lo = jnp.where(valid, starts[req_v], 0).astype(jnp.int32)
    hi = jnp.where(valid, row_ends[req_v], 0).astype(jnp.int32)
    group_count = suffix_len.shape[0] // 4
    blocks = block_group.shape[0]
    owns = block_group[None, :] == jnp.arange(group_count, dtype=jnp.int32)[:, None]
    block_of_group = jnp.sum(
        jnp.where(owns, jnp.arange(blocks, dtype=jnp.int32)[None, :], 0), axis=1
    ).astype(jnp.int32)
    blk = block_of_group[request_group[req_v]].astype(jnp.int32)
    return lo.reshape(-1), hi.reshape(-1), blk.reshape(-1)


def _slot_mask(lo_ref, hi_ref, base, rows):
    seg = lax.broadcasted_iota(jnp.int32, (1, SLOTS * HEAD_SIZE), 1) // HEAD_SIZE
    lo = jnp.zeros(seg.shape, jnp.int32)
    hi = jnp.zeros(seg.shape, jnp.int32)
    for s in range(SLOTS):
        lo = jnp.where(seg == s, lo_ref[base + s], lo)
        hi = jnp.where(seg == s, hi_ref[base + s], hi)
    return (rows >= lo) & (rows < hi)


def _slot_keys(kt_ref, blk_ref, base):
    return jnp.concatenate([kt_ref[blk_ref[base + s]] for s in range(SLOTS)], axis=1)


def _slot_values(v_ref, blk_ref, base):
    return jnp.concatenate([v_ref[blk_ref[base + s]] for s in range(SLOTS)], axis=0)


def max_kernel(lo_ref, hi_ref, blk_ref, q_ref, kt_ref, m_ref, *, heads, scale):
    i = pl.program_id(0)
    tile = q_ref.shape[0]
    base = i * SLOTS
    rows = i * tile + lax.broadcasted_iota(jnp.int32, (tile, 1), 0)
    mask = _slot_mask(lo_ref, hi_ref, base, rows)
    lane = lax.broadcasted_iota(jnp.int32, (1, STAT_LANES), 1)
    stats = jnp.full((tile, STAT_LANES), -jnp.inf, jnp.float32)
    keys = _slot_keys(kt_ref, blk_ref, base)
    for h in range(heads):
        q = q_ref[:, h * HEAD_SIZE : (h + 1) * HEAD_SIZE]
        sc = jnp.dot(q, keys, preferred_element_type=jnp.float32) * scale
        mx = jnp.max(jnp.where(mask, sc, -jnp.inf), axis=1, keepdims=True)
        stats = jnp.where(lane == h, mx, stats)
    m_ref[...] = jnp.transpose(stats)[: m_ref.shape[0], :]


def ctx_kernel(lo_ref, hi_ref, blk_ref, q_ref, kt_ref, v_ref, m_ref, o_ref, t_ref, *, heads, scale):
    i = pl.program_id(0)
    tile = q_ref.shape[0]
    base = i * SLOTS
    rows = i * tile + lax.broadcasted_iota(jnp.int32, (tile, 1), 0)
    mask = _slot_mask(lo_ref, hi_ref, base, rows)
    lane = lax.broadcasted_iota(jnp.int32, (1, STAT_LANES), 1)
    totals = jnp.zeros((tile, STAT_LANES), jnp.float32)
    top = jnp.transpose(m_ref[...])
    keys = _slot_keys(kt_ref, blk_ref, base)
    values = _slot_values(v_ref, blk_ref, base)
    for h in range(heads):
        q = q_ref[:, h * HEAD_SIZE : (h + 1) * HEAD_SIZE]
        sc = jnp.dot(q, keys, preferred_element_type=jnp.float32) * scale
        p = jnp.exp(jnp.where(mask, sc - top[:, h : h + 1], -jnp.inf))
        ctx = jnp.dot(p.astype(jnp.bfloat16), values, preferred_element_type=jnp.float32)
        o_ref[:, h * HEAD_SIZE : (h + 1) * HEAD_SIZE] = ctx
        totals = jnp.where(lane == h, jnp.sum(p, axis=1, keepdims=True), totals)
    t_ref[...] = jnp.transpose(totals)[: t_ref.shape[0], :]


def butterfly(x, axis, combine):
    n = lax.axis_size(axis)
    d = 1
    while d < n:
        x = combine(x, lax.ppermute(x, axis, [(i, i ^ d) for i in range(n)]))
        d *= 2
    return x


def far_part(queries_kv, keys_t, values, lo, hi, blk, kv, heads, blk_index, scale):
    tok_dev, q_cols = queries_kv.shape
    blocks, _, block_len = keys_t.shape
    gathered = lax.all_gather(queries_kv, "blk", axis=0, tiled=True)
    row_count = gathered.shape[0]
    n_tiles = row_count // tok_dev
    stat_rows = 8
    q_spec = pl.BlockSpec((tok_dev, q_cols), lambda i, *_: (i, 0))
    kt_spec = pl.BlockSpec((blocks, HEAD_SIZE, block_len), lambda i, *_: (0, kv, 0))
    v_spec = pl.BlockSpec((blocks, block_len, HEAD_SIZE), lambda i, *_: (0, 0, kv))
    s_spec = pl.BlockSpec((stat_rows, tok_dev), lambda i, *_: (i, 0))
    stat_shape = jax.ShapeDtypeStruct((n_tiles * stat_rows, tok_dev), jnp.float32)
    kw = dict(heads=heads, scale=scale)
    local_max = pl.pallas_call(
        functools.partial(max_kernel, **kw),
        out_shape=stat_shape,
        grid_spec=pltpu.PrefetchScalarGridSpec(
            num_scalar_prefetch=3, grid=(n_tiles,), in_specs=[q_spec, kt_spec], out_specs=s_spec
        ),
    )(lo, hi, blk, gathered, keys_t)
    far_max = butterfly(local_max, "blk", jnp.maximum)
    partial, totals = pl.pallas_call(
        functools.partial(ctx_kernel, **kw),
        out_shape=(jax.ShapeDtypeStruct((row_count, q_cols), jnp.float32), stat_shape),
        grid_spec=pltpu.PrefetchScalarGridSpec(
            num_scalar_prefetch=3,
            grid=(n_tiles,),
            in_specs=[q_spec, kt_spec, v_spec, s_spec],
            out_specs=(pl.BlockSpec((tok_dev, q_cols), lambda i, *_: (i, 0)), s_spec),
        ),
    )(lo, hi, blk, gathered, keys_t, values, far_max)
    context = lax.psum_scatter(partial, "blk", scatter_dimension=0, tiled=True)
    totals = butterfly(totals, "blk", jnp.add)
    own = lambda a: jnp.transpose(
        lax.dynamic_slice_in_dim(a, blk_index * stat_rows, stat_rows, 0)[:heads]
    )
    return context, own(totals), own(far_max)


def per_device(
    queries,
    suffix_key_rows,
    suffix_value_rows,
    prefix_block_keys,
    prefix_block_values,
    block_group,
    suffix_len,
    request_group,
    w_out,
):
    tok_dev = queries.shape[0]
    q_cols = queries.shape[1]
    kv_cols = suffix_key_rows.shape[1]
    local_kv = kv_cols // HEAD_SIZE
    local_heads = q_cols // HEAD_SIZE
    qgw = local_heads // local_kv
    blocks, block_len, _ = prefix_block_keys.shape
    blk_count = lax.axis_size("blk")
    row_count = blk_count * tok_dev
    blk_index = lax.axis_index("blk")
    scale = 1.0 / math.sqrt(HEAD_SIZE)
    tile = tok_dev
    n_tiles = row_count // tile

    lo, hi, blk = tile_tables(suffix_len, request_group, block_group, n_tiles, tile)
    keys_t = jnp.swapaxes(prefix_block_keys, 1, 2)
    parts = [
        far_part(
            queries[:, kv * qgw * HEAD_SIZE : (kv + 1) * qgw * HEAD_SIZE],
            keys_t,
            prefix_block_values,
            lo,
            hi,
            blk,
            kv,
            qgw,
            blk_index,
            scale,
        )
        for kv in range(local_kv)
    ]
    far_context = jnp.concatenate([c for c, _, _ in parts], axis=1).reshape(
        tok_dev, local_kv, qgw, HEAD_SIZE
    )
    far_total = jnp.concatenate([t for _, t, _ in parts], axis=1).reshape(tok_dev, local_kv, qgw)
    own_far_max = jnp.concatenate([m for _, _, m in parts], axis=1).reshape(
        tok_dev, local_kv, qgw
    )

    row_ends = jnp.cumsum(suffix_len)
    starts = row_ends - suffix_len
    own_rows = blk_index * tok_dev + jnp.arange(tok_dev, dtype=jnp.int32)
    earlier_keys, earlier_values = from_behind((suffix_key_rows, suffix_value_rows), "blk", 1)
    near_keys = jnp.concatenate([earlier_keys, suffix_key_rows], axis=0).reshape(
        2 * tok_dev, local_kv, HEAD_SIZE
    )
    near_values = jnp.concatenate([earlier_values, suffix_value_rows], axis=0).reshape(
        2 * tok_dev, local_kv, HEAD_SIZE
    )
    near_rows = (blk_index - 1) * tok_dev + jnp.arange(2 * tok_dev, dtype=jnp.int32)
    own_req = request_of(own_rows, starts, row_ends)
    near_req = request_of(near_rows, starts, row_ends)
    allowed = (
        (own_req[:, None] == near_req[None, :])
        & (near_rows[None, :] <= own_rows[:, None])
        & (near_rows[None, :] >= 0)
    )
    own_queries = queries.reshape(tok_dev, local_kv, qgw, HEAD_SIZE)
    near_scores = (
        jnp.einsum("sgjd,tgd->sgjt", own_queries, near_keys, preferred_element_type=jnp.float32)
        * scale
    )
    near_scores = jnp.where(allowed[:, None, None, :], near_scores, -jnp.inf)
    near_max = jnp.max(near_scores, axis=3)
    top = jnp.maximum(own_far_max, near_max)
    near_prob = jnp.exp(near_scores - top[..., None])
    near_total = jnp.sum(near_prob, axis=3)
    near_context = jnp.einsum(
        "sgjt,tgd->sgjd",
        near_prob.astype(jnp.bfloat16),
        near_values,
        preferred_element_type=jnp.float32,
    )
    far_scale = jnp.exp(own_far_max - top)
    context = far_context * far_scale[..., None] + near_context
    denominator = far_total * far_scale + near_total
    attention = (context / denominator[..., None]).reshape(tok_dev, q_cols).astype(jnp.bfloat16)
    projected = jnp.dot(attention, w_out, preferred_element_type=jnp.float32)
    return lax.psum_scatter(projected, "kvh", scatter_dimension=1, tiled=True).astype(jnp.bfloat16)


def solution(mesh):
    placed = (
        P("blk", "kvh"),
        P("blk", "kvh"),
        P("blk", "kvh"),
        P("blk", None, "kvh"),
        P("blk", None, "kvh"),
        P("blk"),
        P(),
        P(),
        P("kvh", None),
    )
    return jax.shard_map(
        per_device, mesh=mesh, in_specs=placed, out_specs=P("blk", "kvh"), check_vma=False
    )
```

```python
import functools
import math

import jax
import jax.numpy as jnp
from jax import lax
from jax.experimental import pallas as pl
from jax.experimental.pallas import tpu as pltpu
from jax.sharding import PartitionSpec as P

HEAD_SIZE = 128
SLOTS = 5
STAT_LANES = 128


def from_behind(block, axis, distance):
    devices = range(lax.axis_size(axis))
    route = [(i - distance, i) for i in devices if i - distance in devices]
    return lax.ppermute(block, axis, route)


def request_of(row_ids, starts, row_ends):
    inside = (row_ids[:, None] >= starts[None, :]) & (row_ids[:, None] < row_ends[None, :])
    req_ids = jnp.arange(starts.shape[0], dtype=jnp.int32)
    return jnp.sum(jnp.where(inside, req_ids[None, :], 0), axis=1)


def tile_tables(suffix_len, request_group, block_group, n_tiles, tile):
    row_ends = jnp.cumsum(suffix_len).astype(jnp.int32)
    starts = row_ends - suffix_len
    tile_lo = jnp.arange(n_tiles, dtype=jnp.int32) * tile
    first = jnp.sum((row_ends[None, :] <= tile_lo[:, None]).astype(jnp.int32), axis=1)
    last = jnp.sum((row_ends[None, :] <= (tile_lo + tile - 1)[:, None]).astype(jnp.int32), axis=1)
    req = first[:, None] + jnp.arange(SLOTS, dtype=jnp.int32)[None, :]
    valid = req <= last[:, None]
    req_v = jnp.minimum(req, last[:, None])
    lo = jnp.where(valid, starts[req_v], 0).astype(jnp.int32)
    hi = jnp.where(valid, row_ends[req_v], 0).astype(jnp.int32)
    group_count = suffix_len.shape[0] // 4
    blocks = block_group.shape[0]
    owns = block_group[None, :] == jnp.arange(group_count, dtype=jnp.int32)[:, None]
    block_of_group = jnp.sum(
        jnp.where(owns, jnp.arange(blocks, dtype=jnp.int32)[None, :], 0), axis=1
    ).astype(jnp.int32)
    blk = block_of_group[request_group[req_v]].astype(jnp.int32)
    return lo.reshape(-1), hi.reshape(-1), blk.reshape(-1)


def _slot_mask(lo_ref, hi_ref, base, rows):
    seg = lax.broadcasted_iota(jnp.int32, (1, SLOTS * HEAD_SIZE), 1) // HEAD_SIZE
    lo = jnp.zeros(seg.shape, jnp.int32)
    hi = jnp.zeros(seg.shape, jnp.int32)
    for s in range(SLOTS):
        lo = jnp.where(seg == s, lo_ref[base + s], lo)
        hi = jnp.where(seg == s, hi_ref[base + s], hi)
    return (rows >= lo) & (rows < hi)


def _slot_keys(kt_ref, blk_ref, base, kv):
    cols = slice(kv * HEAD_SIZE, (kv + 1) * HEAD_SIZE)
    return jnp.concatenate([kt_ref[blk_ref[base + s], cols, :] for s in range(SLOTS)], axis=1)


def _slot_values(v_ref, blk_ref, base, kv):
    cols = slice(kv * HEAD_SIZE, (kv + 1) * HEAD_SIZE)
    return jnp.concatenate([v_ref[blk_ref[base + s], :, cols] for s in range(SLOTS)], axis=0)


def max_kernel(lo_ref, hi_ref, blk_ref, q_ref, kt_ref, m_ref, *, heads, qgw, scale):
    i = pl.program_id(0)
    tile = q_ref.shape[0]
    base = i * SLOTS
    rows = i * tile + lax.broadcasted_iota(jnp.int32, (tile, 1), 0)
    mask = _slot_mask(lo_ref, hi_ref, base, rows)
    lane = lax.broadcasted_iota(jnp.int32, (1, STAT_LANES), 1)
    stats = jnp.full((tile, STAT_LANES), -jnp.inf, jnp.float32)
    for h in range(heads):
        if h % qgw == 0:
            keys = _slot_keys(kt_ref, blk_ref, base, h // qgw)
        q = q_ref[:, h * HEAD_SIZE : (h + 1) * HEAD_SIZE]
        sc = jnp.dot(q, keys, preferred_element_type=jnp.float32) * scale
        mx = jnp.max(jnp.where(mask, sc, -jnp.inf), axis=1, keepdims=True)
        stats = jnp.where(lane == h, mx, stats)
    m_ref[...] = jnp.transpose(stats)[: m_ref.shape[0], :]


def ctx_kernel(
    lo_ref, hi_ref, blk_ref, q_ref, kt_ref, v_ref, m_ref, o_ref, t_ref, *, heads, qgw, scale
):
    i = pl.program_id(0)
    tile = q_ref.shape[0]
    base = i * SLOTS
    rows = i * tile + lax.broadcasted_iota(jnp.int32, (tile, 1), 0)
    mask = _slot_mask(lo_ref, hi_ref, base, rows)
    lane = lax.broadcasted_iota(jnp.int32, (1, STAT_LANES), 1)
    totals = jnp.zeros((tile, STAT_LANES), jnp.float32)
    top = jnp.transpose(m_ref[...])
    for h in range(heads):
        if h % qgw == 0:
            keys = _slot_keys(kt_ref, blk_ref, base, h // qgw)
            values = _slot_values(v_ref, blk_ref, base, h // qgw)
        q = q_ref[:, h * HEAD_SIZE : (h + 1) * HEAD_SIZE]
        sc = jnp.dot(q, keys, preferred_element_type=jnp.float32) * scale
        p = jnp.exp(jnp.where(mask, sc - top[:, h : h + 1], -jnp.inf))
        ctx = jnp.dot(p.astype(jnp.bfloat16), values, preferred_element_type=jnp.float32)
        o_ref[:, h * HEAD_SIZE : (h + 1) * HEAD_SIZE] = ctx
        totals = jnp.where(lane == h, jnp.sum(p, axis=1, keepdims=True), totals)
    t_ref[...] = jnp.transpose(totals)[: t_ref.shape[0], :]


def butterfly(x, axis, combine):
    n = lax.axis_size(axis)
    d = 1
    while d < n:
        x = combine(x, lax.ppermute(x, axis, [(i, i ^ d) for i in range(n)]))
        d *= 2
    return x


def far_part(queries, keys_t, values, lo, hi, blk, qgw, blk_index, scale):
    tok_dev, q_cols = queries.shape
    heads = q_cols // HEAD_SIZE
    blocks, kv_cols, block_len = keys_t.shape
    gathered = lax.all_gather(queries, "blk", axis=0, tiled=True)
    row_count = gathered.shape[0]
    n_tiles = row_count // tok_dev
    stat_rows = 8
    q_spec = pl.BlockSpec((tok_dev, q_cols), lambda i, *_: (i, 0))
    kt_spec = pl.BlockSpec((blocks, kv_cols, block_len), lambda i, *_: (0, 0, 0))
    v_spec = pl.BlockSpec((blocks, block_len, kv_cols), lambda i, *_: (0, 0, 0))
    s_spec = pl.BlockSpec((stat_rows, tok_dev), lambda i, *_: (i, 0))
    stat_shape = jax.ShapeDtypeStruct((n_tiles * stat_rows, tok_dev), jnp.float32)
    kw = dict(heads=heads, qgw=qgw, scale=scale)
    local_max = pl.pallas_call(
        functools.partial(max_kernel, **kw),
        out_shape=stat_shape,
        grid_spec=pltpu.PrefetchScalarGridSpec(
            num_scalar_prefetch=3, grid=(n_tiles,), in_specs=[q_spec, kt_spec], out_specs=s_spec
        ),
    )(lo, hi, blk, gathered, keys_t)
    far_max = butterfly(local_max, "blk", jnp.maximum)
    partial, totals = pl.pallas_call(
        functools.partial(ctx_kernel, **kw),
        out_shape=(jax.ShapeDtypeStruct((row_count, q_cols), jnp.float32), stat_shape),
        grid_spec=pltpu.PrefetchScalarGridSpec(
            num_scalar_prefetch=3,
            grid=(n_tiles,),
            in_specs=[q_spec, kt_spec, v_spec, s_spec],
            out_specs=(pl.BlockSpec((tok_dev, q_cols), lambda i, *_: (i, 0)), s_spec),
        ),
    )(lo, hi, blk, gathered, keys_t, values, far_max)
    context = lax.psum_scatter(partial, "blk", scatter_dimension=0, tiled=True)
    totals = butterfly(totals, "blk", jnp.add)
    own = lambda a: jnp.transpose(
        lax.dynamic_slice_in_dim(a, blk_index * stat_rows, stat_rows, 0)[:heads]
    )
    return context, own(totals), own(far_max)


def column_sum(x, axis):
    n = lax.axis_size(axis)
    me = lax.axis_index(axis)
    width = x.shape[1] // n
    chunk = lambda k: lax.dynamic_slice_in_dim(x, (k % n) * width, width, 1)
    total = chunk(me)
    for d in range(1, n):
        total = total + lax.ppermute(chunk(me + d), axis, [(i, (i + d) % n) for i in range(n)])
    return total


def per_device(
    queries,
    suffix_key_rows,
    suffix_value_rows,
    prefix_block_keys,
    prefix_block_values,
    block_group,
    suffix_len,
    request_group,
    w_out,
):
    tok_dev = queries.shape[0]
    q_cols = queries.shape[1]
    kv_cols = suffix_key_rows.shape[1]
    local_kv = kv_cols // HEAD_SIZE
    local_heads = q_cols // HEAD_SIZE
    qgw = local_heads // local_kv
    blocks, block_len, _ = prefix_block_keys.shape
    blk_count = lax.axis_size("blk")
    row_count = blk_count * tok_dev
    blk_index = lax.axis_index("blk")
    scale = 1.0 / math.sqrt(HEAD_SIZE)
    tile = tok_dev
    n_tiles = row_count // tile

    lo, hi, blk = tile_tables(suffix_len, request_group, block_group, n_tiles, tile)
    keys_t = jnp.swapaxes(prefix_block_keys, 1, 2)
    far_context, far_total, own_far_max = far_part(
        queries, keys_t, prefix_block_values, lo, hi, blk, qgw, blk_index, scale
    )
    far_context = far_context.reshape(tok_dev, local_kv, qgw, HEAD_SIZE)
    far_total = far_total.reshape(tok_dev, local_kv, qgw)
    own_far_max = own_far_max.reshape(tok_dev, local_kv, qgw)

    row_ends = jnp.cumsum(suffix_len)
    starts = row_ends - suffix_len
    own_rows = blk_index * tok_dev + jnp.arange(tok_dev, dtype=jnp.int32)
    earlier_keys, earlier_values = from_behind((suffix_key_rows, suffix_value_rows), "blk", 1)
    near_keys = jnp.concatenate([earlier_keys, suffix_key_rows], axis=0).reshape(
        2 * tok_dev, local_kv, HEAD_SIZE
    )
    near_values = jnp.concatenate([earlier_values, suffix_value_rows], axis=0).reshape(
        2 * tok_dev, local_kv, HEAD_SIZE
    )
    near_rows = (blk_index - 1) * tok_dev + jnp.arange(2 * tok_dev, dtype=jnp.int32)
    own_req = request_of(own_rows, starts, row_ends)
    near_req = request_of(near_rows, starts, row_ends)
    allowed = (
        (own_req[:, None] == near_req[None, :])
        & (near_rows[None, :] <= own_rows[:, None])
        & (near_rows[None, :] >= 0)
    )
    own_queries = queries.reshape(tok_dev, local_kv, qgw, HEAD_SIZE)
    near_scores = (
        jnp.einsum("sgjd,tgd->sgjt", own_queries, near_keys, preferred_element_type=jnp.float32)
        * scale
    )
    near_scores = jnp.where(allowed[:, None, None, :], near_scores, -jnp.inf)
    near_max = jnp.max(near_scores, axis=3)
    top = jnp.maximum(own_far_max, near_max)
    near_prob = jnp.exp(near_scores - top[..., None])
    near_total = jnp.sum(near_prob, axis=3)
    near_context = jnp.einsum(
        "sgjt,tgd->sgjd",
        near_prob.astype(jnp.bfloat16),
        near_values,
        preferred_element_type=jnp.float32,
    )
    far_scale = jnp.exp(own_far_max - top)
    context = far_context * far_scale[..., None] + near_context
    denominator = far_total * far_scale + near_total
    attention = (context / denominator[..., None]).reshape(tok_dev, q_cols).astype(jnp.bfloat16)
    projected = jnp.dot(attention, w_out, preferred_element_type=jnp.float32)
    return column_sum(projected, "kvh").astype(jnp.bfloat16)


def solution(mesh):
    placed = (
        P("blk", "kvh"),
        P("blk", "kvh"),
        P("blk", "kvh"),
        P("blk", None, "kvh"),
        P("blk", None, "kvh"),
        P("blk"),
        P(),
        P(),
        P("kvh", None),
    )
    return jax.shard_map(
        per_device, mesh=mesh, in_specs=placed, out_specs=P("blk", "kvh"), check_vma=False
    )
```

```python
import functools
import math

import jax
import jax.numpy as jnp
from jax import lax
from jax.experimental import pallas as pl
from jax.experimental.pallas import tpu as pltpu
from jax.sharding import PartitionSpec as P

HEAD_SIZE = 128
SLOTS = 5
STAT_LANES = 128


def from_behind(block, axis, distance):
    devices = range(lax.axis_size(axis))
    route = [(i - distance, i) for i in devices if i - distance in devices]
    return lax.ppermute(block, axis, route)


def request_of(row_ids, starts, row_ends):
    inside = (row_ids[:, None] >= starts[None, :]) & (row_ids[:, None] < row_ends[None, :])
    req_ids = jnp.arange(starts.shape[0], dtype=jnp.int32)
    return jnp.sum(jnp.where(inside, req_ids[None, :], 0), axis=1)


def tile_tables(suffix_len, request_group, block_group, n_tiles, tile):
    row_ends = jnp.cumsum(suffix_len).astype(jnp.int32)
    starts = row_ends - suffix_len
    tile_lo = jnp.arange(n_tiles, dtype=jnp.int32) * tile
    first = jnp.sum((row_ends[None, :] <= tile_lo[:, None]).astype(jnp.int32), axis=1)
    last = jnp.sum((row_ends[None, :] <= (tile_lo + tile - 1)[:, None]).astype(jnp.int32), axis=1)
    req = first[:, None] + jnp.arange(SLOTS, dtype=jnp.int32)[None, :]
    valid = req <= last[:, None]
    req_v = jnp.minimum(req, last[:, None])
    lo = jnp.where(valid, starts[req_v], 0).astype(jnp.int32)
    hi = jnp.where(valid, row_ends[req_v], 0).astype(jnp.int32)
    group_count = suffix_len.shape[0] // 4
    blocks = block_group.shape[0]
    owns = block_group[None, :] == jnp.arange(group_count, dtype=jnp.int32)[:, None]
    block_of_group = jnp.sum(
        jnp.where(owns, jnp.arange(blocks, dtype=jnp.int32)[None, :], 0), axis=1
    ).astype(jnp.int32)
    blk = block_of_group[request_group[req_v]].astype(jnp.int32)
    count = jnp.minimum(last - first + 1, SLOTS).astype(jnp.int32)
    return lo.reshape(-1), hi.reshape(-1), blk.reshape(-1), count


def max_kernel(lo_ref, hi_ref, blk_ref, cnt_ref, q_ref, kt_ref, m_ref, *, heads, qgw, scale):
    i = pl.program_id(0)
    tile = q_ref.shape[0]
    base = i * SLOTS
    rows = i * tile + lax.broadcasted_iota(jnp.int32, (tile, 1), 0)
    lane = lax.broadcasted_iota(jnp.int32, (1, STAT_LANES), 1)
    stats = jnp.full((tile, STAT_LANES), -jnp.inf, jnp.float32)
    for h in range(heads):
        kv = h // qgw
        q = q_ref[:, h * HEAD_SIZE : (h + 1) * HEAD_SIZE]

        def body(s, top):
            j = blk_ref[base + s]
            inside = (rows >= lo_ref[base + s]) & (rows < hi_ref[base + s])
            keys = kt_ref[j, kv * HEAD_SIZE : (kv + 1) * HEAD_SIZE, :]
            sc = jnp.dot(q, keys, preferred_element_type=jnp.float32)
            mx = jnp.max(sc, axis=1, keepdims=True) * scale
            return jnp.where(inside, mx, top)

        top = lax.fori_loop(0, cnt_ref[i], body, jnp.full((tile, 1), -jnp.inf, jnp.float32))
        stats = jnp.where(lane == h, top, stats)
    m_ref[...] = jnp.transpose(stats)[: m_ref.shape[0], :]


def ctx_kernel(
    lo_ref, hi_ref, blk_ref, cnt_ref, q_ref, kt_ref, v_ref, m_ref, o_ref, t_ref, *, heads, qgw, scale
):
    i = pl.program_id(0)
    tile = q_ref.shape[0]
    base = i * SLOTS
    rows = i * tile + lax.broadcasted_iota(jnp.int32, (tile, 1), 0)
    lane = lax.broadcasted_iota(jnp.int32, (1, STAT_LANES), 1)
    totals = jnp.zeros((tile, STAT_LANES), jnp.float32)
    tops = jnp.transpose(m_ref[...])
    for h in range(heads):
        kv = h // qgw
        cols = slice(kv * HEAD_SIZE, (kv + 1) * HEAD_SIZE)
        q = q_ref[:, h * HEAD_SIZE : (h + 1) * HEAD_SIZE]
        top = tops[:, h : h + 1]

        def body(s, carry):
            acc, tot = carry
            j = blk_ref[base + s]
            inside = (rows >= lo_ref[base + s]) & (rows < hi_ref[base + s])
            shift = jnp.where(inside, top, jnp.inf)
            sc = jnp.dot(q, kt_ref[j, cols, :], preferred_element_type=jnp.float32) * scale
            p = jnp.exp(sc - shift)
            acc = acc + jnp.dot(
                p.astype(jnp.bfloat16), v_ref[j, :, cols], preferred_element_type=jnp.float32
            )
            return acc, tot + jnp.sum(p, axis=1, keepdims=True)

        acc, tot = lax.fori_loop(
            0,
            cnt_ref[i],
            body,
            (jnp.zeros((tile, HEAD_SIZE), jnp.float32), jnp.zeros((tile, 1), jnp.float32)),
        )
        o_ref[:, h * HEAD_SIZE : (h + 1) * HEAD_SIZE] = acc
        totals = jnp.where(lane == h, tot, totals)
    t_ref[...] = jnp.transpose(totals)[: t_ref.shape[0], :]


def butterfly(x, axis, combine):
    n = lax.axis_size(axis)
    d = 1
    while d < n:
        x = combine(x, lax.ppermute(x, axis, [(i, i ^ d) for i in range(n)]))
        d *= 2
    return x


def far_part(queries, keys_t, values, tables, qgw, blk_index, scale):
    tok_dev, q_cols = queries.shape
    heads = q_cols // HEAD_SIZE
    blocks, kv_cols, block_len = keys_t.shape
    gathered = lax.all_gather(queries, "blk", axis=0, tiled=True)
    row_count = gathered.shape[0]
    n_tiles = row_count // tok_dev
    stat_rows = 8
    q_spec = pl.BlockSpec((tok_dev, q_cols), lambda i, *_: (i, 0))
    kt_spec = pl.BlockSpec((blocks, kv_cols, block_len), lambda i, *_: (0, 0, 0))
    v_spec = pl.BlockSpec((blocks, block_len, kv_cols), lambda i, *_: (0, 0, 0))
    s_spec = pl.BlockSpec((stat_rows, tok_dev), lambda i, *_: (i, 0))
    stat_shape = jax.ShapeDtypeStruct((n_tiles * stat_rows, tok_dev), jnp.float32)
    kw = dict(heads=heads, qgw=qgw, scale=scale)
    local_max = pl.pallas_call(
        functools.partial(max_kernel, **kw),
        out_shape=stat_shape,
        grid_spec=pltpu.PrefetchScalarGridSpec(
            num_scalar_prefetch=4, grid=(n_tiles,), in_specs=[q_spec, kt_spec], out_specs=s_spec
        ),
    )(*tables, gathered, keys_t)
    far_max = butterfly(local_max, "blk", jnp.maximum)
    partial, totals = pl.pallas_call(
        functools.partial(ctx_kernel, **kw),
        out_shape=(jax.ShapeDtypeStruct((row_count, q_cols), jnp.float32), stat_shape),
        grid_spec=pltpu.PrefetchScalarGridSpec(
            num_scalar_prefetch=4,
            grid=(n_tiles,),
            in_specs=[q_spec, kt_spec, v_spec, s_spec],
            out_specs=(pl.BlockSpec((tok_dev, q_cols), lambda i, *_: (i, 0)), s_spec),
        ),
    )(*tables, gathered, keys_t, values, far_max)
    context = lax.psum_scatter(partial, "blk", scatter_dimension=0, tiled=True)
    totals = butterfly(totals, "blk", jnp.add)
    own = lambda a: jnp.transpose(
        lax.dynamic_slice_in_dim(a, blk_index * stat_rows, stat_rows, 0)[:heads]
    )
    return context, own(totals), own(far_max)


def column_sum(x, axis):
    n = lax.axis_size(axis)
    me = lax.axis_index(axis)
    width = x.shape[1] // n
    chunk = lambda k: lax.dynamic_slice_in_dim(x, (k % n) * width, width, 1)
    total = chunk(me)
    for d in range(1, n):
        total = total + lax.ppermute(chunk(me + d), axis, [(i, (i + d) % n) for i in range(n)])
    return total


def per_device(
    queries,
    suffix_key_rows,
    suffix_value_rows,
    prefix_block_keys,
    prefix_block_values,
    block_group,
    suffix_len,
    request_group,
    w_out,
):
    tok_dev = queries.shape[0]
    q_cols = queries.shape[1]
    kv_cols = suffix_key_rows.shape[1]
    local_kv = kv_cols // HEAD_SIZE
    local_heads = q_cols // HEAD_SIZE
    qgw = local_heads // local_kv
    blocks, block_len, _ = prefix_block_keys.shape
    blk_count = lax.axis_size("blk")
    row_count = blk_count * tok_dev
    blk_index = lax.axis_index("blk")
    scale = 1.0 / math.sqrt(HEAD_SIZE)
    tile = tok_dev
    n_tiles = row_count // tile

    tables = tile_tables(suffix_len, request_group, block_group, n_tiles, tile)
    keys_t = jnp.swapaxes(prefix_block_keys, 1, 2)
    far_context, far_total, own_far_max = far_part(
        queries, keys_t, prefix_block_values, tables, qgw, blk_index, scale
    )
    far_context = far_context.reshape(tok_dev, local_kv, qgw, HEAD_SIZE)
    far_total = far_total.reshape(tok_dev, local_kv, qgw)
    own_far_max = own_far_max.reshape(tok_dev, local_kv, qgw)

    row_ends = jnp.cumsum(suffix_len)
    starts = row_ends - suffix_len
    own_rows = blk_index * tok_dev + jnp.arange(tok_dev, dtype=jnp.int32)
    earlier_keys, earlier_values = from_behind((suffix_key_rows, suffix_value_rows), "blk", 1)
    near_keys = jnp.concatenate([earlier_keys, suffix_key_rows], axis=0).reshape(
        2 * tok_dev, local_kv, HEAD_SIZE
    )
    near_values = jnp.concatenate([earlier_values, suffix_value_rows], axis=0).reshape(
        2 * tok_dev, local_kv, HEAD_SIZE
    )
    near_rows = (blk_index - 1) * tok_dev + jnp.arange(2 * tok_dev, dtype=jnp.int32)
    own_req = request_of(own_rows, starts, row_ends)
    near_req = request_of(near_rows, starts, row_ends)
    allowed = (
        (own_req[:, None] == near_req[None, :])
        & (near_rows[None, :] <= own_rows[:, None])
        & (near_rows[None, :] >= 0)
    )
    own_queries = queries.reshape(tok_dev, local_kv, qgw, HEAD_SIZE)
    near_scores = (
        jnp.einsum("sgjd,tgd->sgjt", own_queries, near_keys, preferred_element_type=jnp.float32)
        * scale
    )
    near_scores = jnp.where(allowed[:, None, None, :], near_scores, -jnp.inf)
    near_max = jnp.max(near_scores, axis=3)
    top = jnp.maximum(own_far_max, near_max)
    near_prob = jnp.exp(near_scores - top[..., None])
    near_total = jnp.sum(near_prob, axis=3)
    near_context = jnp.einsum(
        "sgjt,tgd->sgjd",
        near_prob.astype(jnp.bfloat16),
        near_values,
        preferred_element_type=jnp.float32,
    )
    far_scale = jnp.exp(own_far_max - top)
    context = far_context * far_scale[..., None] + near_context
    denominator = far_total * far_scale + near_total
    attention = (context / denominator[..., None]).reshape(tok_dev, q_cols).astype(jnp.bfloat16)
    projected = jnp.dot(attention, w_out, preferred_element_type=jnp.float32)
    return column_sum(projected, "kvh").astype(jnp.bfloat16)


def solution(mesh):
    placed = (
        P("blk", "kvh"),
        P("blk", "kvh"),
        P("blk", "kvh"),
        P("blk", None, "kvh"),
        P("blk", None, "kvh"),
        P("blk"),
        P(),
        P(),
        P("kvh", None),
    )
    return jax.shard_map(
        per_device, mesh=mesh, in_specs=placed, out_specs=P("blk", "kvh"), check_vma=False
    )
```

```python
import functools
import math

import jax
import jax.numpy as jnp
from jax import lax
from jax.experimental import pallas as pl
from jax.experimental.pallas import tpu as pltpu
from jax.sharding import PartitionSpec as P

HEAD_SIZE = 128
SLOTS = 5
STAT_LANES = 128
CHIP, CORE = "chip", "c"
BLK = (CHIP, CORE)
CORES = 2


def from_behind(block, axis, distance):
    devices = range(blk_size())
    route = [(i - distance, i) for i in devices if i - distance in devices]
    return lax.ppermute(block, axis, route)


def request_of(row_ids, starts, row_ends):
    inside = (row_ids[:, None] >= starts[None, :]) & (row_ids[:, None] < row_ends[None, :])
    req_ids = jnp.arange(starts.shape[0], dtype=jnp.int32)
    return jnp.sum(jnp.where(inside, req_ids[None, :], 0), axis=1)


def tile_tables(suffix_len, request_group, block_group, n_tiles, tile):
    row_ends = jnp.cumsum(suffix_len).astype(jnp.int32)
    starts = row_ends - suffix_len
    tile_lo = jnp.arange(n_tiles, dtype=jnp.int32) * tile
    first = jnp.sum((row_ends[None, :] <= tile_lo[:, None]).astype(jnp.int32), axis=1)
    last = jnp.sum((row_ends[None, :] <= (tile_lo + tile - 1)[:, None]).astype(jnp.int32), axis=1)
    req = first[:, None] + jnp.arange(SLOTS, dtype=jnp.int32)[None, :]
    valid = req <= last[:, None]
    req_v = jnp.minimum(req, last[:, None])
    lo = jnp.where(valid, starts[req_v], 0).astype(jnp.int32)
    hi = jnp.where(valid, row_ends[req_v], 0).astype(jnp.int32)
    group_count = suffix_len.shape[0] // 4
    blocks = block_group.shape[0]
    owns = block_group[None, :] == jnp.arange(group_count, dtype=jnp.int32)[:, None]
    block_of_group = jnp.sum(
        jnp.where(owns, jnp.arange(blocks, dtype=jnp.int32)[None, :], 0), axis=1
    ).astype(jnp.int32)
    blk = block_of_group[request_group[req_v]].astype(jnp.int32)
    return lo.reshape(-1), hi.reshape(-1), blk.reshape(-1)


def _slot_mask(lo_ref, hi_ref, base, rows):
    seg = lax.broadcasted_iota(jnp.int32, (1, SLOTS * HEAD_SIZE), 1) // HEAD_SIZE
    lo = jnp.zeros(seg.shape, jnp.int32)
    hi = jnp.zeros(seg.shape, jnp.int32)
    for s in range(SLOTS):
        lo = jnp.where(seg == s, lo_ref[base + s], lo)
        hi = jnp.where(seg == s, hi_ref[base + s], hi)
    return (rows >= lo) & (rows < hi)


def _slot_keys(kt_ref, blk_ref, base, kv):
    cols = slice(kv * HEAD_SIZE, (kv + 1) * HEAD_SIZE)
    return jnp.concatenate([kt_ref[blk_ref[base + s], cols, :] for s in range(SLOTS)], axis=1)


def _slot_values(v_ref, blk_ref, base, kv):
    cols = slice(kv * HEAD_SIZE, (kv + 1) * HEAD_SIZE)
    return jnp.concatenate([v_ref[blk_ref[base + s], :, cols] for s in range(SLOTS)], axis=0)


def max_kernel(lo_ref, hi_ref, blk_ref, q_ref, kt_ref, m_ref, *, heads, qgw, scale):
    i = pl.program_id(0)
    tile = q_ref.shape[0]
    base = i * SLOTS
    rows = i * tile + lax.broadcasted_iota(jnp.int32, (tile, 1), 0)
    mask = _slot_mask(lo_ref, hi_ref, base, rows)
    lane = lax.broadcasted_iota(jnp.int32, (1, STAT_LANES), 1)
    stats = jnp.full((tile, STAT_LANES), -jnp.inf, jnp.float32)
    for h in range(heads):
        if h % qgw == 0:
            keys = _slot_keys(kt_ref, blk_ref, base, h // qgw)
        q = q_ref[:, h * HEAD_SIZE : (h + 1) * HEAD_SIZE]
        sc = jnp.dot(q, keys, preferred_element_type=jnp.float32) * scale
        mx = jnp.max(jnp.where(mask, sc, -jnp.inf), axis=1, keepdims=True)
        stats = jnp.where(lane == h, mx, stats)
    m_ref[...] = jnp.transpose(stats)[: m_ref.shape[0], :]


def ctx_kernel(
    lo_ref, hi_ref, blk_ref, q_ref, kt_ref, v_ref, m_ref, o_ref, t_ref, *, heads, qgw, scale
):
    i = pl.program_id(0)
    tile = q_ref.shape[0]
    base = i * SLOTS
    rows = i * tile + lax.broadcasted_iota(jnp.int32, (tile, 1), 0)
    mask = _slot_mask(lo_ref, hi_ref, base, rows)
    lane = lax.broadcasted_iota(jnp.int32, (1, STAT_LANES), 1)
    totals = jnp.zeros((tile, STAT_LANES), jnp.float32)
    top = jnp.transpose(m_ref[...])
    for h in range(heads):
        if h % qgw == 0:
            keys = _slot_keys(kt_ref, blk_ref, base, h // qgw)
            values = _slot_values(v_ref, blk_ref, base, h // qgw)
        q = q_ref[:, h * HEAD_SIZE : (h + 1) * HEAD_SIZE]
        sc = jnp.dot(q, keys, preferred_element_type=jnp.float32) * scale
        p = jnp.exp(jnp.where(mask, sc - top[:, h : h + 1], -jnp.inf))
        ctx = jnp.dot(p.astype(jnp.bfloat16), values, preferred_element_type=jnp.float32)
        o_ref[:, h * HEAD_SIZE : (h + 1) * HEAD_SIZE] = ctx
        totals = jnp.where(lane == h, jnp.sum(p, axis=1, keepdims=True), totals)
    t_ref[...] = jnp.transpose(totals)[: t_ref.shape[0], :]


def blk_size():
    return lax.axis_size(CHIP) * lax.axis_size(CORE)


def blk_position():
    return lax.axis_index(CHIP) * lax.axis_size(CORE) + lax.axis_index(CORE)


def chip_then_core_sum(partial, tok_dev):
    cores = lax.axis_size(CORE)
    core = lax.axis_index(CORE)
    split = partial.reshape(-1, cores, tok_dev, partial.shape[1])
    keep = lax.dynamic_index_in_dim(split, core, 1, keepdims=False)
    send = lax.dynamic_index_in_dim(split, 1 - core, 1, keepdims=False)
    pair = keep + lax.ppermute(send, CORE, [(0, 1), (1, 0)])
    return lax.psum_scatter(pair, CHIP, scatter_dimension=0, tiled=True).reshape(tok_dev, -1)


def butterfly(x, axis, combine):
    n = blk_size()
    d = 1
    while d < n:
        x = combine(x, lax.ppermute(x, axis, [(i, i ^ d) for i in range(n)]))
        d *= 2
    return x


def far_part(queries, keys_t, values, lo, hi, blk, qgw, blk_index, scale):
    tok_dev, q_cols = queries.shape
    heads = q_cols // HEAD_SIZE
    blocks, kv_cols, block_len = keys_t.shape
    gathered = lax.all_gather(queries, BLK, axis=0, tiled=True)
    row_count = gathered.shape[0]
    n_tiles = row_count // tok_dev
    stat_rows = 8
    q_spec = pl.BlockSpec((tok_dev, q_cols), lambda i, *_: (i, 0))
    kt_spec = pl.BlockSpec((blocks, kv_cols, block_len), lambda i, *_: (0, 0, 0))
    v_spec = pl.BlockSpec((blocks, block_len, kv_cols), lambda i, *_: (0, 0, 0))
    s_spec = pl.BlockSpec((stat_rows, tok_dev), lambda i, *_: (i, 0))
    stat_shape = jax.ShapeDtypeStruct((n_tiles * stat_rows, tok_dev), jnp.float32)
    kw = dict(heads=heads, qgw=qgw, scale=scale)
    local_max = pl.pallas_call(
        functools.partial(max_kernel, **kw),
        out_shape=stat_shape,
        grid_spec=pltpu.PrefetchScalarGridSpec(
            num_scalar_prefetch=3, grid=(n_tiles,), in_specs=[q_spec, kt_spec], out_specs=s_spec
        ),
    )(lo, hi, blk, gathered, keys_t)
    far_max = butterfly(local_max, BLK, jnp.maximum)
    partial, totals = pl.pallas_call(
        functools.partial(ctx_kernel, **kw),
        out_shape=(jax.ShapeDtypeStruct((row_count, q_cols), jnp.float32), stat_shape),
        grid_spec=pltpu.PrefetchScalarGridSpec(
            num_scalar_prefetch=3,
            grid=(n_tiles,),
            in_specs=[q_spec, kt_spec, v_spec, s_spec],
            out_specs=(pl.BlockSpec((tok_dev, q_cols), lambda i, *_: (i, 0)), s_spec),
        ),
    )(lo, hi, blk, gathered, keys_t, values, far_max)
    context = chip_then_core_sum(partial, tok_dev)
    totals = butterfly(totals, BLK, jnp.add)
    own = lambda a: jnp.transpose(
        lax.dynamic_slice_in_dim(a, blk_index * stat_rows, stat_rows, 0)[:heads]
    )
    return context, own(totals), own(far_max)


def column_sum(x, axis):
    n = lax.axis_size(axis)
    me = lax.axis_index(axis)
    width = x.shape[1] // n
    chunk = lambda k: lax.dynamic_slice_in_dim(x, (k % n) * width, width, 1)
    total = chunk(me)
    for d in range(1, n):
        total = total + lax.ppermute(chunk(me + d), axis, [(i, (i + d) % n) for i in range(n)])
    return total


def per_device(
    queries,
    suffix_key_rows,
    suffix_value_rows,
    prefix_block_keys,
    prefix_block_values,
    block_group,
    suffix_len,
    request_group,
    w_out,
):
    tok_dev = queries.shape[0]
    q_cols = queries.shape[1]
    kv_cols = suffix_key_rows.shape[1]
    local_kv = kv_cols // HEAD_SIZE
    local_heads = q_cols // HEAD_SIZE
    qgw = local_heads // local_kv
    blocks, block_len, _ = prefix_block_keys.shape
    blk_count = blk_size()
    row_count = blk_count * tok_dev
    blk_index = blk_position()
    scale = 1.0 / math.sqrt(HEAD_SIZE)
    tile = tok_dev
    n_tiles = row_count // tile

    lo, hi, blk = tile_tables(suffix_len, request_group, block_group, n_tiles, tile)
    keys_t = jnp.swapaxes(prefix_block_keys, 1, 2)
    far_context, far_total, own_far_max = far_part(
        queries, keys_t, prefix_block_values, lo, hi, blk, qgw, blk_index, scale
    )
    far_context = far_context.reshape(tok_dev, local_kv, qgw, HEAD_SIZE)
    far_total = far_total.reshape(tok_dev, local_kv, qgw)
    own_far_max = own_far_max.reshape(tok_dev, local_kv, qgw)

    row_ends = jnp.cumsum(suffix_len)
    starts = row_ends - suffix_len
    own_rows = blk_index * tok_dev + jnp.arange(tok_dev, dtype=jnp.int32)
    earlier_keys, earlier_values = from_behind((suffix_key_rows, suffix_value_rows), BLK, 1)
    near_keys = jnp.concatenate([earlier_keys, suffix_key_rows], axis=0).reshape(
        2 * tok_dev, local_kv, HEAD_SIZE
    )
    near_values = jnp.concatenate([earlier_values, suffix_value_rows], axis=0).reshape(
        2 * tok_dev, local_kv, HEAD_SIZE
    )
    near_rows = (blk_index - 1) * tok_dev + jnp.arange(2 * tok_dev, dtype=jnp.int32)
    own_req = request_of(own_rows, starts, row_ends)
    near_req = request_of(near_rows, starts, row_ends)
    allowed = (
        (own_req[:, None] == near_req[None, :])
        & (near_rows[None, :] <= own_rows[:, None])
        & (near_rows[None, :] >= 0)
    )
    own_queries = queries.reshape(tok_dev, local_kv, qgw, HEAD_SIZE)
    near_scores = (
        jnp.einsum("sgjd,tgd->sgjt", own_queries, near_keys, preferred_element_type=jnp.float32)
        * scale
    )
    near_scores = jnp.where(allowed[:, None, None, :], near_scores, -jnp.inf)
    near_max = jnp.max(near_scores, axis=3)
    top = jnp.maximum(own_far_max, near_max)
    near_prob = jnp.exp(near_scores - top[..., None])
    near_total = jnp.sum(near_prob, axis=3)
    near_context = jnp.einsum(
        "sgjt,tgd->sgjd",
        near_prob.astype(jnp.bfloat16),
        near_values,
        preferred_element_type=jnp.float32,
    )
    far_scale = jnp.exp(own_far_max - top)
    context = far_context * far_scale[..., None] + near_context
    denominator = far_total * far_scale + near_total
    attention = (context / denominator[..., None]).reshape(tok_dev, q_cols).astype(jnp.bfloat16)
    projected = jnp.dot(attention, w_out, preferred_element_type=jnp.float32)
    return column_sum(projected, "kvh").astype(jnp.bfloat16)


def solution(mesh):
    devices = mesh.devices
    split = jax.sharding.Mesh(
        devices.reshape(devices.shape[0], devices.shape[1] // CORES, CORES), ("kvh",) + BLK
    )
    placed = (
        P(BLK, "kvh"),
        P(BLK, "kvh"),
        P(BLK, "kvh"),
        P(BLK, None, "kvh"),
        P(BLK, None, "kvh"),
        P(BLK),
        P(),
        P(),
        P("kvh", None),
    )
    return jax.shard_map(
        per_device, mesh=split, in_specs=placed, out_specs=P(BLK, "kvh"), check_vma=False
    )
```

```python
import functools
import math

import jax
import jax.numpy as jnp
from jax import lax
from jax.experimental import pallas as pl
from jax.experimental.pallas import tpu as pltpu
from jax.sharding import PartitionSpec as P

HEAD_SIZE = 128
SLOTS = 5
STAT_LANES = 128


def from_behind(block, axis, distance):
    devices = range(lax.axis_size(axis))
    route = [(i - distance, i) for i in devices if i - distance in devices]
    return lax.ppermute(block, axis, route)


def request_of(row_ids, starts, row_ends):
    inside = (row_ids[:, None] >= starts[None, :]) & (row_ids[:, None] < row_ends[None, :])
    req_ids = jnp.arange(starts.shape[0], dtype=jnp.int32)
    return jnp.sum(jnp.where(inside, req_ids[None, :], 0), axis=1)


def tile_tables(suffix_len, request_group, block_group, n_tiles, tile):
    row_ends = jnp.cumsum(suffix_len).astype(jnp.int32)
    starts = row_ends - suffix_len
    tile_lo = jnp.arange(n_tiles, dtype=jnp.int32) * tile
    first = jnp.sum((row_ends[None, :] <= tile_lo[:, None]).astype(jnp.int32), axis=1)
    last = jnp.sum((row_ends[None, :] <= (tile_lo + tile - 1)[:, None]).astype(jnp.int32), axis=1)
    req = first[:, None] + jnp.arange(SLOTS, dtype=jnp.int32)[None, :]
    valid = req <= last[:, None]
    req_v = jnp.minimum(req, last[:, None])
    lo = jnp.where(valid, starts[req_v], 0).astype(jnp.int32)
    hi = jnp.where(valid, row_ends[req_v], 0).astype(jnp.int32)
    group_count = suffix_len.shape[0] // 4
    blocks = block_group.shape[0]
    owns = block_group[None, :] == jnp.arange(group_count, dtype=jnp.int32)[:, None]
    block_of_group = jnp.sum(
        jnp.where(owns, jnp.arange(blocks, dtype=jnp.int32)[None, :], 0), axis=1
    ).astype(jnp.int32)
    blk = block_of_group[request_group[req_v]].astype(jnp.int32)
    return lo.reshape(-1), hi.reshape(-1), blk.reshape(-1)


def _slot_mask(lo_ref, hi_ref, base, rows):
    seg = lax.broadcasted_iota(jnp.int32, (1, SLOTS * HEAD_SIZE), 1) // HEAD_SIZE
    lo = jnp.zeros(seg.shape, jnp.int32)
    hi = jnp.zeros(seg.shape, jnp.int32)
    for s in range(SLOTS):
        lo = jnp.where(seg == s, lo_ref[base + s], lo)
        hi = jnp.where(seg == s, hi_ref[base + s], hi)
    return (rows >= lo) & (rows < hi)


def _slot_keys(kt_ref, blk_ref, base, kv):
    cols = slice(kv * HEAD_SIZE, (kv + 1) * HEAD_SIZE)
    return jnp.concatenate([kt_ref[blk_ref[base + s], cols, :] for s in range(SLOTS)], axis=1)


def _slot_values(v_ref, blk_ref, base, kv):
    cols = slice(kv * HEAD_SIZE, (kv + 1) * HEAD_SIZE)
    return jnp.concatenate([v_ref[blk_ref[base + s], :, cols] for s in range(SLOTS)], axis=0)


def max_kernel(lo_ref, hi_ref, blk_ref, q_ref, kt_ref, m_ref, *, heads, qgw, scale):
    i = pl.program_id(0)
    tile = q_ref.shape[0]
    base = i * SLOTS
    rows = i * tile + lax.broadcasted_iota(jnp.int32, (tile, 1), 0)
    mask = _slot_mask(lo_ref, hi_ref, base, rows)
    lane = lax.broadcasted_iota(jnp.int32, (1, STAT_LANES), 1)
    stats = jnp.full((tile, STAT_LANES), -jnp.inf, jnp.float32)
    for h in range(heads):
        if h % qgw == 0:
            keys = _slot_keys(kt_ref, blk_ref, base, h // qgw)
        q = q_ref[:, h * HEAD_SIZE : (h + 1) * HEAD_SIZE]
        sc = jnp.dot(q, keys, preferred_element_type=jnp.float32) * scale
        mx = jnp.max(jnp.where(mask, sc, -jnp.inf), axis=1, keepdims=True)
        stats = jnp.where(lane == h, mx, stats)
    m_ref[...] = jnp.transpose(stats)[: m_ref.shape[0], :]


def ctx_kernel(
    lo_ref, hi_ref, blk_ref, q_ref, kt_ref, v_ref, m_ref, o_ref, t_ref, *, heads, qgw, scale
):
    i = pl.program_id(0)
    tile = q_ref.shape[0]
    base = i * SLOTS
    rows = i * tile + lax.broadcasted_iota(jnp.int32, (tile, 1), 0)
    mask = _slot_mask(lo_ref, hi_ref, base, rows)
    lane = lax.broadcasted_iota(jnp.int32, (1, STAT_LANES), 1)
    totals = jnp.zeros((tile, STAT_LANES), jnp.float32)
    top = jnp.transpose(m_ref[...])
    for h in range(heads):
        if h % qgw == 0:
            keys = _slot_keys(kt_ref, blk_ref, base, h // qgw)
            values = _slot_values(v_ref, blk_ref, base, h // qgw)
        q = q_ref[:, h * HEAD_SIZE : (h + 1) * HEAD_SIZE]
        sc = jnp.dot(q, keys, preferred_element_type=jnp.float32) * scale
        p = jnp.exp(jnp.where(mask, sc - top[:, h : h + 1], -jnp.inf))
        ctx = jnp.dot(p.astype(jnp.bfloat16), values, preferred_element_type=jnp.float32)
        o_ref[:, h * HEAD_SIZE : (h + 1) * HEAD_SIZE] = ctx
        totals = jnp.where(lane == h, jnp.sum(p, axis=1, keepdims=True), totals)
    t_ref[...] = jnp.transpose(totals)[: t_ref.shape[0], :]


def butterfly(x, axis, combine):
    n = lax.axis_size(axis)
    stride = 1
    while stride < n:
        radix = 2 if stride == 1 or n % (stride * 4) else 4
        digit = lambda i: (i // stride) % radix
        got = [
            lax.ppermute(
                x,
                axis,
                [(i, i + ((digit(i) + d) % radix - digit(i)) * stride) for i in range(n)],
            )
            for d in range(1, radix)
        ]
        for g in got:
            x = combine(x, g)
        stride *= radix
    return x


def far_part(queries, keys_t, values, lo, hi, blk, qgw, blk_index, scale):
    tok_dev, q_cols = queries.shape
    heads = q_cols // HEAD_SIZE
    blocks, kv_cols, block_len = keys_t.shape
    gathered = lax.all_gather(queries, "blk", axis=0, tiled=True)
    row_count = gathered.shape[0]
    n_tiles = row_count // tok_dev
    stat_rows = 8
    q_spec = pl.BlockSpec((tok_dev, q_cols), lambda i, *_: (i, 0))
    kt_spec = pl.BlockSpec((blocks, kv_cols, block_len), lambda i, *_: (0, 0, 0))
    v_spec = pl.BlockSpec((blocks, block_len, kv_cols), lambda i, *_: (0, 0, 0))
    s_spec = pl.BlockSpec((stat_rows, tok_dev), lambda i, *_: (i, 0))
    stat_shape = jax.ShapeDtypeStruct((n_tiles * stat_rows, tok_dev), jnp.float32)
    kw = dict(heads=heads, qgw=qgw, scale=scale)
    local_max = pl.pallas_call(
        functools.partial(max_kernel, **kw),
        out_shape=stat_shape,
        grid_spec=pltpu.PrefetchScalarGridSpec(
            num_scalar_prefetch=3, grid=(n_tiles,), in_specs=[q_spec, kt_spec], out_specs=s_spec
        ),
    )(lo, hi, blk, gathered, keys_t)
    far_max = butterfly(local_max, "blk", jnp.maximum)
    partial, totals = pl.pallas_call(
        functools.partial(ctx_kernel, **kw),
        out_shape=(jax.ShapeDtypeStruct((row_count, q_cols), jnp.float32), stat_shape),
        grid_spec=pltpu.PrefetchScalarGridSpec(
            num_scalar_prefetch=3,
            grid=(n_tiles,),
            in_specs=[q_spec, kt_spec, v_spec, s_spec],
            out_specs=(pl.BlockSpec((tok_dev, q_cols), lambda i, *_: (i, 0)), s_spec),
        ),
    )(lo, hi, blk, gathered, keys_t, values, far_max)
    context = lax.psum_scatter(partial, "blk", scatter_dimension=0, tiled=True)
    totals = butterfly(totals, "blk", jnp.add)
    own = lambda a: jnp.transpose(
        lax.dynamic_slice_in_dim(a, blk_index * stat_rows, stat_rows, 0)[:heads]
    )
    return context, own(totals), own(far_max)


def column_sum(x, axis):
    n = lax.axis_size(axis)
    me = lax.axis_index(axis)
    width = x.shape[1] // n
    chunk = lambda k: lax.dynamic_slice_in_dim(x, (k % n) * width, width, 1)
    total = chunk(me)
    for d in range(1, n):
        sent = chunk(me + d).astype(jnp.bfloat16)
        got = lax.ppermute(sent, axis, [(i, (i + d) % n) for i in range(n)])
        total = total + got.astype(jnp.float32)
    return total


def per_device(
    queries,
    suffix_key_rows,
    suffix_value_rows,
    prefix_block_keys,
    prefix_block_values,
    block_group,
    suffix_len,
    request_group,
    w_out,
):
    tok_dev = queries.shape[0]
    q_cols = queries.shape[1]
    kv_cols = suffix_key_rows.shape[1]
    local_kv = kv_cols // HEAD_SIZE
    local_heads = q_cols // HEAD_SIZE
    qgw = local_heads // local_kv
    blocks, block_len, _ = prefix_block_keys.shape
    blk_count = lax.axis_size("blk")
    row_count = blk_count * tok_dev
    blk_index = lax.axis_index("blk")
    scale = 1.0 / math.sqrt(HEAD_SIZE)
    tile = tok_dev
    n_tiles = row_count // tile

    lo, hi, blk = tile_tables(suffix_len, request_group, block_group, n_tiles, tile)
    keys_t = jnp.swapaxes(prefix_block_keys, 1, 2)
    far_context, far_total, own_far_max = far_part(
        queries, keys_t, prefix_block_values, lo, hi, blk, qgw, blk_index, scale
    )
    far_context = far_context.reshape(tok_dev, local_kv, qgw, HEAD_SIZE)
    far_total = far_total.reshape(tok_dev, local_kv, qgw)
    own_far_max = own_far_max.reshape(tok_dev, local_kv, qgw)

    row_ends = jnp.cumsum(suffix_len)
    starts = row_ends - suffix_len
    own_rows = blk_index * tok_dev + jnp.arange(tok_dev, dtype=jnp.int32)
    earlier_keys, earlier_values = from_behind((suffix_key_rows, suffix_value_rows), "blk", 1)
    near_keys = jnp.concatenate([earlier_keys, suffix_key_rows], axis=0).reshape(
        2 * tok_dev, local_kv, HEAD_SIZE
    )
    near_values = jnp.concatenate([earlier_values, suffix_value_rows], axis=0).reshape(
        2 * tok_dev, local_kv, HEAD_SIZE
    )
    near_rows = (blk_index - 1) * tok_dev + jnp.arange(2 * tok_dev, dtype=jnp.int32)
    own_req = request_of(own_rows, starts, row_ends)
    near_req = request_of(near_rows, starts, row_ends)
    allowed = (
        (own_req[:, None] == near_req[None, :])
        & (near_rows[None, :] <= own_rows[:, None])
        & (near_rows[None, :] >= 0)
    )
    own_queries = queries.reshape(tok_dev, local_kv, qgw, HEAD_SIZE)
    near_scores = (
        jnp.einsum("sgjd,tgd->sgjt", own_queries, near_keys, preferred_element_type=jnp.float32)
        * scale
    )
    near_scores = jnp.where(allowed[:, None, None, :], near_scores, -jnp.inf)
    near_max = jnp.max(near_scores, axis=3)
    top = jnp.maximum(own_far_max, near_max)
    near_prob = jnp.exp(near_scores - top[..., None])
    near_total = jnp.sum(near_prob, axis=3)
    near_context = jnp.einsum(
        "sgjt,tgd->sgjd",
        near_prob.astype(jnp.bfloat16),
        near_values,
        preferred_element_type=jnp.float32,
    )
    far_scale = jnp.exp(own_far_max - top)
    context = far_context * far_scale[..., None] + near_context
    denominator = far_total * far_scale + near_total
    attention = (context / denominator[..., None]).reshape(tok_dev, q_cols).astype(jnp.bfloat16)
    projected = jnp.dot(attention, w_out, preferred_element_type=jnp.float32)
    return column_sum(projected, "kvh").astype(jnp.bfloat16)


def solution(mesh):
    placed = (
        P("blk", "kvh"),
        P("blk", "kvh"),
        P("blk", "kvh"),
        P("blk", None, "kvh"),
        P("blk", None, "kvh"),
        P("blk"),
        P(),
        P(),
        P("kvh", None),
    )
    return jax.shard_map(
        per_device, mesh=mesh, in_specs=placed, out_specs=P("blk", "kvh"), check_vma=False
    )
```

```python
import functools
import math

import jax
import jax.numpy as jnp
from jax import lax
from jax.experimental import pallas as pl
from jax.experimental.pallas import tpu as pltpu
from jax.sharding import PartitionSpec as P

HEAD_SIZE = 128
SLOTS = 5
STAT_LANES = 128


def from_behind(block, axis, distance):
    devices = range(lax.axis_size(axis))
    route = [(i - distance, i) for i in devices if i - distance in devices]
    return lax.ppermute(block, axis, route)


def request_of(row_ids, starts, row_ends):
    inside = (row_ids[:, None] >= starts[None, :]) & (row_ids[:, None] < row_ends[None, :])
    req_ids = jnp.arange(starts.shape[0], dtype=jnp.int32)
    return jnp.sum(jnp.where(inside, req_ids[None, :], 0), axis=1)


def tile_tables(suffix_len, request_group, block_group, n_tiles, tile):
    row_ends = jnp.cumsum(suffix_len).astype(jnp.int32)
    starts = row_ends - suffix_len
    tile_lo = jnp.arange(n_tiles, dtype=jnp.int32) * tile
    first = jnp.sum((row_ends[None, :] <= tile_lo[:, None]).astype(jnp.int32), axis=1)
    last = jnp.sum((row_ends[None, :] <= (tile_lo + tile - 1)[:, None]).astype(jnp.int32), axis=1)
    req = first[:, None] + jnp.arange(SLOTS, dtype=jnp.int32)[None, :]
    valid = req <= last[:, None]
    req_v = jnp.minimum(req, last[:, None])
    lo = jnp.where(valid, starts[req_v], 0).astype(jnp.int32)
    hi = jnp.where(valid, row_ends[req_v], 0).astype(jnp.int32)
    group_count = suffix_len.shape[0] // 4
    blocks = block_group.shape[0]
    owns = block_group[None, :] == jnp.arange(group_count, dtype=jnp.int32)[:, None]
    block_of_group = jnp.sum(
        jnp.where(owns, jnp.arange(blocks, dtype=jnp.int32)[None, :], 0), axis=1
    ).astype(jnp.int32)
    blk = block_of_group[request_group[req_v]].astype(jnp.int32)
    return lo.reshape(-1), hi.reshape(-1), blk.reshape(-1)


def _slot_mask(lo_ref, hi_ref, base, rows):
    seg = lax.broadcasted_iota(jnp.int32, (1, SLOTS * HEAD_SIZE), 1) // HEAD_SIZE
    lo = jnp.zeros(seg.shape, jnp.int32)
    hi = jnp.zeros(seg.shape, jnp.int32)
    for s in range(SLOTS):
        lo = jnp.where(seg == s, lo_ref[base + s], lo)
        hi = jnp.where(seg == s, hi_ref[base + s], hi)
    return (rows >= lo) & (rows < hi)


def _slot_keys(kt_ref, blk_ref, base, kv):
    cols = slice(kv * HEAD_SIZE, (kv + 1) * HEAD_SIZE)
    return jnp.concatenate([kt_ref[blk_ref[base + s], cols, :] for s in range(SLOTS)], axis=1)


def _slot_values(v_ref, blk_ref, base, kv):
    cols = slice(kv * HEAD_SIZE, (kv + 1) * HEAD_SIZE)
    return jnp.concatenate([v_ref[blk_ref[base + s], :, cols] for s in range(SLOTS)], axis=0)


def max_kernel(lo_ref, hi_ref, blk_ref, q_ref, kt_ref, m_ref, *, heads, qgw, scale):
    i = pl.program_id(0)
    tile = q_ref.shape[0]
    base = i * SLOTS
    rows = i * tile + lax.broadcasted_iota(jnp.int32, (tile, 1), 0)
    mask = _slot_mask(lo_ref, hi_ref, base, rows)
    lane = lax.broadcasted_iota(jnp.int32, (1, STAT_LANES), 1)
    stats = jnp.full((tile, STAT_LANES), -jnp.inf, jnp.float32)
    for h in range(heads):
        if h % qgw == 0:
            keys = _slot_keys(kt_ref, blk_ref, base, h // qgw)
        q = q_ref[:, h * HEAD_SIZE : (h + 1) * HEAD_SIZE]
        sc = jnp.dot(q, keys, preferred_element_type=jnp.float32)
        mx = jnp.max(jnp.where(mask, sc, -jnp.inf), axis=1, keepdims=True) * scale
        stats = jnp.where(lane == h, mx, stats)
    m_ref[...] = jnp.transpose(stats)[: m_ref.shape[0], :]


def ctx_kernel(
    lo_ref, hi_ref, blk_ref, q_ref, kt_ref, v_ref, m_ref, o_ref, t_ref, *, heads, qgw, scale
):
    i = pl.program_id(0)
    tile = q_ref.shape[0]
    base = i * SLOTS
    rows = i * tile + lax.broadcasted_iota(jnp.int32, (tile, 1), 0)
    mask = _slot_mask(lo_ref, hi_ref, base, rows)
    lane = lax.broadcasted_iota(jnp.int32, (1, STAT_LANES), 1)
    totals = jnp.zeros((tile, STAT_LANES), jnp.float32)
    ones = jnp.ones((SLOTS * HEAD_SIZE, STAT_LANES), jnp.bfloat16)
    top = jnp.transpose(m_ref[...])
    for h in range(heads):
        if h % qgw == 0:
            keys = _slot_keys(kt_ref, blk_ref, base, h // qgw)
            values = _slot_values(v_ref, blk_ref, base, h // qgw)
        q = q_ref[:, h * HEAD_SIZE : (h + 1) * HEAD_SIZE]
        sc = jnp.dot(q, keys, preferred_element_type=jnp.float32) * scale
        p = jnp.exp(jnp.where(mask, sc - top[:, h : h + 1], -jnp.inf))
        weights = p.astype(jnp.bfloat16)
        ctx = jnp.dot(weights, values, preferred_element_type=jnp.float32)
        o_ref[:, h * HEAD_SIZE : (h + 1) * HEAD_SIZE] = ctx
        row_sum = jnp.dot(weights, ones, preferred_element_type=jnp.float32)
        totals = jnp.where(lane == h, row_sum, totals)
    t_ref[...] = jnp.transpose(totals)[: t_ref.shape[0], :]


def butterfly(x, axis, combine):
    n = lax.axis_size(axis)
    stride = 1
    while stride < n:
        radix = 2 if stride == 1 or n % (stride * 4) else 4
        digit = lambda i: (i // stride) % radix
        got = [
            lax.ppermute(
                x,
                axis,
                [(i, i + ((digit(i) + d) % radix - digit(i)) * stride) for i in range(n)],
            )
            for d in range(1, radix)
        ]
        for g in got:
            x = combine(x, g)
        stride *= radix
    return x


def far_part(queries, keys_t, values, lo, hi, blk, qgw, blk_index, scale):
    tok_dev, q_cols = queries.shape
    heads = q_cols // HEAD_SIZE
    blocks, kv_cols, block_len = keys_t.shape
    gathered = lax.all_gather(queries, "blk", axis=0, tiled=True)
    row_count = gathered.shape[0]
    n_tiles = row_count // tok_dev
    stat_rows = 8
    q_spec = pl.BlockSpec((tok_dev, q_cols), lambda i, *_: (i, 0))
    kt_spec = pl.BlockSpec((blocks, kv_cols, block_len), lambda i, *_: (0, 0, 0))
    v_spec = pl.BlockSpec((blocks, block_len, kv_cols), lambda i, *_: (0, 0, 0))
    s_spec = pl.BlockSpec((stat_rows, tok_dev), lambda i, *_: (i, 0))
    stat_shape = jax.ShapeDtypeStruct((n_tiles * stat_rows, tok_dev), jnp.float32)
    kw = dict(heads=heads, qgw=qgw, scale=scale)
    local_max = pl.pallas_call(
        functools.partial(max_kernel, **kw),
        out_shape=stat_shape,
        grid_spec=pltpu.PrefetchScalarGridSpec(
            num_scalar_prefetch=3, grid=(n_tiles,), in_specs=[q_spec, kt_spec], out_specs=s_spec
        ),
    )(lo, hi, blk, gathered, keys_t)
    far_max = butterfly(local_max, "blk", jnp.maximum)
    partial, totals = pl.pallas_call(
        functools.partial(ctx_kernel, **kw),
        out_shape=(jax.ShapeDtypeStruct((row_count, q_cols), jnp.float32), stat_shape),
        grid_spec=pltpu.PrefetchScalarGridSpec(
            num_scalar_prefetch=3,
            grid=(n_tiles,),
            in_specs=[q_spec, kt_spec, v_spec, s_spec],
            out_specs=(pl.BlockSpec((tok_dev, q_cols), lambda i, *_: (i, 0)), s_spec),
        ),
    )(lo, hi, blk, gathered, keys_t, values, far_max)
    context = lax.psum_scatter(partial, "blk", scatter_dimension=0, tiled=True)
    totals = butterfly(totals, "blk", jnp.add)
    own = lambda a: jnp.transpose(
        lax.dynamic_slice_in_dim(a, blk_index * stat_rows, stat_rows, 0)[:heads]
    )
    return context, own(totals), own(far_max)


def column_sum(x, axis):
    n = lax.axis_size(axis)
    me = lax.axis_index(axis)
    width = x.shape[1] // n
    chunk = lambda k: lax.dynamic_slice_in_dim(x, (k % n) * width, width, 1)
    total = chunk(me)
    for d in range(1, n):
        sent = chunk(me + d).astype(jnp.bfloat16)
        got = lax.ppermute(sent, axis, [(i, (i + d) % n) for i in range(n)])
        total = total + got.astype(jnp.float32)
    return total


def per_device(
    queries,
    suffix_key_rows,
    suffix_value_rows,
    prefix_block_keys,
    prefix_block_values,
    block_group,
    suffix_len,
    request_group,
    w_out,
):
    tok_dev = queries.shape[0]
    q_cols = queries.shape[1]
    kv_cols = suffix_key_rows.shape[1]
    local_kv = kv_cols // HEAD_SIZE
    local_heads = q_cols // HEAD_SIZE
    qgw = local_heads // local_kv
    blocks, block_len, _ = prefix_block_keys.shape
    blk_count = lax.axis_size("blk")
    row_count = blk_count * tok_dev
    blk_index = lax.axis_index("blk")
    scale = 1.0 / math.sqrt(HEAD_SIZE)
    tile = tok_dev
    n_tiles = row_count // tile

    lo, hi, blk = tile_tables(suffix_len, request_group, block_group, n_tiles, tile)
    keys_t = jnp.swapaxes(prefix_block_keys, 1, 2)
    far_context, far_total, own_far_max = far_part(
        queries, keys_t, prefix_block_values, lo, hi, blk, qgw, blk_index, scale
    )
    far_context = far_context.reshape(tok_dev, local_kv, qgw, HEAD_SIZE)
    far_total = far_total.reshape(tok_dev, local_kv, qgw)
    own_far_max = own_far_max.reshape(tok_dev, local_kv, qgw)

    row_ends = jnp.cumsum(suffix_len)
    starts = row_ends - suffix_len
    own_rows = blk_index * tok_dev + jnp.arange(tok_dev, dtype=jnp.int32)
    earlier_keys, earlier_values = from_behind((suffix_key_rows, suffix_value_rows), "blk", 1)
    near_keys = jnp.concatenate([earlier_keys, suffix_key_rows], axis=0).reshape(
        2 * tok_dev, local_kv, HEAD_SIZE
    )
    near_values = jnp.concatenate([earlier_values, suffix_value_rows], axis=0).reshape(
        2 * tok_dev, local_kv, HEAD_SIZE
    )
    near_rows = (blk_index - 1) * tok_dev + jnp.arange(2 * tok_dev, dtype=jnp.int32)
    own_req = request_of(own_rows, starts, row_ends)
    near_req = request_of(near_rows, starts, row_ends)
    allowed = (
        (own_req[:, None] == near_req[None, :])
        & (near_rows[None, :] <= own_rows[:, None])
        & (near_rows[None, :] >= 0)
    )
    own_queries = queries.reshape(tok_dev, local_kv, qgw, HEAD_SIZE)
    near_scores = (
        jnp.einsum("sgjd,tgd->sgjt", own_queries, near_keys, preferred_element_type=jnp.float32)
        * scale
    )
    near_scores = jnp.where(allowed[:, None, None, :], near_scores, -jnp.inf)
    near_max = jnp.max(near_scores, axis=3)
    top = jnp.maximum(own_far_max, near_max)
    near_prob = jnp.exp(near_scores - top[..., None])
    near_total = jnp.sum(near_prob, axis=3)
    near_context = jnp.einsum(
        "sgjt,tgd->sgjd",
        near_prob.astype(jnp.bfloat16),
        near_values,
        preferred_element_type=jnp.float32,
    )
    far_scale = jnp.exp(own_far_max - top)
    context = far_context * far_scale[..., None] + near_context
    denominator = far_total * far_scale + near_total
    attention = (context / denominator[..., None]).reshape(tok_dev, q_cols).astype(jnp.bfloat16)
    projected = jnp.dot(attention, w_out, preferred_element_type=jnp.float32)
    return column_sum(projected, "kvh").astype(jnp.bfloat16)


def solution(mesh):
    placed = (
        P("blk", "kvh"),
        P("blk", "kvh"),
        P("blk", "kvh"),
        P("blk", None, "kvh"),
        P("blk", None, "kvh"),
        P("blk"),
        P(),
        P(),
        P("kvh", None),
    )
    return jax.shard_map(
        per_device, mesh=mesh, in_specs=placed, out_specs=P("blk", "kvh"), check_vma=False
    )
```

```python
import functools
import math

import jax
import jax.numpy as jnp
from jax import lax
from jax.experimental import pallas as pl
from jax.experimental.pallas import tpu as pltpu
from jax.sharding import PartitionSpec as P

HEAD_SIZE = 128
SLOTS = 5
STAT_LANES = 128


def from_behind(block, axis, distance):
    devices = range(lax.axis_size(axis))
    route = [(i - distance, i) for i in devices if i - distance in devices]
    return lax.ppermute(block, axis, route)


def request_of(row_ids, starts, row_ends):
    inside = (row_ids[:, None] >= starts[None, :]) & (row_ids[:, None] < row_ends[None, :])
    req_ids = jnp.arange(starts.shape[0], dtype=jnp.int32)
    return jnp.sum(jnp.where(inside, req_ids[None, :], 0), axis=1)


def tile_tables(suffix_len, request_group, block_group, n_tiles, tile):
    row_ends = jnp.cumsum(suffix_len).astype(jnp.int32)
    starts = row_ends - suffix_len
    tile_lo = jnp.arange(n_tiles, dtype=jnp.int32) * tile
    first = jnp.sum((row_ends[None, :] <= tile_lo[:, None]).astype(jnp.int32), axis=1)
    last = jnp.sum((row_ends[None, :] <= (tile_lo + tile - 1)[:, None]).astype(jnp.int32), axis=1)
    req = first[:, None] + jnp.arange(SLOTS, dtype=jnp.int32)[None, :]
    valid = req <= last[:, None]
    req_v = jnp.minimum(req, last[:, None])
    lo = jnp.where(valid, starts[req_v], 0).astype(jnp.int32)
    hi = jnp.where(valid, row_ends[req_v], 0).astype(jnp.int32)
    group_count = suffix_len.shape[0] // 4
    blocks = block_group.shape[0]
    owns = block_group[None, :] == jnp.arange(group_count, dtype=jnp.int32)[:, None]
    block_of_group = jnp.sum(
        jnp.where(owns, jnp.arange(blocks, dtype=jnp.int32)[None, :], 0), axis=1
    ).astype(jnp.int32)
    blk = block_of_group[request_group[req_v]].astype(jnp.int32)
    return lo.reshape(-1), hi.reshape(-1), blk.reshape(-1)


def _slot_mask(lo_ref, hi_ref, base, rows):
    seg = lax.broadcasted_iota(jnp.int32, (1, SLOTS * HEAD_SIZE), 1) // HEAD_SIZE
    lo = jnp.zeros(seg.shape, jnp.int32)
    hi = jnp.zeros(seg.shape, jnp.int32)
    for s in range(SLOTS):
        lo = jnp.where(seg == s, lo_ref[base + s], lo)
        hi = jnp.where(seg == s, hi_ref[base + s], hi)
    return (rows >= lo) & (rows < hi)


def _slot_keys(kt_ref, blk_ref, base, kv):
    cols = slice(kv * HEAD_SIZE, (kv + 1) * HEAD_SIZE)
    return jnp.concatenate([kt_ref[blk_ref[base + s], cols, :] for s in range(SLOTS)], axis=1)


def _slot_values(v_ref, blk_ref, base, kv):
    cols = slice(kv * HEAD_SIZE, (kv + 1) * HEAD_SIZE)
    return jnp.concatenate([v_ref[blk_ref[base + s], :, cols] for s in range(SLOTS)], axis=0)


def _stacked(q_ref, kv, qgw):
    return jnp.concatenate(
        [q_ref[:, h * HEAD_SIZE : (h + 1) * HEAD_SIZE] for h in range(kv * qgw, (kv + 1) * qgw)],
        axis=0,
    )


def max_kernel(lo_ref, hi_ref, blk_ref, q_ref, kt_ref, m_ref, *, heads, qgw, scale):
    i = pl.program_id(0)
    tile = q_ref.shape[0]
    base = i * SLOTS
    rows = i * tile + lax.broadcasted_iota(jnp.int32, (qgw * tile, 1), 0) % tile
    mask = _slot_mask(lo_ref, hi_ref, base, rows)
    lane = lax.broadcasted_iota(jnp.int32, (1, STAT_LANES), 1)
    stats = jnp.full((tile, STAT_LANES), -jnp.inf, jnp.float32)
    for kv in range(heads // qgw):
        keys = _slot_keys(kt_ref, blk_ref, base, kv)
        sc = jnp.dot(_stacked(q_ref, kv, qgw), keys, preferred_element_type=jnp.float32) * scale
        mx = jnp.max(jnp.where(mask, sc, -jnp.inf), axis=1, keepdims=True)
        for j in range(qgw):
            stats = jnp.where(lane == kv * qgw + j, mx[j * tile : (j + 1) * tile], stats)
    m_ref[...] = jnp.transpose(stats)[: m_ref.shape[0], :]


def ctx_kernel(
    lo_ref, hi_ref, blk_ref, q_ref, kt_ref, v_ref, m_ref, o_ref, t_ref, *, heads, qgw, scale
):
    i = pl.program_id(0)
    tile = q_ref.shape[0]
    base = i * SLOTS
    rows = i * tile + lax.broadcasted_iota(jnp.int32, (qgw * tile, 1), 0) % tile
    mask = _slot_mask(lo_ref, hi_ref, base, rows)
    lane = lax.broadcasted_iota(jnp.int32, (1, STAT_LANES), 1)
    totals = jnp.zeros((tile, STAT_LANES), jnp.float32)
    tops = jnp.transpose(m_ref[...])
    for kv in range(heads // qgw):
        group = range(kv * qgw, (kv + 1) * qgw)
        keys = _slot_keys(kt_ref, blk_ref, base, kv)
        values = _slot_values(v_ref, blk_ref, base, kv)
        sc = jnp.dot(_stacked(q_ref, kv, qgw), keys, preferred_element_type=jnp.float32) * scale
        top = jnp.concatenate([tops[:, h : h + 1] for h in group], axis=0)
        p = jnp.exp(jnp.where(mask, sc - top, -jnp.inf))
        ctx = jnp.dot(p.astype(jnp.bfloat16), values, preferred_element_type=jnp.float32)
        tot = jnp.sum(p, axis=1, keepdims=True)
        for j, h in enumerate(group):
            o_ref[:, h * HEAD_SIZE : (h + 1) * HEAD_SIZE] = ctx[j * tile : (j + 1) * tile]
            totals = jnp.where(lane == h, tot[j * tile : (j + 1) * tile], totals)
    t_ref[...] = jnp.transpose(totals)[: t_ref.shape[0], :]


def butterfly(x, axis, combine):
    n = lax.axis_size(axis)
    stride = 1
    while stride < n:
        radix = 2 if stride == 1 or n % (stride * 4) else 4
        digit = lambda i: (i // stride) % radix
        got = [
            lax.ppermute(
                x,
                axis,
                [(i, i + ((digit(i) + d) % radix - digit(i)) * stride) for i in range(n)],
            )
            for d in range(1, radix)
        ]
        for g in got:
            x = combine(x, g)
        stride *= radix
    return x


def far_part(queries, keys_t, values, lo, hi, blk, qgw, blk_index, scale):
    tok_dev, q_cols = queries.shape
    heads = q_cols // HEAD_SIZE
    blocks, kv_cols, block_len = keys_t.shape
    gathered = lax.all_gather(queries, "blk", axis=0, tiled=True)
    row_count = gathered.shape[0]
    n_tiles = row_count // tok_dev
    stat_rows = 8
    q_spec = pl.BlockSpec((tok_dev, q_cols), lambda i, *_: (i, 0))
    kt_spec = pl.BlockSpec((blocks, kv_cols, block_len), lambda i, *_: (0, 0, 0))
    v_spec = pl.BlockSpec((blocks, block_len, kv_cols), lambda i, *_: (0, 0, 0))
    s_spec = pl.BlockSpec((stat_rows, tok_dev), lambda i, *_: (i, 0))
    stat_shape = jax.ShapeDtypeStruct((n_tiles * stat_rows, tok_dev), jnp.float32)
    kw = dict(heads=heads, qgw=qgw, scale=scale)
    local_max = pl.pallas_call(
        functools.partial(max_kernel, **kw),
        out_shape=stat_shape,
        grid_spec=pltpu.PrefetchScalarGridSpec(
            num_scalar_prefetch=3, grid=(n_tiles,), in_specs=[q_spec, kt_spec], out_specs=s_spec
        ),
    )(lo, hi, blk, gathered, keys_t)
    far_max = butterfly(local_max, "blk", jnp.maximum)
    partial, totals = pl.pallas_call(
        functools.partial(ctx_kernel, **kw),
        out_shape=(jax.ShapeDtypeStruct((row_count, q_cols), jnp.float32), stat_shape),
        grid_spec=pltpu.PrefetchScalarGridSpec(
            num_scalar_prefetch=3,
            grid=(n_tiles,),
            in_specs=[q_spec, kt_spec, v_spec, s_spec],
            out_specs=(pl.BlockSpec((tok_dev, q_cols), lambda i, *_: (i, 0)), s_spec),
        ),
    )(lo, hi, blk, gathered, keys_t, values, far_max)
    context = lax.psum_scatter(partial, "blk", scatter_dimension=0, tiled=True)
    totals = butterfly(totals, "blk", jnp.add)
    own = lambda a: jnp.transpose(
        lax.dynamic_slice_in_dim(a, blk_index * stat_rows, stat_rows, 0)[:heads]
    )
    return context, own(totals), own(far_max)


def column_sum(x, axis):
    n = lax.axis_size(axis)
    me = lax.axis_index(axis)
    width = x.shape[1] // n
    chunk = lambda k: lax.dynamic_slice_in_dim(x, (k % n) * width, width, 1)
    total = chunk(me)
    for d in range(1, n):
        sent = chunk(me + d).astype(jnp.bfloat16)
        got = lax.ppermute(sent, axis, [(i, (i + d) % n) for i in range(n)])
        total = total + got.astype(jnp.float32)
    return total


def per_device(
    queries,
    suffix_key_rows,
    suffix_value_rows,
    prefix_block_keys,
    prefix_block_values,
    block_group,
    suffix_len,
    request_group,
    w_out,
):
    tok_dev = queries.shape[0]
    q_cols = queries.shape[1]
    kv_cols = suffix_key_rows.shape[1]
    local_kv = kv_cols // HEAD_SIZE
    local_heads = q_cols // HEAD_SIZE
    qgw = local_heads // local_kv
    blocks, block_len, _ = prefix_block_keys.shape
    blk_count = lax.axis_size("blk")
    row_count = blk_count * tok_dev
    blk_index = lax.axis_index("blk")
    scale = 1.0 / math.sqrt(HEAD_SIZE)
    tile = tok_dev
    n_tiles = row_count // tile

    lo, hi, blk = tile_tables(suffix_len, request_group, block_group, n_tiles, tile)
    keys_t = jnp.swapaxes(prefix_block_keys, 1, 2)
    far_context, far_total, own_far_max = far_part(
        queries, keys_t, prefix_block_values, lo, hi, blk, qgw, blk_index, scale
    )
    far_context = far_context.reshape(tok_dev, local_kv, qgw, HEAD_SIZE)
    far_total = far_total.reshape(tok_dev, local_kv, qgw)
    own_far_max = own_far_max.reshape(tok_dev, local_kv, qgw)

    row_ends = jnp.cumsum(suffix_len)
    starts = row_ends - suffix_len
    own_rows = blk_index * tok_dev + jnp.arange(tok_dev, dtype=jnp.int32)
    earlier_keys, earlier_values = from_behind((suffix_key_rows, suffix_value_rows), "blk", 1)
    near_keys = jnp.concatenate([earlier_keys, suffix_key_rows], axis=0).reshape(
        2 * tok_dev, local_kv, HEAD_SIZE
    )
    near_values = jnp.concatenate([earlier_values, suffix_value_rows], axis=0).reshape(
        2 * tok_dev, local_kv, HEAD_SIZE
    )
    near_rows = (blk_index - 1) * tok_dev + jnp.arange(2 * tok_dev, dtype=jnp.int32)
    own_req = request_of(own_rows, starts, row_ends)
    near_req = request_of(near_rows, starts, row_ends)
    allowed = (
        (own_req[:, None] == near_req[None, :])
        & (near_rows[None, :] <= own_rows[:, None])
        & (near_rows[None, :] >= 0)
    )
    own_queries = queries.reshape(tok_dev, local_kv, qgw, HEAD_SIZE)
    near_scores = (
        jnp.einsum("sgjd,tgd->sgjt", own_queries, near_keys, preferred_element_type=jnp.float32)
        * scale
    )
    near_scores = jnp.where(allowed[:, None, None, :], near_scores, -jnp.inf)
    near_max = jnp.max(near_scores, axis=3)
    top = jnp.maximum(own_far_max, near_max)
    near_prob = jnp.exp(near_scores - top[..., None])
    near_total = jnp.sum(near_prob, axis=3)
    near_context = jnp.einsum(
        "sgjt,tgd->sgjd",
        near_prob.astype(jnp.bfloat16),
        near_values,
        preferred_element_type=jnp.float32,
    )
    far_scale = jnp.exp(own_far_max - top)
    context = far_context * far_scale[..., None] + near_context
    denominator = far_total * far_scale + near_total
    attention = (context / denominator[..., None]).reshape(tok_dev, q_cols).astype(jnp.bfloat16)
    projected = jnp.dot(attention, w_out, preferred_element_type=jnp.float32)
    return column_sum(projected, "kvh").astype(jnp.bfloat16)


def solution(mesh):
    placed = (
        P("blk", "kvh"),
        P("blk", "kvh"),
        P("blk", "kvh"),
        P("blk", None, "kvh"),
        P("blk", None, "kvh"),
        P("blk"),
        P(),
        P(),
        P("kvh", None),
    )
    return jax.shard_map(
        per_device, mesh=mesh, in_specs=placed, out_specs=P("blk", "kvh"), check_vma=False
    )
```

```python
import functools
import math

import jax
import jax.numpy as jnp
from jax import lax
from jax.experimental import pallas as pl
from jax.experimental.pallas import tpu as pltpu
from jax.sharding import PartitionSpec as P

HEAD_SIZE = 128
TILE = 64
MIN_LEN = 32
SLOTS = TILE // MIN_LEN + 1
STAT_LANES = 128


def from_behind(block, axis, distance):
    devices = range(lax.axis_size(axis))
    route = [(i - distance, i) for i in devices if i - distance in devices]
    return lax.ppermute(block, axis, route)


def request_of(row_ids, starts, row_ends):
    inside = (row_ids[:, None] >= starts[None, :]) & (row_ids[:, None] < row_ends[None, :])
    req_ids = jnp.arange(starts.shape[0], dtype=jnp.int32)
    return jnp.sum(jnp.where(inside, req_ids[None, :], 0), axis=1)


def tile_tables(suffix_len, request_group, block_group, n_tiles, tile):
    row_ends = jnp.cumsum(suffix_len).astype(jnp.int32)
    starts = row_ends - suffix_len
    tile_lo = jnp.arange(n_tiles, dtype=jnp.int32) * tile
    first = jnp.sum((row_ends[None, :] <= tile_lo[:, None]).astype(jnp.int32), axis=1)
    last = jnp.sum((row_ends[None, :] <= (tile_lo + tile - 1)[:, None]).astype(jnp.int32), axis=1)
    req = first[:, None] + jnp.arange(SLOTS, dtype=jnp.int32)[None, :]
    valid = req <= last[:, None]
    req_v = jnp.minimum(req, last[:, None])
    lo = jnp.where(valid, starts[req_v], 0).astype(jnp.int32)
    hi = jnp.where(valid, row_ends[req_v], 0).astype(jnp.int32)
    group_count = suffix_len.shape[0] // 4
    blocks = block_group.shape[0]
    owns = block_group[None, :] == jnp.arange(group_count, dtype=jnp.int32)[:, None]
    block_of_group = jnp.sum(
        jnp.where(owns, jnp.arange(blocks, dtype=jnp.int32)[None, :], 0), axis=1
    ).astype(jnp.int32)
    blk = block_of_group[request_group[req_v]].astype(jnp.int32)
    return lo.reshape(-1), hi.reshape(-1), blk.reshape(-1)


def _slot_mask(lo_ref, hi_ref, base, rows):
    seg = lax.broadcasted_iota(jnp.int32, (1, SLOTS * HEAD_SIZE), 1) // HEAD_SIZE
    lo = jnp.zeros(seg.shape, jnp.int32)
    hi = jnp.zeros(seg.shape, jnp.int32)
    for s in range(SLOTS):
        lo = jnp.where(seg == s, lo_ref[base + s], lo)
        hi = jnp.where(seg == s, hi_ref[base + s], hi)
    return (rows >= lo) & (rows < hi)


def _slot_keys(kt_ref, blk_ref, base, kv):
    cols = slice(kv * HEAD_SIZE, (kv + 1) * HEAD_SIZE)
    return jnp.concatenate([kt_ref[blk_ref[base + s], cols, :] for s in range(SLOTS)], axis=1)


def _slot_values(v_ref, blk_ref, base, kv):
    cols = slice(kv * HEAD_SIZE, (kv + 1) * HEAD_SIZE)
    return jnp.concatenate([v_ref[blk_ref[base + s], :, cols] for s in range(SLOTS)], axis=0)


def _stacked(q_ref, kv, qgw):
    return jnp.concatenate(
        [q_ref[:, h * HEAD_SIZE : (h + 1) * HEAD_SIZE] for h in range(kv * qgw, (kv + 1) * qgw)],
        axis=0,
    )


def max_kernel(lo_ref, hi_ref, blk_ref, q_ref, kt_ref, m_ref, *, heads, qgw, scale):
    i = pl.program_id(0)
    tile = q_ref.shape[0]
    base = i * SLOTS
    rows = i * tile + lax.broadcasted_iota(jnp.int32, (qgw * tile, 1), 0) % tile
    mask = _slot_mask(lo_ref, hi_ref, base, rows)
    lane = lax.broadcasted_iota(jnp.int32, (1, STAT_LANES), 1)
    stats = jnp.full((tile, STAT_LANES), -jnp.inf, jnp.float32)
    for kv in range(heads // qgw):
        keys = _slot_keys(kt_ref, blk_ref, base, kv)
        sc = jnp.dot(_stacked(q_ref, kv, qgw), keys, preferred_element_type=jnp.float32) * scale
        mx = jnp.max(jnp.where(mask, sc, -jnp.inf), axis=1, keepdims=True)
        for j in range(qgw):
            stats = jnp.where(lane == kv * qgw + j, mx[j * tile : (j + 1) * tile], stats)
    m_ref[...] = jnp.transpose(stats)[: m_ref.shape[0], :]


def ctx_kernel(
    lo_ref, hi_ref, blk_ref, q_ref, kt_ref, v_ref, m_ref, o_ref, t_ref, *, heads, qgw, scale
):
    i = pl.program_id(0)
    tile = q_ref.shape[0]
    base = i * SLOTS
    rows = i * tile + lax.broadcasted_iota(jnp.int32, (qgw * tile, 1), 0) % tile
    mask = _slot_mask(lo_ref, hi_ref, base, rows)
    lane = lax.broadcasted_iota(jnp.int32, (1, STAT_LANES), 1)
    totals = jnp.zeros((tile, STAT_LANES), jnp.float32)
    tops = jnp.transpose(m_ref[...])
    for kv in range(heads // qgw):
        group = range(kv * qgw, (kv + 1) * qgw)
        keys = _slot_keys(kt_ref, blk_ref, base, kv)
        values = _slot_values(v_ref, blk_ref, base, kv)
        sc = jnp.dot(_stacked(q_ref, kv, qgw), keys, preferred_element_type=jnp.float32) * scale
        top = jnp.concatenate([tops[:, h : h + 1] for h in group], axis=0)
        p = jnp.exp(jnp.where(mask, sc - top, -jnp.inf))
        ctx = jnp.dot(p.astype(jnp.bfloat16), values, preferred_element_type=jnp.float32)
        tot = jnp.sum(p, axis=1, keepdims=True)
        for j, h in enumerate(group):
            o_ref[:, h * HEAD_SIZE : (h + 1) * HEAD_SIZE] = ctx[j * tile : (j + 1) * tile]
            totals = jnp.where(lane == h, tot[j * tile : (j + 1) * tile], totals)
    t_ref[...] = jnp.transpose(totals)[: t_ref.shape[0], :]


def butterfly(x, axis, combine):
    n = lax.axis_size(axis)
    stride = 1
    while stride < n:
        radix = 2 if stride == 1 or n % (stride * 4) else 4
        digit = lambda i: (i // stride) % radix
        got = [
            lax.ppermute(
                x,
                axis,
                [(i, i + ((digit(i) + d) % radix - digit(i)) * stride) for i in range(n)],
            )
            for d in range(1, radix)
        ]
        for g in got:
            x = combine(x, g)
        stride *= radix
    return x


def far_part(queries, keys_t, values, lo, hi, blk, qgw, blk_index, scale):
    tok_dev, q_cols = queries.shape
    heads = q_cols // HEAD_SIZE
    blocks, kv_cols, block_len = keys_t.shape
    gathered = lax.all_gather(queries, "blk", axis=0, tiled=True)
    row_count = gathered.shape[0]
    tile = TILE
    n_tiles = row_count // tile
    stat_rows = 8
    q_spec = pl.BlockSpec((tile, q_cols), lambda i, *_: (i, 0))
    kt_spec = pl.BlockSpec((blocks, kv_cols, block_len), lambda i, *_: (0, 0, 0))
    v_spec = pl.BlockSpec((blocks, block_len, kv_cols), lambda i, *_: (0, 0, 0))
    s_spec = pl.BlockSpec((stat_rows, tile), lambda i, *_: (i, 0))
    stat_shape = jax.ShapeDtypeStruct((n_tiles * stat_rows, tile), jnp.float32)
    kw = dict(heads=heads, qgw=qgw, scale=scale)
    local_max = pl.pallas_call(
        functools.partial(max_kernel, **kw),
        out_shape=stat_shape,
        grid_spec=pltpu.PrefetchScalarGridSpec(
            num_scalar_prefetch=3, grid=(n_tiles,), in_specs=[q_spec, kt_spec], out_specs=s_spec
        ),
    )(lo, hi, blk, gathered, keys_t)
    far_max = butterfly(local_max, "blk", jnp.maximum)
    partial, totals = pl.pallas_call(
        functools.partial(ctx_kernel, **kw),
        out_shape=(jax.ShapeDtypeStruct((row_count, q_cols), jnp.float32), stat_shape),
        grid_spec=pltpu.PrefetchScalarGridSpec(
            num_scalar_prefetch=3,
            grid=(n_tiles,),
            in_specs=[q_spec, kt_spec, v_spec, s_spec],
            out_specs=(pl.BlockSpec((tile, q_cols), lambda i, *_: (i, 0)), s_spec),
        ),
    )(lo, hi, blk, gathered, keys_t, values, far_max)
    context = lax.psum_scatter(partial, "blk", scatter_dimension=0, tiled=True)
    totals = butterfly(totals, "blk", jnp.add)
    per_dev = tok_dev // tile

    def own(a):
        mine = lax.dynamic_slice_in_dim(a, blk_index * per_dev * stat_rows, per_dev * stat_rows, 0)
        mine = mine.reshape(per_dev, stat_rows, tile)[:, :heads]
        return jnp.transpose(mine, (0, 2, 1)).reshape(tok_dev, heads)

    return context, own(totals), own(far_max)


def column_sum(x, axis):
    n = lax.axis_size(axis)
    me = lax.axis_index(axis)
    width = x.shape[1] // n
    chunk = lambda k: lax.dynamic_slice_in_dim(x, (k % n) * width, width, 1)
    total = chunk(me)
    for d in range(1, n):
        sent = chunk(me + d).astype(jnp.bfloat16)
        got = lax.ppermute(sent, axis, [(i, (i + d) % n) for i in range(n)])
        total = total + got.astype(jnp.float32)
    return total


def per_device(
    queries,
    suffix_key_rows,
    suffix_value_rows,
    prefix_block_keys,
    prefix_block_values,
    block_group,
    suffix_len,
    request_group,
    w_out,
):
    tok_dev = queries.shape[0]
    q_cols = queries.shape[1]
    kv_cols = suffix_key_rows.shape[1]
    local_kv = kv_cols // HEAD_SIZE
    local_heads = q_cols // HEAD_SIZE
    qgw = local_heads // local_kv
    blocks, block_len, _ = prefix_block_keys.shape
    blk_count = lax.axis_size("blk")
    row_count = blk_count * tok_dev
    blk_index = lax.axis_index("blk")
    scale = 1.0 / math.sqrt(HEAD_SIZE)
    tile = TILE
    n_tiles = row_count // tile

    lo, hi, blk = tile_tables(suffix_len, request_group, block_group, n_tiles, tile)
    keys_t = jnp.swapaxes(prefix_block_keys, 1, 2)
    far_context, far_total, own_far_max = far_part(
        queries, keys_t, prefix_block_values, lo, hi, blk, qgw, blk_index, scale
    )
    far_context = far_context.reshape(tok_dev, local_kv, qgw, HEAD_SIZE)
    far_total = far_total.reshape(tok_dev, local_kv, qgw)
    own_far_max = own_far_max.reshape(tok_dev, local_kv, qgw)

    row_ends = jnp.cumsum(suffix_len)
    starts = row_ends - suffix_len
    own_rows = blk_index * tok_dev + jnp.arange(tok_dev, dtype=jnp.int32)
    earlier_keys, earlier_values = from_behind((suffix_key_rows, suffix_value_rows), "blk", 1)
    near_keys = jnp.concatenate([earlier_keys, suffix_key_rows], axis=0).reshape(
        2 * tok_dev, local_kv, HEAD_SIZE
    )
    near_values = jnp.concatenate([earlier_values, suffix_value_rows], axis=0).reshape(
        2 * tok_dev, local_kv, HEAD_SIZE
    )
    near_rows = (blk_index - 1) * tok_dev + jnp.arange(2 * tok_dev, dtype=jnp.int32)
    own_req = request_of(own_rows, starts, row_ends)
    near_req = request_of(near_rows, starts, row_ends)
    allowed = (
        (own_req[:, None] == near_req[None, :])
        & (near_rows[None, :] <= own_rows[:, None])
        & (near_rows[None, :] >= 0)
    )
    own_queries = queries.reshape(tok_dev, local_kv, qgw, HEAD_SIZE)
    near_scores = (
        jnp.einsum("sgjd,tgd->sgjt", own_queries, near_keys, preferred_element_type=jnp.float32)
        * scale
    )
    near_scores = jnp.where(allowed[:, None, None, :], near_scores, -jnp.inf)
    near_max = jnp.max(near_scores, axis=3)
    top = jnp.maximum(own_far_max, near_max)
    near_prob = jnp.exp(near_scores - top[..., None])
    near_total = jnp.sum(near_prob, axis=3)
    near_context = jnp.einsum(
        "sgjt,tgd->sgjd",
        near_prob.astype(jnp.bfloat16),
        near_values,
        preferred_element_type=jnp.float32,
    )
    far_scale = jnp.exp(own_far_max - top)
    context = far_context * far_scale[..., None] + near_context
    denominator = far_total * far_scale + near_total
    attention = (context / denominator[..., None]).reshape(tok_dev, q_cols).astype(jnp.bfloat16)
    projected = jnp.dot(attention, w_out, preferred_element_type=jnp.float32)
    return column_sum(projected, "kvh").astype(jnp.bfloat16)


def solution(mesh):
    placed = (
        P("blk", "kvh"),
        P("blk", "kvh"),
        P("blk", "kvh"),
        P("blk", None, "kvh"),
        P("blk", None, "kvh"),
        P("blk"),
        P(),
        P(),
        P("kvh", None),
    )
    return jax.shard_map(
        per_device, mesh=mesh, in_specs=placed, out_specs=P("blk", "kvh"), check_vma=False
    )
```

```python
import functools
import math

import jax
import jax.numpy as jnp
from jax import lax
from jax.experimental import pallas as pl
from jax.experimental.pallas import tpu as pltpu
from jax.sharding import PartitionSpec as P

HEAD_SIZE = 128
SLOTS = 5
STAT_LANES = 128


def from_behind(block, axis, distance):
    devices = range(lax.axis_size(axis))
    route = [(i - distance, i) for i in devices if i - distance in devices]
    return lax.ppermute(block, axis, route)


def request_of(row_ids, starts, row_ends):
    inside = (row_ids[:, None] >= starts[None, :]) & (row_ids[:, None] < row_ends[None, :])
    req_ids = jnp.arange(starts.shape[0], dtype=jnp.int32)
    return jnp.sum(jnp.where(inside, req_ids[None, :], 0), axis=1)


def tile_tables(suffix_len, request_group, block_group, n_tiles, tile):
    row_ends = jnp.cumsum(suffix_len).astype(jnp.int32)
    starts = row_ends - suffix_len
    tile_lo = jnp.arange(n_tiles, dtype=jnp.int32) * tile
    first = jnp.sum((row_ends[None, :] <= tile_lo[:, None]).astype(jnp.int32), axis=1)
    last = jnp.sum((row_ends[None, :] <= (tile_lo + tile - 1)[:, None]).astype(jnp.int32), axis=1)
    req = first[:, None] + jnp.arange(SLOTS, dtype=jnp.int32)[None, :]
    valid = req <= last[:, None]
    req_v = jnp.minimum(req, last[:, None])
    lo = jnp.where(valid, starts[req_v], 0).astype(jnp.int32)
    hi = jnp.where(valid, row_ends[req_v], 0).astype(jnp.int32)
    group_count = suffix_len.shape[0] // 4
    blocks = block_group.shape[0]
    owns = block_group[None, :] == jnp.arange(group_count, dtype=jnp.int32)[:, None]
    block_of_group = jnp.sum(
        jnp.where(owns, jnp.arange(blocks, dtype=jnp.int32)[None, :], 0), axis=1
    ).astype(jnp.int32)
    blk = block_of_group[request_group[req_v]].astype(jnp.int32)
    return lo.reshape(-1), hi.reshape(-1), blk.reshape(-1)


def _slot_mask(lo_ref, hi_ref, base, rows):
    seg = lax.broadcasted_iota(jnp.int32, (1, SLOTS * HEAD_SIZE), 1) // HEAD_SIZE
    own = jnp.zeros(rows.shape, jnp.int32)
    for s in range(SLOTS):
        inside = (rows >= lo_ref[base + s]) & (rows < hi_ref[base + s])
        own = jnp.where(inside, s, own)
    return seg == own


def _slot_keys(kt_ref, blk_ref, base, kv):
    cols = slice(kv * HEAD_SIZE, (kv + 1) * HEAD_SIZE)
    return jnp.concatenate([kt_ref[blk_ref[base + s], cols, :] for s in range(SLOTS)], axis=1)


def _slot_values(v_ref, blk_ref, base, kv):
    cols = slice(kv * HEAD_SIZE, (kv + 1) * HEAD_SIZE)
    return jnp.concatenate([v_ref[blk_ref[base + s], :, cols] for s in range(SLOTS)], axis=0)


def _stacked(q_ref, kv, qgw):
    return jnp.concatenate(
        [q_ref[:, h * HEAD_SIZE : (h + 1) * HEAD_SIZE] for h in range(kv * qgw, (kv + 1) * qgw)],
        axis=0,
    )


def max_kernel(lo_ref, hi_ref, blk_ref, q_ref, kt_ref, m_ref, *, heads, qgw, scale):
    i = pl.program_id(0)
    tile = q_ref.shape[0]
    base = i * SLOTS
    rows = i * tile + lax.broadcasted_iota(jnp.int32, (qgw * tile, 1), 0) % tile
    mask = _slot_mask(lo_ref, hi_ref, base, rows)
    lane = lax.broadcasted_iota(jnp.int32, (1, STAT_LANES), 1)
    stats = jnp.full((tile, STAT_LANES), -jnp.inf, jnp.float32)
    for kv in range(heads // qgw):
        keys = _slot_keys(kt_ref, blk_ref, base, kv)
        sc = jnp.dot(_stacked(q_ref, kv, qgw), keys, preferred_element_type=jnp.float32)
        mx = jnp.max(jnp.where(mask, sc, -jnp.inf), axis=1, keepdims=True) * scale
        for j in range(qgw):
            stats = jnp.where(lane == kv * qgw + j, mx[j * tile : (j + 1) * tile], stats)
    m_ref[...] = jnp.transpose(stats)[: m_ref.shape[0], :]


def ctx_kernel(
    lo_ref, hi_ref, blk_ref, q_ref, kt_ref, v_ref, m_ref, o_ref, t_ref, *, heads, qgw, scale
):
    i = pl.program_id(0)
    tile = q_ref.shape[0]
    base = i * SLOTS
    rows = i * tile + lax.broadcasted_iota(jnp.int32, (qgw * tile, 1), 0) % tile
    mask = _slot_mask(lo_ref, hi_ref, base, rows)
    lane = lax.broadcasted_iota(jnp.int32, (1, STAT_LANES), 1)
    totals = jnp.zeros((tile, STAT_LANES), jnp.float32)
    tops = jnp.transpose(m_ref[...])
    for kv in range(heads // qgw):
        group = range(kv * qgw, (kv + 1) * qgw)
        keys = _slot_keys(kt_ref, blk_ref, base, kv)
        values = _slot_values(v_ref, blk_ref, base, kv)
        sc = jnp.dot(_stacked(q_ref, kv, qgw), keys, preferred_element_type=jnp.float32) * scale
        top = jnp.concatenate([tops[:, h : h + 1] for h in group], axis=0)
        p = jnp.exp(jnp.where(mask, sc - top, -jnp.inf))
        ctx = jnp.dot(p.astype(jnp.bfloat16), values, preferred_element_type=jnp.float32)
        tot = jnp.sum(p, axis=1, keepdims=True)
        for j, h in enumerate(group):
            o_ref[:, h * HEAD_SIZE : (h + 1) * HEAD_SIZE] = ctx[j * tile : (j + 1) * tile]
            totals = jnp.where(lane == h, tot[j * tile : (j + 1) * tile], totals)
    t_ref[...] = jnp.transpose(totals)[: t_ref.shape[0], :]


def butterfly(x, axis, combine):
    n = lax.axis_size(axis)
    stride = 1
    while stride < n:
        radix = 2 if stride == 1 or n % (stride * 4) else 4
        digit = lambda i: (i // stride) % radix
        got = [
            lax.ppermute(
                x,
                axis,
                [(i, i + ((digit(i) + d) % radix - digit(i)) * stride) for i in range(n)],
            )
            for d in range(1, radix)
        ]
        for g in got:
            x = combine(x, g)
        stride *= radix
    return x


def far_part(queries, keys_t, values, lo, hi, blk, qgw, blk_index, scale):
    tok_dev, q_cols = queries.shape
    heads = q_cols // HEAD_SIZE
    blocks, kv_cols, block_len = keys_t.shape
    gathered = lax.all_gather(queries, "blk", axis=0, tiled=True)
    row_count = gathered.shape[0]
    n_tiles = row_count // tok_dev
    stat_rows = 8
    q_spec = pl.BlockSpec((tok_dev, q_cols), lambda i, *_: (i, 0))
    kt_spec = pl.BlockSpec((blocks, kv_cols, block_len), lambda i, *_: (0, 0, 0))
    v_spec = pl.BlockSpec((blocks, block_len, kv_cols), lambda i, *_: (0, 0, 0))
    s_spec = pl.BlockSpec((stat_rows, tok_dev), lambda i, *_: (i, 0))
    stat_shape = jax.ShapeDtypeStruct((n_tiles * stat_rows, tok_dev), jnp.float32)
    kw = dict(heads=heads, qgw=qgw, scale=scale)
    local_max = pl.pallas_call(
        functools.partial(max_kernel, **kw),
        out_shape=stat_shape,
        grid_spec=pltpu.PrefetchScalarGridSpec(
            num_scalar_prefetch=3, grid=(n_tiles,), in_specs=[q_spec, kt_spec], out_specs=s_spec
        ),
    )(lo, hi, blk, gathered, keys_t)
    far_max = butterfly(local_max, "blk", jnp.maximum)
    partial, totals = pl.pallas_call(
        functools.partial(ctx_kernel, **kw),
        out_shape=(jax.ShapeDtypeStruct((row_count, q_cols), jnp.float32), stat_shape),
        grid_spec=pltpu.PrefetchScalarGridSpec(
            num_scalar_prefetch=3,
            grid=(n_tiles,),
            in_specs=[q_spec, kt_spec, v_spec, s_spec],
            out_specs=(pl.BlockSpec((tok_dev, q_cols), lambda i, *_: (i, 0)), s_spec),
        ),
    )(lo, hi, blk, gathered, keys_t, values, far_max)
    context = lax.psum_scatter(partial, "blk", scatter_dimension=0, tiled=True)
    totals = butterfly(totals, "blk", jnp.add)
    own = lambda a: jnp.transpose(
        lax.dynamic_slice_in_dim(a, blk_index * stat_rows, stat_rows, 0)[:heads]
    )
    return context, own(totals), own(far_max)


def column_sum(x, axis):
    n = lax.axis_size(axis)
    me = lax.axis_index(axis)
    width = x.shape[1] // n
    chunk = lambda k: lax.dynamic_slice_in_dim(x, (k % n) * width, width, 1)
    total = chunk(me)
    for d in range(1, n):
        sent = chunk(me + d).astype(jnp.bfloat16)
        got = lax.ppermute(sent, axis, [(i, (i + d) % n) for i in range(n)])
        total = total + got.astype(jnp.float32)
    return total


def per_device(
    queries,
    suffix_key_rows,
    suffix_value_rows,
    prefix_block_keys,
    prefix_block_values,
    block_group,
    suffix_len,
    request_group,
    w_out,
):
    tok_dev = queries.shape[0]
    q_cols = queries.shape[1]
    kv_cols = suffix_key_rows.shape[1]
    local_kv = kv_cols // HEAD_SIZE
    local_heads = q_cols // HEAD_SIZE
    qgw = local_heads // local_kv
    blocks, block_len, _ = prefix_block_keys.shape
    blk_count = lax.axis_size("blk")
    row_count = blk_count * tok_dev
    blk_index = lax.axis_index("blk")
    scale = 1.0 / math.sqrt(HEAD_SIZE)
    tile = tok_dev
    n_tiles = row_count // tile

    lo, hi, blk = tile_tables(suffix_len, request_group, block_group, n_tiles, tile)
    keys_t = jnp.swapaxes(prefix_block_keys, 1, 2)
    far_context, far_total, own_far_max = far_part(
        queries, keys_t, prefix_block_values, lo, hi, blk, qgw, blk_index, scale
    )
    far_context = far_context.reshape(tok_dev, local_kv, qgw, HEAD_SIZE)
    far_total = far_total.reshape(tok_dev, local_kv, qgw)
    own_far_max = own_far_max.reshape(tok_dev, local_kv, qgw)

    row_ends = jnp.cumsum(suffix_len)
    starts = row_ends - suffix_len
    own_rows = blk_index * tok_dev + jnp.arange(tok_dev, dtype=jnp.int32)
    earlier_keys, earlier_values = from_behind((suffix_key_rows, suffix_value_rows), "blk", 1)
    near_keys = jnp.concatenate([earlier_keys, suffix_key_rows], axis=0).reshape(
        2 * tok_dev, local_kv, HEAD_SIZE
    )
    near_values = jnp.concatenate([earlier_values, suffix_value_rows], axis=0).reshape(
        2 * tok_dev, local_kv, HEAD_SIZE
    )
    near_rows = (blk_index - 1) * tok_dev + jnp.arange(2 * tok_dev, dtype=jnp.int32)
    own_req = request_of(own_rows, starts, row_ends)
    near_req = request_of(near_rows, starts, row_ends)
    allowed = (
        (own_req[:, None] == near_req[None, :])
        & (near_rows[None, :] <= own_rows[:, None])
        & (near_rows[None, :] >= 0)
    )
    own_queries = queries.reshape(tok_dev, local_kv, qgw, HEAD_SIZE)
    near_scores = (
        jnp.einsum("sgjd,tgd->sgjt", own_queries, near_keys, preferred_element_type=jnp.float32)
        * scale
    )
    near_scores = jnp.where(allowed[:, None, None, :], near_scores, -jnp.inf)
    near_max = jnp.max(near_scores, axis=3)
    top = jnp.maximum(own_far_max, near_max)
    near_prob = jnp.exp(near_scores - top[..., None])
    near_total = jnp.sum(near_prob, axis=3)
    near_context = jnp.einsum(
        "sgjt,tgd->sgjd",
        near_prob.astype(jnp.bfloat16),
        near_values,
        preferred_element_type=jnp.float32,
    )
    far_scale = jnp.exp(own_far_max - top)
    context = far_context * far_scale[..., None] + near_context
    denominator = far_total * far_scale + near_total
    attention = (context / denominator[..., None]).reshape(tok_dev, q_cols).astype(jnp.bfloat16)
    projected = jnp.dot(attention, w_out, preferred_element_type=jnp.float32)
    return column_sum(projected, "kvh").astype(jnp.bfloat16)


def solution(mesh):
    placed = (
        P("blk", "kvh"),
        P("blk", "kvh"),
        P("blk", "kvh"),
        P("blk", None, "kvh"),
        P("blk", None, "kvh"),
        P("blk"),
        P(),
        P(),
        P("kvh", None),
    )
    return jax.shard_map(
        per_device, mesh=mesh, in_specs=placed, out_specs=P("blk", "kvh"), check_vma=False
    )
```

```python
import functools
import math

import jax
import jax.numpy as jnp
from jax import lax
from jax.experimental import pallas as pl
from jax.experimental.pallas import tpu as pltpu
from jax.sharding import PartitionSpec as P

HEAD_SIZE = 128
SLOTS = 5
STAT_LANES = 128


def from_behind(block, axis, distance):
    devices = range(lax.axis_size(axis))
    route = [(i - distance, i) for i in devices if i - distance in devices]
    return lax.ppermute(block, axis, route)


def request_of(row_ids, starts, row_ends):
    inside = (row_ids[:, None] >= starts[None, :]) & (row_ids[:, None] < row_ends[None, :])
    req_ids = jnp.arange(starts.shape[0], dtype=jnp.int32)
    return jnp.sum(jnp.where(inside, req_ids[None, :], 0), axis=1)


def tile_tables(suffix_len, request_group, block_group, n_tiles, tile):
    row_ends = jnp.cumsum(suffix_len).astype(jnp.int32)
    starts = row_ends - suffix_len
    tile_lo = jnp.arange(n_tiles, dtype=jnp.int32) * tile
    first = jnp.sum((row_ends[None, :] <= tile_lo[:, None]).astype(jnp.int32), axis=1)
    last = jnp.sum((row_ends[None, :] <= (tile_lo + tile - 1)[:, None]).astype(jnp.int32), axis=1)
    req = first[:, None] + jnp.arange(SLOTS, dtype=jnp.int32)[None, :]
    valid = req <= last[:, None]
    req_v = jnp.minimum(req, last[:, None])
    lo = jnp.where(valid, starts[req_v], 0).astype(jnp.int32)
    hi = jnp.where(valid, row_ends[req_v], 0).astype(jnp.int32)
    group_count = suffix_len.shape[0] // 4
    blocks = block_group.shape[0]
    owns = block_group[None, :] == jnp.arange(group_count, dtype=jnp.int32)[:, None]
    block_of_group = jnp.sum(
        jnp.where(owns, jnp.arange(blocks, dtype=jnp.int32)[None, :], 0), axis=1
    ).astype(jnp.int32)
    blk = block_of_group[request_group[req_v]].astype(jnp.int32)
    return lo.reshape(-1), hi.reshape(-1), blk.reshape(-1)


def _slot_mask(lo_ref, hi_ref, base, rows):
    seg = lax.broadcasted_iota(jnp.int32, (1, SLOTS * HEAD_SIZE), 1) // HEAD_SIZE
    own = jnp.zeros(rows.shape, jnp.int32)
    for s in range(SLOTS):
        inside = (rows >= lo_ref[base + s]) & (rows < hi_ref[base + s])
        own = jnp.where(inside, s, own)
    return seg == own


def _slot_keys(kt_ref, blk_ref, base, kv):
    cols = slice(kv * HEAD_SIZE, (kv + 1) * HEAD_SIZE)
    return jnp.concatenate([kt_ref[blk_ref[base + s], cols, :] for s in range(SLOTS)], axis=1)


def _slot_values(v_ref, blk_ref, base, kv):
    cols = slice(kv * HEAD_SIZE, (kv + 1) * HEAD_SIZE)
    return jnp.concatenate([v_ref[blk_ref[base + s], :, cols] for s in range(SLOTS)], axis=0)


def _stacked(q_ref, kv, qgw):
    return jnp.concatenate(
        [q_ref[:, h * HEAD_SIZE : (h + 1) * HEAD_SIZE] for h in range(kv * qgw, (kv + 1) * qgw)],
        axis=0,
    )


def max_kernel(lo_ref, hi_ref, blk_ref, q_ref, kt_ref, m_ref, *, heads, qgw, scale):
    i = pl.program_id(0)
    tile = q_ref.shape[0]
    base = i * SLOTS
    rows = i * tile + lax.broadcasted_iota(jnp.int32, (qgw * tile, 1), 0) % tile
    mask = _slot_mask(lo_ref, hi_ref, base, rows)
    lane = lax.broadcasted_iota(jnp.int32, (1, STAT_LANES), 1)
    stats = jnp.full((tile, STAT_LANES), -jnp.inf, jnp.float32)
    for kv in range(heads // qgw):
        keys = _slot_keys(kt_ref, blk_ref, base, kv)
        sc = jnp.dot(_stacked(q_ref, kv, qgw), keys, preferred_element_type=jnp.float32)
        mx = jnp.max(jnp.where(mask, sc, -jnp.inf), axis=1, keepdims=True) * scale
        for j in range(qgw):
            stats = jnp.where(lane == kv * qgw + j, mx[j * tile : (j + 1) * tile], stats)
    m_ref[...] = jnp.transpose(stats)[: m_ref.shape[0], :]


def ctx_kernel(
    lo_ref, hi_ref, blk_ref, q_ref, kt_ref, v_ref, o_ref, t_ref, m_ref, *, heads, qgw, scale
):
    i = pl.program_id(0)
    tile = q_ref.shape[0]
    base = i * SLOTS
    rows = i * tile + lax.broadcasted_iota(jnp.int32, (qgw * tile, 1), 0) % tile
    mask = _slot_mask(lo_ref, hi_ref, base, rows)
    lane = lax.broadcasted_iota(jnp.int32, (1, STAT_LANES), 1)
    totals = jnp.zeros((tile, STAT_LANES), jnp.float32)
    maxes = jnp.full((tile, STAT_LANES), -jnp.inf, jnp.float32)
    for kv in range(heads // qgw):
        group = range(kv * qgw, (kv + 1) * qgw)
        keys = _slot_keys(kt_ref, blk_ref, base, kv)
        values = _slot_values(v_ref, blk_ref, base, kv)
        sc = jnp.dot(_stacked(q_ref, kv, qgw), keys, preferred_element_type=jnp.float32)
        sc = jnp.where(mask, sc, -jnp.inf)
        top = jnp.max(sc, axis=1, keepdims=True) * scale
        p = jnp.exp(sc * scale - top)
        ctx = jnp.dot(p.astype(jnp.bfloat16), values, preferred_element_type=jnp.float32)
        tot = jnp.sum(p, axis=1, keepdims=True)
        for j, h in enumerate(group):
            o_ref[:, h * HEAD_SIZE : (h + 1) * HEAD_SIZE] = ctx[j * tile : (j + 1) * tile]
            totals = jnp.where(lane == h, tot[j * tile : (j + 1) * tile], totals)
            maxes = jnp.where(lane == h, top[j * tile : (j + 1) * tile], maxes)
    t_ref[...] = jnp.transpose(totals)[: t_ref.shape[0], :]
    m_ref[...] = jnp.transpose(maxes)[: m_ref.shape[0], :]


def butterfly(x, axis, combine):
    n = lax.axis_size(axis)
    stride = 1
    while stride < n:
        radix = 2 if stride == 1 or n % (stride * 4) else 4
        digit = lambda i: (i // stride) % radix
        got = [
            lax.ppermute(
                x,
                axis,
                [(i, i + ((digit(i) + d) % radix - digit(i)) * stride) for i in range(n)],
            )
            for d in range(1, radix)
        ]
        for g in got:
            x = combine(x, g)
        stride *= radix
    return x


def far_part(queries, keys_t, values, lo, hi, blk, qgw, blk_index, scale):
    tok_dev, q_cols = queries.shape
    heads = q_cols // HEAD_SIZE
    blocks, kv_cols, block_len = keys_t.shape
    gathered = lax.all_gather(queries, "blk", axis=0, tiled=True)
    row_count = gathered.shape[0]
    n_tiles = row_count // tok_dev
    stat_rows = 8
    q_spec = pl.BlockSpec((tok_dev, q_cols), lambda i, *_: (i, 0))
    kt_spec = pl.BlockSpec((blocks, kv_cols, block_len), lambda i, *_: (0, 0, 0))
    v_spec = pl.BlockSpec((blocks, block_len, kv_cols), lambda i, *_: (0, 0, 0))
    s_spec = pl.BlockSpec((stat_rows, tok_dev), lambda i, *_: (i, 0))
    stat_shape = jax.ShapeDtypeStruct((n_tiles * stat_rows, tok_dev), jnp.float32)
    kw = dict(heads=heads, qgw=qgw, scale=scale)
    partial, totals, local_max = pl.pallas_call(
        functools.partial(ctx_kernel, **kw),
        out_shape=(jax.ShapeDtypeStruct((row_count, q_cols), jnp.float32), stat_shape, stat_shape),
        grid_spec=pltpu.PrefetchScalarGridSpec(
            num_scalar_prefetch=3,
            grid=(n_tiles,),
            in_specs=[q_spec, kt_spec, v_spec],
            out_specs=(pl.BlockSpec((tok_dev, q_cols), lambda i, *_: (i, 0)), s_spec, s_spec),
        ),
    )(lo, hi, blk, gathered, keys_t, values)
    far_max = butterfly(local_max, "blk", jnp.maximum)
    factor = jnp.exp(local_max - far_max)
    row_factor = jnp.transpose(
        factor.reshape(n_tiles, stat_rows, tok_dev)[:, :heads], (0, 2, 1)
    ).reshape(row_count, heads, 1)
    partial = (partial.reshape(row_count, heads, HEAD_SIZE) * row_factor).reshape(row_count, q_cols)
    totals = totals * factor
    context = lax.psum_scatter(partial, "blk", scatter_dimension=0, tiled=True)
    totals = butterfly(totals, "blk", jnp.add)
    own = lambda a: jnp.transpose(
        lax.dynamic_slice_in_dim(a, blk_index * stat_rows, stat_rows, 0)[:heads]
    )
    return context, own(totals), own(far_max)


def column_sum(x, axis):
    n = lax.axis_size(axis)
    me = lax.axis_index(axis)
    width = x.shape[1] // n
    chunk = lambda k: lax.dynamic_slice_in_dim(x, (k % n) * width, width, 1)
    total = chunk(me)
    for d in range(1, n):
        sent = chunk(me + d).astype(jnp.bfloat16)
        got = lax.ppermute(sent, axis, [(i, (i + d) % n) for i in range(n)])
        total = total + got.astype(jnp.float32)
    return total


def per_device(
    queries,
    suffix_key_rows,
    suffix_value_rows,
    prefix_block_keys,
    prefix_block_values,
    block_group,
    suffix_len,
    request_group,
    w_out,
):
    tok_dev = queries.shape[0]
    q_cols = queries.shape[1]
    kv_cols = suffix_key_rows.shape[1]
    local_kv = kv_cols // HEAD_SIZE
    local_heads = q_cols // HEAD_SIZE
    qgw = local_heads // local_kv
    blocks, block_len, _ = prefix_block_keys.shape
    blk_count = lax.axis_size("blk")
    row_count = blk_count * tok_dev
    blk_index = lax.axis_index("blk")
    scale = 1.0 / math.sqrt(HEAD_SIZE)
    tile = tok_dev
    n_tiles = row_count // tile

    lo, hi, blk = tile_tables(suffix_len, request_group, block_group, n_tiles, tile)
    keys_t = jnp.swapaxes(prefix_block_keys, 1, 2)
    far_context, far_total, own_far_max = far_part(
        queries, keys_t, prefix_block_values, lo, hi, blk, qgw, blk_index, scale
    )
    far_context = far_context.reshape(tok_dev, local_kv, qgw, HEAD_SIZE)
    far_total = far_total.reshape(tok_dev, local_kv, qgw)
    own_far_max = own_far_max.reshape(tok_dev, local_kv, qgw)

    row_ends = jnp.cumsum(suffix_len)
    starts = row_ends - suffix_len
    own_rows = blk_index * tok_dev + jnp.arange(tok_dev, dtype=jnp.int32)
    earlier_keys, earlier_values = from_behind((suffix_key_rows, suffix_value_rows), "blk", 1)
    near_keys = jnp.concatenate([earlier_keys, suffix_key_rows], axis=0).reshape(
        2 * tok_dev, local_kv, HEAD_SIZE
    )
    near_values = jnp.concatenate([earlier_values, suffix_value_rows], axis=0).reshape(
        2 * tok_dev, local_kv, HEAD_SIZE
    )
    near_rows = (blk_index - 1) * tok_dev + jnp.arange(2 * tok_dev, dtype=jnp.int32)
    own_req = request_of(own_rows, starts, row_ends)
    near_req = request_of(near_rows, starts, row_ends)
    allowed = (
        (own_req[:, None] == near_req[None, :])
        & (near_rows[None, :] <= own_rows[:, None])
        & (near_rows[None, :] >= 0)
    )
    own_queries = queries.reshape(tok_dev, local_kv, qgw, HEAD_SIZE)
    near_scores = (
        jnp.einsum("sgjd,tgd->sgjt", own_queries, near_keys, preferred_element_type=jnp.float32)
        * scale
    )
    near_scores = jnp.where(allowed[:, None, None, :], near_scores, -jnp.inf)
    near_max = jnp.max(near_scores, axis=3)
    top = jnp.maximum(own_far_max, near_max)
    near_prob = jnp.exp(near_scores - top[..., None])
    near_total = jnp.sum(near_prob, axis=3)
    near_context = jnp.einsum(
        "sgjt,tgd->sgjd",
        near_prob.astype(jnp.bfloat16),
        near_values,
        preferred_element_type=jnp.float32,
    )
    far_scale = jnp.exp(own_far_max - top)
    context = far_context * far_scale[..., None] + near_context
    denominator = far_total * far_scale + near_total
    attention = (context / denominator[..., None]).reshape(tok_dev, q_cols).astype(jnp.bfloat16)
    projected = jnp.dot(attention, w_out, preferred_element_type=jnp.float32)
    return column_sum(projected, "kvh").astype(jnp.bfloat16)


def solution(mesh):
    placed = (
        P("blk", "kvh"),
        P("blk", "kvh"),
        P("blk", "kvh"),
        P("blk", None, "kvh"),
        P("blk", None, "kvh"),
        P("blk"),
        P(),
        P(),
        P("kvh", None),
    )
    return jax.shard_map(
        per_device, mesh=mesh, in_specs=placed, out_specs=P("blk", "kvh"), check_vma=False
    )
```

```python
import functools
import math

import jax
import jax.numpy as jnp
from jax import lax
from jax.experimental import pallas as pl
from jax.experimental.pallas import tpu as pltpu
from jax.sharding import PartitionSpec as P

HEAD_SIZE = 128
SLOTS = 5
STAT_LANES = 128


def from_behind(block, axis, distance):
    devices = range(lax.axis_size(axis))
    route = [(i - distance, i) for i in devices if i - distance in devices]
    return lax.ppermute(block, axis, route)


def request_of(row_ids, starts, row_ends):
    inside = (row_ids[:, None] >= starts[None, :]) & (row_ids[:, None] < row_ends[None, :])
    req_ids = jnp.arange(starts.shape[0], dtype=jnp.int32)
    return jnp.sum(jnp.where(inside, req_ids[None, :], 0), axis=1)


def tile_tables(suffix_len, request_group, block_group, n_tiles, tile):
    row_ends = jnp.cumsum(suffix_len).astype(jnp.int32)
    starts = row_ends - suffix_len
    tile_lo = jnp.arange(n_tiles, dtype=jnp.int32) * tile
    first = jnp.sum((row_ends[None, :] <= tile_lo[:, None]).astype(jnp.int32), axis=1)
    last = jnp.sum((row_ends[None, :] <= (tile_lo + tile - 1)[:, None]).astype(jnp.int32), axis=1)
    req = first[:, None] + jnp.arange(SLOTS, dtype=jnp.int32)[None, :]
    valid = req <= last[:, None]
    req_v = jnp.minimum(req, last[:, None])
    lo = jnp.where(valid, starts[req_v], 0).astype(jnp.int32)
    hi = jnp.where(valid, row_ends[req_v], 0).astype(jnp.int32)
    group_count = suffix_len.shape[0] // 4
    blocks = block_group.shape[0]
    owns = block_group[None, :] == jnp.arange(group_count, dtype=jnp.int32)[:, None]
    block_of_group = jnp.sum(
        jnp.where(owns, jnp.arange(blocks, dtype=jnp.int32)[None, :], 0), axis=1
    ).astype(jnp.int32)
    blk = block_of_group[request_group[req_v]].astype(jnp.int32)
    return lo.reshape(-1), hi.reshape(-1), blk.reshape(-1)


def _slot_mask(lo_ref, hi_ref, base, rows):
    seg = lax.broadcasted_iota(jnp.int32, (1, SLOTS * HEAD_SIZE), 1) // HEAD_SIZE
    own = jnp.zeros(rows.shape, jnp.int32)
    for s in range(SLOTS):
        inside = (rows >= lo_ref[base + s]) & (rows < hi_ref[base + s])
        own = jnp.where(inside, s, own)
    return seg == own


def _slot_keys(kt_ref, blk_ref, base, kv):
    cols = slice(kv * HEAD_SIZE, (kv + 1) * HEAD_SIZE)
    return jnp.concatenate([kt_ref[blk_ref[base + s], cols, :] for s in range(SLOTS)], axis=1)


def _slot_values(v_ref, blk_ref, base, kv):
    cols = slice(kv * HEAD_SIZE, (kv + 1) * HEAD_SIZE)
    return jnp.concatenate([v_ref[blk_ref[base + s], :, cols] for s in range(SLOTS)], axis=0)


def _stacked(q_ref, kv, qgw):
    return jnp.concatenate(
        [q_ref[:, h * HEAD_SIZE : (h + 1) * HEAD_SIZE] for h in range(kv * qgw, (kv + 1) * qgw)],
        axis=0,
    )


def max_kernel(lo_ref, hi_ref, blk_ref, q_ref, kt_ref, m_ref, *, heads, qgw, scale):
    i = pl.program_id(0)
    tile = q_ref.shape[0]
    base = i * SLOTS
    rows = i * tile + lax.broadcasted_iota(jnp.int32, (qgw * tile, 1), 0) % tile
    mask = _slot_mask(lo_ref, hi_ref, base, rows)
    lane = lax.broadcasted_iota(jnp.int32, (1, STAT_LANES), 1)
    stats = jnp.full((tile, STAT_LANES), -jnp.inf, jnp.float32)
    for kv in range(heads // qgw):
        keys = _slot_keys(kt_ref, blk_ref, base, kv)
        sc = jnp.dot(_stacked(q_ref, kv, qgw), keys, preferred_element_type=jnp.float32)
        mx = jnp.max(jnp.where(mask, sc, -jnp.inf), axis=1, keepdims=True) * scale
        for j in range(qgw):
            stats = jnp.where(lane == kv * qgw + j, mx[j * tile : (j + 1) * tile], stats)
    m_ref[...] = jnp.transpose(stats)[: m_ref.shape[0], :]


def ctx_kernel(
    lo_ref, hi_ref, blk_ref, q_ref, kt_ref, v_ref, m_ref, o_ref, t_ref, *, heads, qgw, scale
):
    i = pl.program_id(0)
    tile = q_ref.shape[0]
    base = i * SLOTS
    rows = i * tile + lax.broadcasted_iota(jnp.int32, (qgw * tile, 1), 0) % tile
    mask = _slot_mask(lo_ref, hi_ref, base, rows)
    lane = lax.broadcasted_iota(jnp.int32, (1, STAT_LANES), 1)
    totals = jnp.zeros((tile, STAT_LANES), jnp.float32)
    tops = jnp.transpose(m_ref[...])
    for kv in range(heads // qgw):
        group = range(kv * qgw, (kv + 1) * qgw)
        keys = _slot_keys(kt_ref, blk_ref, base, kv)
        values = _slot_values(v_ref, blk_ref, base, kv)
        sc = jnp.dot(_stacked(q_ref, kv, qgw), keys, preferred_element_type=jnp.float32) * scale
        top = jnp.concatenate([tops[:, h : h + 1] for h in group], axis=0)
        p = jnp.exp(jnp.where(mask, sc - top, -jnp.inf))
        ctx = jnp.dot(p.astype(jnp.bfloat16), values, preferred_element_type=jnp.float32)
        tot = jnp.sum(p, axis=1, keepdims=True)
        for j, h in enumerate(group):
            o_ref[:, h * HEAD_SIZE : (h + 1) * HEAD_SIZE] = ctx[j * tile : (j + 1) * tile]
            totals = jnp.where(lane == h, tot[j * tile : (j + 1) * tile], totals)
    t_ref[...] = jnp.transpose(totals)[: t_ref.shape[0], :]


def butterfly(x, axis, combine):
    n = lax.axis_size(axis)
    stride = 1
    while stride < n:
        radix = 2 if stride == 1 or n % (stride * 4) else 4
        digit = lambda i: (i // stride) % radix
        got = [
            lax.ppermute(
                x,
                axis,
                [(i, i + ((digit(i) + d) % radix - digit(i)) * stride) for i in range(n)],
            )
            for d in range(1, radix)
        ]
        for g in got:
            x = combine(x, g)
        stride *= radix
    return x


def far_part(queries, keys_t, values, lo, hi, blk, qgw, blk_index, scale):
    tok_dev, q_cols = queries.shape
    heads = q_cols // HEAD_SIZE
    blocks, kv_cols, block_len = keys_t.shape
    gathered = lax.all_gather(queries, "blk", axis=0, tiled=True)
    row_count = gathered.shape[0]
    n_tiles = row_count // tok_dev
    stat_rows = 8
    q_spec = pl.BlockSpec((tok_dev, q_cols), lambda i, *_: (i, 0))
    kt_spec = pl.BlockSpec((blocks, kv_cols, block_len), lambda i, *_: (0, 0, 0))
    v_spec = pl.BlockSpec((blocks, block_len, kv_cols), lambda i, *_: (0, 0, 0))
    s_spec = pl.BlockSpec((stat_rows, tok_dev), lambda i, *_: (i, 0))
    stat_shape = jax.ShapeDtypeStruct((n_tiles * stat_rows, tok_dev), jnp.float32)
    kw = dict(heads=heads, qgw=qgw, scale=scale)
    local_max = pl.pallas_call(
        functools.partial(max_kernel, **kw),
        out_shape=stat_shape,
        grid_spec=pltpu.PrefetchScalarGridSpec(
            num_scalar_prefetch=3, grid=(n_tiles,), in_specs=[q_spec, kt_spec], out_specs=s_spec
        ),
    )(lo, hi, blk, gathered, keys_t)
    far_max = butterfly(local_max, "blk", jnp.maximum)
    partial, totals = pl.pallas_call(
        functools.partial(ctx_kernel, **kw),
        out_shape=(jax.ShapeDtypeStruct((row_count, q_cols), jnp.float32), stat_shape),
        grid_spec=pltpu.PrefetchScalarGridSpec(
            num_scalar_prefetch=3,
            grid=(n_tiles,),
            in_specs=[q_spec, kt_spec, v_spec, s_spec],
            out_specs=(pl.BlockSpec((tok_dev, q_cols), lambda i, *_: (i, 0)), s_spec),
        ),
    )(lo, hi, blk, gathered, keys_t, values, far_max)
    context = lax.psum_scatter(partial, "blk", scatter_dimension=0, tiled=True)
    totals = butterfly(totals, "blk", jnp.add)
    own = lambda a: jnp.transpose(
        lax.dynamic_slice_in_dim(a, blk_index * stat_rows, stat_rows, 0)[:heads]
    )
    return context, own(totals), own(far_max)


def column_sum(x, axis):
    n = lax.axis_size(axis)
    me = lax.axis_index(axis)
    width = x.shape[1] // n
    chunk = lambda k: lax.dynamic_slice_in_dim(x, (k % n) * width, width, 1)
    total = chunk(me)
    for d in range(1, n):
        sent = chunk(me + d).astype(jnp.bfloat16)
        got = lax.ppermute(sent, axis, [(i, (i + d) % n) for i in range(n)])
        total = total + got.astype(jnp.float32)
    return total


def per_device(
    queries,
    suffix_key_rows,
    suffix_value_rows,
    prefix_block_keys,
    prefix_block_values,
    block_group,
    suffix_len,
    request_group,
    w_out,
):
    tok_dev = queries.shape[0]
    q_cols = queries.shape[1]
    kv_cols = suffix_key_rows.shape[1]
    local_kv = kv_cols // HEAD_SIZE
    local_heads = q_cols // HEAD_SIZE
    qgw = local_heads // local_kv
    blocks, block_len, _ = prefix_block_keys.shape
    blk_count = lax.axis_size("blk")
    row_count = blk_count * tok_dev
    blk_index = lax.axis_index("blk")
    scale = 1.0 / math.sqrt(HEAD_SIZE)
    tile = tok_dev
    n_tiles = row_count // tile

    lo, hi, blk = tile_tables(suffix_len, request_group, block_group, n_tiles, tile)
    keys_t = jnp.swapaxes(prefix_block_keys, 1, 2)
    far_context, far_total, own_far_max = far_part(
        queries, keys_t, prefix_block_values, lo, hi, blk, qgw, blk_index, scale
    )
    far_context = far_context.reshape(tok_dev, local_kv, qgw, HEAD_SIZE)
    far_total = far_total.reshape(tok_dev, local_kv, qgw)
    own_far_max = own_far_max.reshape(tok_dev, local_kv, qgw)

    row_ends = jnp.cumsum(suffix_len)
    starts = row_ends - suffix_len
    own_rows = blk_index * tok_dev + jnp.arange(tok_dev, dtype=jnp.int32)
    earlier_keys, earlier_values = from_behind((suffix_key_rows, suffix_value_rows), "blk", 1)
    near_keys = jnp.concatenate([earlier_keys, suffix_key_rows], axis=0).reshape(
        2 * tok_dev, local_kv, HEAD_SIZE
    )
    near_values = jnp.concatenate([earlier_values, suffix_value_rows], axis=0).reshape(
        2 * tok_dev, local_kv, HEAD_SIZE
    )
    near_rows = (blk_index - 1) * tok_dev + jnp.arange(2 * tok_dev, dtype=jnp.int32)
    own_req = request_of(own_rows, starts, row_ends)
    near_req = request_of(near_rows, starts, row_ends)
    allowed = (
        (own_req[:, None] == near_req[None, :])
        & (near_rows[None, :] <= own_rows[:, None])
        & (near_rows[None, :] >= 0)
    )
    own_queries = queries.reshape(tok_dev, local_kv, qgw, HEAD_SIZE)
    near_scores = (
        jnp.einsum("sgjd,tgd->sgjt", own_queries, near_keys, preferred_element_type=jnp.float32)
        * scale
    )
    near_scores = jnp.where(allowed[:, None, None, :], near_scores, -jnp.inf)
    near_max = jnp.max(near_scores, axis=3)
    top = jnp.maximum(own_far_max, near_max)
    near_prob = jnp.exp(near_scores - top[..., None])
    near_total = jnp.sum(near_prob, axis=3)
    near_context = jnp.einsum(
        "sgjt,tgd->sgjd",
        near_prob.astype(jnp.bfloat16),
        near_values,
        preferred_element_type=jnp.float32,
    )
    far_scale = jnp.exp(own_far_max - top)
    near_context, near_total, far_scale = lax.optimization_barrier(
        (near_context, near_total, far_scale)
    )
    context = far_context * far_scale[..., None] + near_context
    denominator = far_total * far_scale + near_total
    attention = (context / denominator[..., None]).reshape(tok_dev, q_cols).astype(jnp.bfloat16)
    projected = jnp.dot(attention, w_out, preferred_element_type=jnp.float32)
    return column_sum(projected, "kvh").astype(jnp.bfloat16)


def solution(mesh):
    placed = (
        P("blk", "kvh"),
        P("blk", "kvh"),
        P("blk", "kvh"),
        P("blk", None, "kvh"),
        P("blk", None, "kvh"),
        P("blk"),
        P(),
        P(),
        P("kvh", None),
    )
    return jax.shard_map(
        per_device, mesh=mesh, in_specs=placed, out_specs=P("blk", "kvh"), check_vma=False
    )
```

```python
import functools
import math

import jax
import jax.numpy as jnp
from jax import lax
from jax.experimental import pallas as pl
from jax.experimental.pallas import tpu as pltpu
from jax.sharding import PartitionSpec as P

HEAD_SIZE = 128
SLOTS = 5
STAT_LANES = 128


def from_behind(block, axis, distance):
    devices = range(lax.axis_size(axis))
    route = [(i - distance, i) for i in devices if i - distance in devices]
    return lax.ppermute(block, axis, route)


def request_of(row_ids, starts, row_ends):
    inside = (row_ids[:, None] >= starts[None, :]) & (row_ids[:, None] < row_ends[None, :])
    req_ids = jnp.arange(starts.shape[0], dtype=jnp.int32)
    return jnp.sum(jnp.where(inside, req_ids[None, :], 0), axis=1)


def tile_tables(suffix_len, request_group, block_group, n_tiles, tile):
    row_ends = jnp.cumsum(suffix_len).astype(jnp.int32)
    starts = row_ends - suffix_len
    tile_lo = jnp.arange(n_tiles, dtype=jnp.int32) * tile
    first = jnp.sum((row_ends[None, :] <= tile_lo[:, None]).astype(jnp.int32), axis=1)
    last = jnp.sum((row_ends[None, :] <= (tile_lo + tile - 1)[:, None]).astype(jnp.int32), axis=1)
    req = first[:, None] + jnp.arange(SLOTS, dtype=jnp.int32)[None, :]
    valid = req <= last[:, None]
    req_v = jnp.minimum(req, last[:, None])
    lo = jnp.where(valid, starts[req_v], 0).astype(jnp.int32)
    hi = jnp.where(valid, row_ends[req_v], 0).astype(jnp.int32)
    group_count = suffix_len.shape[0] // 4
    blocks = block_group.shape[0]
    owns = block_group[None, :] == jnp.arange(group_count, dtype=jnp.int32)[:, None]
    block_of_group = jnp.sum(
        jnp.where(owns, jnp.arange(blocks, dtype=jnp.int32)[None, :], 0), axis=1
    ).astype(jnp.int32)
    blk = block_of_group[request_group[req_v]].astype(jnp.int32)
    return lo.reshape(-1), hi.reshape(-1), blk.reshape(-1)


def _slot_mask(lo_ref, hi_ref, base, rows):
    seg = lax.broadcasted_iota(jnp.int32, (1, SLOTS * HEAD_SIZE), 1) // HEAD_SIZE
    own = jnp.zeros(rows.shape, jnp.int32)
    for s in range(SLOTS):
        inside = (rows >= lo_ref[base + s]) & (rows < hi_ref[base + s])
        own = jnp.where(inside, s, own)
    return seg == own


def _slot_keys(kt_ref, blk_ref, base, kv):
    cols = slice(kv * HEAD_SIZE, (kv + 1) * HEAD_SIZE)
    return jnp.concatenate([kt_ref[blk_ref[base + s], cols, :] for s in range(SLOTS)], axis=1)


def _slot_values(v_ref, blk_ref, base, kv):
    cols = slice(kv * HEAD_SIZE, (kv + 1) * HEAD_SIZE)
    return jnp.concatenate([v_ref[blk_ref[base + s], :, cols] for s in range(SLOTS)], axis=0)


def _stacked(q_ref, kv, qgw):
    return jnp.concatenate(
        [q_ref[:, h * HEAD_SIZE : (h + 1) * HEAD_SIZE] for h in range(kv * qgw, (kv + 1) * qgw)],
        axis=0,
    )


def max_kernel(lo_ref, hi_ref, blk_ref, q_ref, kt_ref, m_ref, *, heads, qgw, scale):
    i = pl.program_id(0)
    tile = q_ref.shape[0]
    base = i * SLOTS
    rows = i * tile + lax.broadcasted_iota(jnp.int32, (qgw * tile, 1), 0) % tile
    mask = _slot_mask(lo_ref, hi_ref, base, rows)
    lane = lax.broadcasted_iota(jnp.int32, (1, STAT_LANES), 1)
    stats = jnp.full((tile, STAT_LANES), -jnp.inf, jnp.float32)
    for kv in range(heads // qgw):
        keys = _slot_keys(kt_ref, blk_ref, base, kv)
        sc = jnp.dot(_stacked(q_ref, kv, qgw), keys, preferred_element_type=jnp.float32)
        mx = jnp.max(jnp.where(mask, sc, -jnp.inf), axis=1, keepdims=True) * scale
        for j in range(qgw):
            stats = jnp.where(lane == kv * qgw + j, mx[j * tile : (j + 1) * tile], stats)
    m_ref[...] = jnp.transpose(stats)[: m_ref.shape[0], :]


def ctx_kernel(
    lo_ref, hi_ref, blk_ref, q_ref, kt_ref, v_ref, m_ref, o_ref, t_ref, *, heads, qgw, scale
):
    i = pl.program_id(0)
    tile = q_ref.shape[0]
    base = i * SLOTS
    rows = i * tile + lax.broadcasted_iota(jnp.int32, (qgw * tile, 1), 0) % tile
    mask = _slot_mask(lo_ref, hi_ref, base, rows)
    lane = lax.broadcasted_iota(jnp.int32, (1, STAT_LANES), 1)
    totals = jnp.zeros((tile, STAT_LANES), jnp.float32)
    tops = jnp.transpose(m_ref[...])
    for kv in range(heads // qgw):
        group = range(kv * qgw, (kv + 1) * qgw)
        keys = _slot_keys(kt_ref, blk_ref, base, kv)
        values = _slot_values(v_ref, blk_ref, base, kv)
        sc = jnp.dot(_stacked(q_ref, kv, qgw), keys, preferred_element_type=jnp.float32) * scale
        top = jnp.concatenate([tops[:, h : h + 1] for h in group], axis=0)
        p = jnp.exp(jnp.where(mask, sc - top, -jnp.inf))
        ctx = jnp.dot(p.astype(jnp.bfloat16), values, preferred_element_type=jnp.float32)
        tot = jnp.sum(p, axis=1, keepdims=True)
        for j, h in enumerate(group):
            o_ref[:, h * HEAD_SIZE : (h + 1) * HEAD_SIZE] = ctx[j * tile : (j + 1) * tile]
            totals = jnp.where(lane == h, tot[j * tile : (j + 1) * tile], totals)
    t_ref[...] = jnp.transpose(totals)[: t_ref.shape[0], :]


def butterfly(x, axis, combine):
    n = lax.axis_size(axis)
    stride = 1
    while stride < n:
        radix = 2 if stride == 1 or n % (stride * 4) else 4
        digit = lambda i: (i // stride) % radix
        got = [
            lax.ppermute(
                x,
                axis,
                [(i, i + ((digit(i) + d) % radix - digit(i)) * stride) for i in range(n)],
            )
            for d in range(1, radix)
        ]
        for g in got:
            x = combine(x, g)
        stride *= radix
    return x


def far_part(queries, keys_t, values, lo, hi, blk, qgw, blk_index, scale):
    tok_dev, q_cols = queries.shape
    heads = q_cols // HEAD_SIZE
    blocks, kv_cols, block_len = keys_t.shape
    gathered = lax.all_gather(queries, "blk", axis=0, tiled=True)
    row_count = gathered.shape[0]
    n_tiles = row_count // tok_dev
    stat_rows = 8
    q_spec = pl.BlockSpec((tok_dev, q_cols), lambda i, *_: (i, 0))
    kt_spec = pl.BlockSpec((blocks, kv_cols, block_len), lambda i, *_: (0, 0, 0))
    v_spec = pl.BlockSpec((blocks, block_len, kv_cols), lambda i, *_: (0, 0, 0))
    s_spec = pl.BlockSpec((stat_rows, tok_dev), lambda i, *_: (i, 0))
    stat_shape = jax.ShapeDtypeStruct((n_tiles * stat_rows, tok_dev), jnp.float32)
    kw = dict(heads=heads, qgw=qgw, scale=scale)
    local_max = pl.pallas_call(
        functools.partial(max_kernel, **kw),
        out_shape=stat_shape,
        grid_spec=pltpu.PrefetchScalarGridSpec(
            num_scalar_prefetch=3, grid=(n_tiles,), in_specs=[q_spec, kt_spec], out_specs=s_spec
        ),
    )(lo, hi, blk, gathered, keys_t)
    far_max = butterfly(local_max, "blk", jnp.maximum)
    partial, totals = pl.pallas_call(
        functools.partial(ctx_kernel, **kw),
        out_shape=(jax.ShapeDtypeStruct((row_count, q_cols), jnp.float32), stat_shape),
        grid_spec=pltpu.PrefetchScalarGridSpec(
            num_scalar_prefetch=3,
            grid=(n_tiles,),
            in_specs=[q_spec, kt_spec, v_spec, s_spec],
            out_specs=(pl.BlockSpec((tok_dev, q_cols), lambda i, *_: (i, 0)), s_spec),
        ),
    )(lo, hi, blk, gathered, keys_t, values, far_max)
    context = lax.psum_scatter(
        partial.astype(jnp.bfloat16), "blk", scatter_dimension=0, tiled=True
    ).astype(jnp.float32)
    totals = butterfly(totals, "blk", jnp.add)
    own = lambda a: jnp.transpose(
        lax.dynamic_slice_in_dim(a, blk_index * stat_rows, stat_rows, 0)[:heads]
    )
    return context, own(totals), own(far_max)


def column_sum(x, axis):
    n = lax.axis_size(axis)
    me = lax.axis_index(axis)
    width = x.shape[1] // n
    chunk = lambda k: lax.dynamic_slice_in_dim(x, (k % n) * width, width, 1)
    total = chunk(me)
    for d in range(1, n):
        sent = chunk(me + d).astype(jnp.bfloat16)
        got = lax.ppermute(sent, axis, [(i, (i + d) % n) for i in range(n)])
        total = total + got.astype(jnp.float32)
    return total


def per_device(
    queries,
    suffix_key_rows,
    suffix_value_rows,
    prefix_block_keys,
    prefix_block_values,
    block_group,
    suffix_len,
    request_group,
    w_out,
):
    tok_dev = queries.shape[0]
    q_cols = queries.shape[1]
    kv_cols = suffix_key_rows.shape[1]
    local_kv = kv_cols // HEAD_SIZE
    local_heads = q_cols // HEAD_SIZE
    qgw = local_heads // local_kv
    blocks, block_len, _ = prefix_block_keys.shape
    blk_count = lax.axis_size("blk")
    row_count = blk_count * tok_dev
    blk_index = lax.axis_index("blk")
    scale = 1.0 / math.sqrt(HEAD_SIZE)
    tile = tok_dev
    n_tiles = row_count // tile

    lo, hi, blk = tile_tables(suffix_len, request_group, block_group, n_tiles, tile)
    keys_t = jnp.swapaxes(prefix_block_keys, 1, 2)
    far_context, far_total, own_far_max = far_part(
        queries, keys_t, prefix_block_values, lo, hi, blk, qgw, blk_index, scale
    )
    far_context = far_context.reshape(tok_dev, local_kv, qgw, HEAD_SIZE)
    far_total = far_total.reshape(tok_dev, local_kv, qgw)
    own_far_max = own_far_max.reshape(tok_dev, local_kv, qgw)

    row_ends = jnp.cumsum(suffix_len)
    starts = row_ends - suffix_len
    own_rows = blk_index * tok_dev + jnp.arange(tok_dev, dtype=jnp.int32)
    earlier_keys, earlier_values = from_behind((suffix_key_rows, suffix_value_rows), "blk", 1)
    near_keys = jnp.concatenate([earlier_keys, suffix_key_rows], axis=0).reshape(
        2 * tok_dev, local_kv, HEAD_SIZE
    )
    near_values = jnp.concatenate([earlier_values, suffix_value_rows], axis=0).reshape(
        2 * tok_dev, local_kv, HEAD_SIZE
    )
    near_rows = (blk_index - 1) * tok_dev + jnp.arange(2 * tok_dev, dtype=jnp.int32)
    own_req = request_of(own_rows, starts, row_ends)
    near_req = request_of(near_rows, starts, row_ends)
    allowed = (
        (own_req[:, None] == near_req[None, :])
        & (near_rows[None, :] <= own_rows[:, None])
        & (near_rows[None, :] >= 0)
    )
    own_queries = queries.reshape(tok_dev, local_kv, qgw, HEAD_SIZE)
    near_scores = (
        jnp.einsum("sgjd,tgd->sgjt", own_queries, near_keys, preferred_element_type=jnp.float32)
        * scale
    )
    near_scores = jnp.where(allowed[:, None, None, :], near_scores, -jnp.inf)
    near_max = jnp.max(near_scores, axis=3)
    top = jnp.maximum(own_far_max, near_max)
    near_prob = jnp.exp(near_scores - top[..., None])
    near_total = jnp.sum(near_prob, axis=3)
    near_context = jnp.einsum(
        "sgjt,tgd->sgjd",
        near_prob.astype(jnp.bfloat16),
        near_values,
        preferred_element_type=jnp.float32,
    )
    far_scale = jnp.exp(own_far_max - top)
    near_context, near_total, far_scale = lax.optimization_barrier(
        (near_context, near_total, far_scale)
    )
    context = far_context * far_scale[..., None] + near_context
    denominator = far_total * far_scale + near_total
    attention = (context / denominator[..., None]).reshape(tok_dev, q_cols).astype(jnp.bfloat16)
    projected = jnp.dot(attention, w_out, preferred_element_type=jnp.float32)
    return column_sum(projected, "kvh").astype(jnp.bfloat16)


def solution(mesh):
    placed = (
        P("blk", "kvh"),
        P("blk", "kvh"),
        P("blk", "kvh"),
        P("blk", None, "kvh"),
        P("blk", None, "kvh"),
        P("blk"),
        P(),
        P(),
        P("kvh", None),
    )
    return jax.shard_map(
        per_device, mesh=mesh, in_specs=placed, out_specs=P("blk", "kvh"), check_vma=False
    )
```

```python
import functools
import math

import jax
import jax.numpy as jnp
from jax import lax
from jax.experimental import pallas as pl
from jax.experimental.pallas import tpu as pltpu
from jax.sharding import PartitionSpec as P

HEAD_SIZE = 128
SLOTS = 5
STAT_LANES = 128


def from_behind(block, axis, distance):
    devices = range(lax.axis_size(axis))
    route = [(i - distance, i) for i in devices if i - distance in devices]
    return lax.ppermute(block, axis, route)


def request_of(row_ids, starts, row_ends):
    inside = (row_ids[:, None] >= starts[None, :]) & (row_ids[:, None] < row_ends[None, :])
    req_ids = jnp.arange(starts.shape[0], dtype=jnp.int32)
    return jnp.sum(jnp.where(inside, req_ids[None, :], 0), axis=1)


def tile_tables(suffix_len, request_group, block_group, n_tiles, tile):
    row_ends = jnp.cumsum(suffix_len).astype(jnp.int32)
    starts = row_ends - suffix_len
    tile_lo = jnp.arange(n_tiles, dtype=jnp.int32) * tile
    first = jnp.sum((row_ends[None, :] <= tile_lo[:, None]).astype(jnp.int32), axis=1)
    last = jnp.sum((row_ends[None, :] <= (tile_lo + tile - 1)[:, None]).astype(jnp.int32), axis=1)
    req = first[:, None] + jnp.arange(SLOTS, dtype=jnp.int32)[None, :]
    valid = req <= last[:, None]
    req_v = jnp.minimum(req, last[:, None])
    lo = jnp.where(valid, starts[req_v], 0).astype(jnp.int32)
    hi = jnp.where(valid, row_ends[req_v], 0).astype(jnp.int32)
    group_count = suffix_len.shape[0] // 4
    blocks = block_group.shape[0]
    owns = block_group[None, :] == jnp.arange(group_count, dtype=jnp.int32)[:, None]
    block_of_group = jnp.sum(
        jnp.where(owns, jnp.arange(blocks, dtype=jnp.int32)[None, :], 0), axis=1
    ).astype(jnp.int32)
    blk = block_of_group[request_group[req_v]].astype(jnp.int32)
    return lo.reshape(-1), hi.reshape(-1), blk.reshape(-1)


def _slot_mask(lo_ref, hi_ref, base, rows):
    seg = lax.broadcasted_iota(jnp.int32, (1, SLOTS * HEAD_SIZE), 1) // HEAD_SIZE
    own = jnp.zeros(rows.shape, jnp.int32)
    for s in range(SLOTS):
        inside = (rows >= lo_ref[base + s]) & (rows < hi_ref[base + s])
        own = jnp.where(inside, s, own)
    return seg == own


def _slot_keys(kt_ref, blk_ref, base, kv):
    cols = slice(kv * HEAD_SIZE, (kv + 1) * HEAD_SIZE)
    return jnp.concatenate([kt_ref[blk_ref[base + s], cols, :] for s in range(SLOTS)], axis=1)


def _slot_values(v_ref, blk_ref, base, kv):
    cols = slice(kv * HEAD_SIZE, (kv + 1) * HEAD_SIZE)
    return jnp.concatenate([v_ref[blk_ref[base + s], :, cols] for s in range(SLOTS)], axis=0)


def _stacked(q_ref, kv, qgw):
    return jnp.concatenate(
        [q_ref[:, h * HEAD_SIZE : (h + 1) * HEAD_SIZE] for h in range(kv * qgw, (kv + 1) * qgw)],
        axis=0,
    )


def max_kernel(lo_ref, hi_ref, blk_ref, q_ref, kt_ref, m_ref, *, heads, qgw, scale):
    i = pl.program_id(0)
    tile = q_ref.shape[0]
    base = i * SLOTS
    rows = i * tile + lax.broadcasted_iota(jnp.int32, (qgw * tile, 1), 0) % tile
    mask = _slot_mask(lo_ref, hi_ref, base, rows)
    lane = lax.broadcasted_iota(jnp.int32, (1, STAT_LANES), 1)
    stats = jnp.full((tile, STAT_LANES), -jnp.inf, jnp.float32)
    for kv in range(heads // qgw):
        keys = _slot_keys(kt_ref, blk_ref, base, kv)
        sc = jnp.dot(_stacked(q_ref, kv, qgw), keys, preferred_element_type=jnp.float32)
        mx = jnp.max(jnp.where(mask, sc, -jnp.inf), axis=1, keepdims=True) * scale
        for j in range(qgw):
            stats = jnp.where(lane == kv * qgw + j, mx[j * tile : (j + 1) * tile], stats)
    m_ref[...] = jnp.transpose(stats)[: m_ref.shape[0], :]


def ctx_kernel(
    lo_ref, hi_ref, blk_ref, q_ref, kt_ref, v_ref, m_ref, o_ref, t_ref, *, heads, qgw, scale
):
    i = pl.program_id(0)
    tile = q_ref.shape[0]
    base = i * SLOTS
    rows = i * tile + lax.broadcasted_iota(jnp.int32, (qgw * tile, 1), 0) % tile
    mask = _slot_mask(lo_ref, hi_ref, base, rows)
    lane = lax.broadcasted_iota(jnp.int32, (1, STAT_LANES), 1)
    totals = jnp.zeros((tile, STAT_LANES), jnp.float32)
    tops = jnp.transpose(m_ref[...])
    for kv in range(heads // qgw):
        group = range(kv * qgw, (kv + 1) * qgw)
        keys = _slot_keys(kt_ref, blk_ref, base, kv)
        values = _slot_values(v_ref, blk_ref, base, kv)
        sc = jnp.dot(_stacked(q_ref, kv, qgw), keys, preferred_element_type=jnp.float32) * scale
        top = jnp.concatenate([tops[:, h : h + 1] for h in group], axis=0)
        p = jnp.exp(jnp.where(mask, sc - top, -jnp.inf))
        ctx = jnp.dot(p.astype(jnp.bfloat16), values, preferred_element_type=jnp.float32)
        tot = jnp.sum(p, axis=1, keepdims=True)
        for j, h in enumerate(group):
            o_ref[:, h * HEAD_SIZE : (h + 1) * HEAD_SIZE] = ctx[j * tile : (j + 1) * tile]
            totals = jnp.where(lane == h, tot[j * tile : (j + 1) * tile], totals)
    t_ref[...] = jnp.transpose(totals)[: t_ref.shape[0], :]


def butterfly(x, axis, combine):
    n = lax.axis_size(axis)
    stride = 1
    while stride < n:
        radix = 8 if stride == 1 and n % 8 == 0 else (4 if n % (stride * 4) == 0 else 2)
        digit = lambda i: (i // stride) % radix
        got = [
            lax.ppermute(
                x,
                axis,
                [(i, i + ((digit(i) + d) % radix - digit(i)) * stride) for i in range(n)],
            )
            for d in range(1, radix)
        ]
        for g in got:
            x = combine(x, g)
        stride *= radix
    return x


def far_part(queries, keys_t, values, lo, hi, blk, qgw, blk_index, scale):
    tok_dev, q_cols = queries.shape
    heads = q_cols // HEAD_SIZE
    blocks, kv_cols, block_len = keys_t.shape
    gathered = lax.all_gather(queries, "blk", axis=0, tiled=True)
    row_count = gathered.shape[0]
    n_tiles = row_count // tok_dev
    stat_rows = 8
    q_spec = pl.BlockSpec((tok_dev, q_cols), lambda i, *_: (i, 0))
    kt_spec = pl.BlockSpec((blocks, kv_cols, block_len), lambda i, *_: (0, 0, 0))
    v_spec = pl.BlockSpec((blocks, block_len, kv_cols), lambda i, *_: (0, 0, 0))
    s_spec = pl.BlockSpec((stat_rows, tok_dev), lambda i, *_: (i, 0))
    stat_shape = jax.ShapeDtypeStruct((n_tiles * stat_rows, tok_dev), jnp.float32)
    kw = dict(heads=heads, qgw=qgw, scale=scale)
    local_max = pl.pallas_call(
        functools.partial(max_kernel, **kw),
        out_shape=stat_shape,
        grid_spec=pltpu.PrefetchScalarGridSpec(
            num_scalar_prefetch=3, grid=(n_tiles,), in_specs=[q_spec, kt_spec], out_specs=s_spec
        ),
    )(lo, hi, blk, gathered, keys_t)
    far_max = butterfly(local_max, "blk", jnp.maximum)
    partial, totals = pl.pallas_call(
        functools.partial(ctx_kernel, **kw),
        out_shape=(jax.ShapeDtypeStruct((row_count, q_cols), jnp.float32), stat_shape),
        grid_spec=pltpu.PrefetchScalarGridSpec(
            num_scalar_prefetch=3,
            grid=(n_tiles,),
            in_specs=[q_spec, kt_spec, v_spec, s_spec],
            out_specs=(pl.BlockSpec((tok_dev, q_cols), lambda i, *_: (i, 0)), s_spec),
        ),
    )(lo, hi, blk, gathered, keys_t, values, far_max)
    context = lax.psum_scatter(
        partial.astype(jnp.bfloat16), "blk", scatter_dimension=0, tiled=True
    ).astype(jnp.float32)
    totals = butterfly(totals, "blk", jnp.add)
    own = lambda a: jnp.transpose(
        lax.dynamic_slice_in_dim(a, blk_index * stat_rows, stat_rows, 0)[:heads]
    )
    return context, own(totals), own(far_max)


def column_sum(x, axis):
    n = lax.axis_size(axis)
    me = lax.axis_index(axis)
    width = x.shape[1] // n
    chunk = lambda k: lax.dynamic_slice_in_dim(x, (k % n) * width, width, 1)
    total = chunk(me)
    for d in range(1, n):
        sent = chunk(me + d).astype(jnp.bfloat16)
        got = lax.ppermute(sent, axis, [(i, (i + d) % n) for i in range(n)])
        total = total + got.astype(jnp.float32)
    return total


def per_device(
    queries,
    suffix_key_rows,
    suffix_value_rows,
    prefix_block_keys,
    prefix_block_values,
    block_group,
    suffix_len,
    request_group,
    w_out,
):
    tok_dev = queries.shape[0]
    q_cols = queries.shape[1]
    kv_cols = suffix_key_rows.shape[1]
    local_kv = kv_cols // HEAD_SIZE
    local_heads = q_cols // HEAD_SIZE
    qgw = local_heads // local_kv
    blocks, block_len, _ = prefix_block_keys.shape
    blk_count = lax.axis_size("blk")
    row_count = blk_count * tok_dev
    blk_index = lax.axis_index("blk")
    scale = 1.0 / math.sqrt(HEAD_SIZE)
    tile = tok_dev
    n_tiles = row_count // tile

    lo, hi, blk = tile_tables(suffix_len, request_group, block_group, n_tiles, tile)
    keys_t = jnp.swapaxes(prefix_block_keys, 1, 2)
    far_context, far_total, own_far_max = far_part(
        queries, keys_t, prefix_block_values, lo, hi, blk, qgw, blk_index, scale
    )
    far_context = far_context.reshape(tok_dev, local_kv, qgw, HEAD_SIZE)
    far_total = far_total.reshape(tok_dev, local_kv, qgw)
    own_far_max = own_far_max.reshape(tok_dev, local_kv, qgw)

    row_ends = jnp.cumsum(suffix_len)
    starts = row_ends - suffix_len
    own_rows = blk_index * tok_dev + jnp.arange(tok_dev, dtype=jnp.int32)
    earlier_keys, earlier_values = from_behind((suffix_key_rows, suffix_value_rows), "blk", 1)
    near_keys = jnp.concatenate([earlier_keys, suffix_key_rows], axis=0).reshape(
        2 * tok_dev, local_kv, HEAD_SIZE
    )
    near_values = jnp.concatenate([earlier_values, suffix_value_rows], axis=0).reshape(
        2 * tok_dev, local_kv, HEAD_SIZE
    )
    near_rows = (blk_index - 1) * tok_dev + jnp.arange(2 * tok_dev, dtype=jnp.int32)
    own_req = request_of(own_rows, starts, row_ends)
    near_req = request_of(near_rows, starts, row_ends)
    allowed = (
        (own_req[:, None] == near_req[None, :])
        & (near_rows[None, :] <= own_rows[:, None])
        & (near_rows[None, :] >= 0)
    )
    own_queries = queries.reshape(tok_dev, local_kv, qgw, HEAD_SIZE)
    near_scores = (
        jnp.einsum("sgjd,tgd->sgjt", own_queries, near_keys, preferred_element_type=jnp.float32)
        * scale
    )
    near_scores = jnp.where(allowed[:, None, None, :], near_scores, -jnp.inf)
    near_max = jnp.max(near_scores, axis=3)
    top = jnp.maximum(own_far_max, near_max)
    near_prob = jnp.exp(near_scores - top[..., None])
    near_total = jnp.sum(near_prob, axis=3)
    near_context = jnp.einsum(
        "sgjt,tgd->sgjd",
        near_prob.astype(jnp.bfloat16),
        near_values,
        preferred_element_type=jnp.float32,
    )
    far_scale = jnp.exp(own_far_max - top)
    near_context, near_total, far_scale = lax.optimization_barrier(
        (near_context, near_total, far_scale)
    )
    context = far_context * far_scale[..., None] + near_context
    denominator = far_total * far_scale + near_total
    attention = (context / denominator[..., None]).reshape(tok_dev, q_cols).astype(jnp.bfloat16)
    projected = jnp.dot(attention, w_out, preferred_element_type=jnp.float32)
    return column_sum(projected, "kvh").astype(jnp.bfloat16)


def solution(mesh):
    placed = (
        P("blk", "kvh"),
        P("blk", "kvh"),
        P("blk", "kvh"),
        P("blk", None, "kvh"),
        P("blk", None, "kvh"),
        P("blk"),
        P(),
        P(),
        P("kvh", None),
    )
    return jax.shard_map(
        per_device, mesh=mesh, in_specs=placed, out_specs=P("blk", "kvh"), check_vma=False
    )
```

```python
import functools
import math

import jax
import jax.numpy as jnp
from jax import lax
from jax.experimental import pallas as pl
from jax.experimental.pallas import tpu as pltpu
from jax.sharding import PartitionSpec as P

HEAD_SIZE = 128
SLOTS = 5
STAT_LANES = 128


def from_behind(block, axis, distance):
    devices = range(lax.axis_size(axis))
    route = [(i - distance, i) for i in devices if i - distance in devices]
    return lax.ppermute(block, axis, route)


def request_of(row_ids, starts, row_ends):
    inside = (row_ids[:, None] >= starts[None, :]) & (row_ids[:, None] < row_ends[None, :])
    req_ids = jnp.arange(starts.shape[0], dtype=jnp.int32)
    return jnp.sum(jnp.where(inside, req_ids[None, :], 0), axis=1)


def tile_tables(suffix_len, request_group, block_group, n_tiles, tile):
    row_ends = jnp.cumsum(suffix_len).astype(jnp.int32)
    starts = row_ends - suffix_len
    tile_lo = jnp.arange(n_tiles, dtype=jnp.int32) * tile
    first = jnp.sum((row_ends[None, :] <= tile_lo[:, None]).astype(jnp.int32), axis=1)
    last = jnp.sum((row_ends[None, :] <= (tile_lo + tile - 1)[:, None]).astype(jnp.int32), axis=1)
    req = first[:, None] + jnp.arange(SLOTS, dtype=jnp.int32)[None, :]
    valid = req <= last[:, None]
    req_v = jnp.minimum(req, last[:, None])
    lo = jnp.where(valid, starts[req_v], 0).astype(jnp.int32)
    hi = jnp.where(valid, row_ends[req_v], 0).astype(jnp.int32)
    group_count = suffix_len.shape[0] // 4
    blocks = block_group.shape[0]
    owns = block_group[None, :] == jnp.arange(group_count, dtype=jnp.int32)[:, None]
    block_of_group = jnp.sum(
        jnp.where(owns, jnp.arange(blocks, dtype=jnp.int32)[None, :], 0), axis=1
    ).astype(jnp.int32)
    blk = block_of_group[request_group[req_v]].astype(jnp.int32)
    return lo.reshape(-1), hi.reshape(-1), blk.reshape(-1)


def _slot_mask(lo_ref, hi_ref, base, rows):
    seg = lax.broadcasted_iota(jnp.int32, (1, SLOTS * HEAD_SIZE), 1) // HEAD_SIZE
    own = jnp.zeros(rows.shape, jnp.int32)
    for s in range(SLOTS):
        inside = (rows >= lo_ref[base + s]) & (rows < hi_ref[base + s])
        own = jnp.where(inside, s, own)
    return seg == own


def _slot_keys(kt_ref, blk_ref, base, kv):
    cols = slice(kv * HEAD_SIZE, (kv + 1) * HEAD_SIZE)
    return jnp.concatenate([kt_ref[blk_ref[base + s], cols, :] for s in range(SLOTS)], axis=1)


def _slot_values(v_ref, blk_ref, base, kv):
    cols = slice(kv * HEAD_SIZE, (kv + 1) * HEAD_SIZE)
    return jnp.concatenate([v_ref[blk_ref[base + s], :, cols] for s in range(SLOTS)], axis=0)


def _stacked(q_ref, kv, qgw):
    return jnp.concatenate(
        [q_ref[:, h * HEAD_SIZE : (h + 1) * HEAD_SIZE] for h in range(kv * qgw, (kv + 1) * qgw)],
        axis=0,
    )


def max_kernel(lo_ref, hi_ref, blk_ref, q_ref, kt_ref, m_ref, *, heads, qgw, scale):
    i = pl.program_id(0)
    tile = q_ref.shape[0]
    base = i * SLOTS
    rows = i * tile + lax.broadcasted_iota(jnp.int32, (qgw * tile, 1), 0) % tile
    mask = _slot_mask(lo_ref, hi_ref, base, rows)
    lane = lax.broadcasted_iota(jnp.int32, (1, STAT_LANES), 1)
    stats = jnp.full((tile, STAT_LANES), -jnp.inf, jnp.float32)
    for kv in range(heads // qgw):
        keys = _slot_keys(kt_ref, blk_ref, base, kv)
        sc = jnp.dot(_stacked(q_ref, kv, qgw), keys, preferred_element_type=jnp.float32)
        mx = jnp.max(jnp.where(mask, sc, -jnp.inf), axis=1, keepdims=True) * scale
        for j in range(qgw):
            stats = jnp.where(lane == kv * qgw + j, mx[j * tile : (j + 1) * tile], stats)
    m_ref[...] = jnp.transpose(stats)[: m_ref.shape[0], :]


def ctx_kernel(
    lo_ref, hi_ref, blk_ref, q_ref, kt_ref, v_ref, m_ref, o_ref, t_ref, *, heads, qgw, scale
):
    i = pl.program_id(0)
    tile = q_ref.shape[0]
    base = i * SLOTS
    rows = i * tile + lax.broadcasted_iota(jnp.int32, (qgw * tile, 1), 0) % tile
    mask = _slot_mask(lo_ref, hi_ref, base, rows)
    lane = lax.broadcasted_iota(jnp.int32, (1, STAT_LANES), 1)
    totals = jnp.zeros((tile, STAT_LANES), jnp.float32)
    tops = jnp.transpose(m_ref[...])
    for kv in range(heads // qgw):
        group = range(kv * qgw, (kv + 1) * qgw)
        keys = _slot_keys(kt_ref, blk_ref, base, kv)
        values = _slot_values(v_ref, blk_ref, base, kv)
        sc = jnp.dot(_stacked(q_ref, kv, qgw), keys, preferred_element_type=jnp.float32) * scale
        top = jnp.concatenate([tops[:, h : h + 1] for h in group], axis=0)
        p = jnp.exp(jnp.where(mask, sc - top, -jnp.inf))
        ctx = jnp.dot(p.astype(jnp.bfloat16), values, preferred_element_type=jnp.float32)
        tot = jnp.sum(p, axis=1, keepdims=True)
        for j, h in enumerate(group):
            o_ref[:, h * HEAD_SIZE : (h + 1) * HEAD_SIZE] = ctx[j * tile : (j + 1) * tile].astype(
                o_ref.dtype
            )
            totals = jnp.where(lane == h, tot[j * tile : (j + 1) * tile], totals)
    t_ref[...] = jnp.transpose(totals)[: t_ref.shape[0], :]


def butterfly(x, axis, combine):
    n = lax.axis_size(axis)
    stride = 1
    while stride < n:
        radix = 2 if stride == 1 or n % (stride * 4) else 4
        digit = lambda i: (i // stride) % radix
        got = [
            lax.ppermute(
                x,
                axis,
                [(i, i + ((digit(i) + d) % radix - digit(i)) * stride) for i in range(n)],
            )
            for d in range(1, radix)
        ]
        for g in got:
            x = combine(x, g)
        stride *= radix
    return x


def far_part(queries, keys_t, values, lo, hi, blk, qgw, blk_index, scale):
    tok_dev, q_cols = queries.shape
    heads = q_cols // HEAD_SIZE
    blocks, kv_cols, block_len = keys_t.shape
    gathered = lax.all_gather(queries, "blk", axis=0, tiled=True)
    row_count = gathered.shape[0]
    n_tiles = row_count // tok_dev
    stat_rows = 8
    q_spec = pl.BlockSpec((tok_dev, q_cols), lambda i, *_: (i, 0))
    kt_spec = pl.BlockSpec((blocks, kv_cols, block_len), lambda i, *_: (0, 0, 0))
    v_spec = pl.BlockSpec((blocks, block_len, kv_cols), lambda i, *_: (0, 0, 0))
    s_spec = pl.BlockSpec((stat_rows, tok_dev), lambda i, *_: (i, 0))
    stat_shape = jax.ShapeDtypeStruct((n_tiles * stat_rows, tok_dev), jnp.float32)
    kw = dict(heads=heads, qgw=qgw, scale=scale)
    local_max = pl.pallas_call(
        functools.partial(max_kernel, **kw),
        out_shape=stat_shape,
        grid_spec=pltpu.PrefetchScalarGridSpec(
            num_scalar_prefetch=3, grid=(n_tiles,), in_specs=[q_spec, kt_spec], out_specs=s_spec
        ),
    )(lo, hi, blk, gathered, keys_t)
    far_max = butterfly(local_max, "blk", jnp.maximum)
    partial, totals = pl.pallas_call(
        functools.partial(ctx_kernel, **kw),
        out_shape=(jax.ShapeDtypeStruct((row_count, q_cols), jnp.bfloat16), stat_shape),
        grid_spec=pltpu.PrefetchScalarGridSpec(
            num_scalar_prefetch=3,
            grid=(n_tiles,),
            in_specs=[q_spec, kt_spec, v_spec, s_spec],
            out_specs=(pl.BlockSpec((tok_dev, q_cols), lambda i, *_: (i, 0)), s_spec),
        ),
    )(lo, hi, blk, gathered, keys_t, values, far_max)
    context = lax.psum_scatter(
        partial, "blk", scatter_dimension=0, tiled=True
    ).astype(jnp.float32)
    totals = butterfly(totals, "blk", jnp.add)
    own = lambda a: jnp.transpose(
        lax.dynamic_slice_in_dim(a, blk_index * stat_rows, stat_rows, 0)[:heads]
    )
    return context, own(totals), own(far_max)


def column_sum(x, axis):
    n = lax.axis_size(axis)
    me = lax.axis_index(axis)
    width = x.shape[1] // n
    chunk = lambda k: lax.dynamic_slice_in_dim(x, (k % n) * width, width, 1)
    total = chunk(me)
    for d in range(1, n):
        sent = chunk(me + d).astype(jnp.bfloat16)
        got = lax.ppermute(sent, axis, [(i, (i + d) % n) for i in range(n)])
        total = total + got.astype(jnp.float32)
    return total


def per_device(
    queries,
    suffix_key_rows,
    suffix_value_rows,
    prefix_block_keys,
    prefix_block_values,
    block_group,
    suffix_len,
    request_group,
    w_out,
):
    tok_dev = queries.shape[0]
    q_cols = queries.shape[1]
    kv_cols = suffix_key_rows.shape[1]
    local_kv = kv_cols // HEAD_SIZE
    local_heads = q_cols // HEAD_SIZE
    qgw = local_heads // local_kv
    blocks, block_len, _ = prefix_block_keys.shape
    blk_count = lax.axis_size("blk")
    row_count = blk_count * tok_dev
    blk_index = lax.axis_index("blk")
    scale = 1.0 / math.sqrt(HEAD_SIZE)
    tile = tok_dev
    n_tiles = row_count // tile

    lo, hi, blk = tile_tables(suffix_len, request_group, block_group, n_tiles, tile)
    keys_t = jnp.swapaxes(prefix_block_keys, 1, 2)
    far_context, far_total, own_far_max = far_part(
        queries, keys_t, prefix_block_values, lo, hi, blk, qgw, blk_index, scale
    )
    far_context = far_context.reshape(tok_dev, local_kv, qgw, HEAD_SIZE)
    far_total = far_total.reshape(tok_dev, local_kv, qgw)
    own_far_max = own_far_max.reshape(tok_dev, local_kv, qgw)

    row_ends = jnp.cumsum(suffix_len)
    starts = row_ends - suffix_len
    own_rows = blk_index * tok_dev + jnp.arange(tok_dev, dtype=jnp.int32)
    earlier_keys, earlier_values = from_behind((suffix_key_rows, suffix_value_rows), "blk", 1)
    near_keys = jnp.concatenate([earlier_keys, suffix_key_rows], axis=0).reshape(
        2 * tok_dev, local_kv, HEAD_SIZE
    )
    near_values = jnp.concatenate([earlier_values, suffix_value_rows], axis=0).reshape(
        2 * tok_dev, local_kv, HEAD_SIZE
    )
    near_rows = (blk_index - 1) * tok_dev + jnp.arange(2 * tok_dev, dtype=jnp.int32)
    own_req = request_of(own_rows, starts, row_ends)
    near_req = request_of(near_rows, starts, row_ends)
    allowed = (
        (own_req[:, None] == near_req[None, :])
        & (near_rows[None, :] <= own_rows[:, None])
        & (near_rows[None, :] >= 0)
    )
    own_queries = queries.reshape(tok_dev, local_kv, qgw, HEAD_SIZE)
    near_scores = (
        jnp.einsum("sgjd,tgd->sgjt", own_queries, near_keys, preferred_element_type=jnp.float32)
        * scale
    )
    near_scores = jnp.where(allowed[:, None, None, :], near_scores, -jnp.inf)
    near_max = jnp.max(near_scores, axis=3)
    top = jnp.maximum(own_far_max, near_max)
    near_prob = jnp.exp(near_scores - top[..., None])
    near_total = jnp.sum(near_prob, axis=3)
    near_context = jnp.einsum(
        "sgjt,tgd->sgjd",
        near_prob.astype(jnp.bfloat16),
        near_values,
        preferred_element_type=jnp.float32,
    )
    far_scale = jnp.exp(own_far_max - top)
    near_context, near_total, far_scale = lax.optimization_barrier(
        (near_context, near_total, far_scale)
    )
    context = far_context * far_scale[..., None] + near_context
    denominator = far_total * far_scale + near_total
    attention = (context / denominator[..., None]).reshape(tok_dev, q_cols).astype(jnp.bfloat16)
    projected = jnp.dot(attention, w_out, preferred_element_type=jnp.float32)
    return column_sum(projected, "kvh").astype(jnp.bfloat16)


def solution(mesh):
    placed = (
        P("blk", "kvh"),
        P("blk", "kvh"),
        P("blk", "kvh"),
        P("blk", None, "kvh"),
        P("blk", None, "kvh"),
        P("blk"),
        P(),
        P(),
        P("kvh", None),
    )
    return jax.shard_map(
        per_device, mesh=mesh, in_specs=placed, out_specs=P("blk", "kvh"), check_vma=False
    )
```
